256 devices in a mesh: dp: 64 (over y, z, core), tensor: 4 (over x).
Axes of the slice: x: 4, y: 4, z: 8, core: 2. Of those that a mesh axis runs over, the one named last changes fastest.
Arguments:
- query: bfloat16 [4096, 2560], P('dp', 'tensor'), may hold values from -18 to 18
- new_kv: bfloat16 [2, 4096, 512], P(None, 'dp', 'tensor'), may hold values from -7 to 7
- key_value_pages: bfloat16 [2, 6080, 128, 512], P(None, 'dp', None, 'tensor'), may hold values from -7 to 7
- page_table: int32 [4096, 32], P('dp'), may hold values from 0 to 6079, as said below
- cache_len: int32 [4096], P('dp'), may hold values from 1 to 4096, as said below
- residual: bfloat16 [4096, 2560], P('dp'), may hold values from -6 to 6
- out_weight: bfloat16 [2560, 2560], P('tensor'), may hold values from -0.125 to 0.125
- norm_gain: float32 [2560], replicated, may hold values from 0.25 to 1.75
- expert_ids: int32 [4096, 6], P('dp'), may hold values from 0 to 63, all different within a row; in each aligned block of 64 rows (0 to 63, 64 to 127, ...) at most 9 rows name the same one
- combine_weights: float32 [4096, 6], P('dp'), may hold values from 0.1 to 1
- expert_w1: bfloat16 [64, 2560, 2, 1536], P('dp', None, None, 'tensor'), may hold values from -0.125 to 0.125
- expert_w2: bfloat16 [64, 1536, 2560], P('dp', 'tensor'), may hold values from -0.15625 to 0.15625
Outputs:
- layer_out: bfloat16 [4096, 2560], P('dp', 'tensor')
The draws below stay inside these ranges and needn't reach their ends.
Inputs may be any that keep to these rules, and one draw needn't show every extreme that they name: `page_table`: entry j of a request's row is the page holding its cache positions j * 128 to (j + 1) * 128 - 1; the pages of request r are among the 95 pages from (r // 64) * 95 on; no page serves two requests; entries past the last used page repeat it. `cache_len`: 6 requests, in 6 different blocks of 64 requests, hold more than (31) * 128 tokens, one of them exactly 4096; all others hold fewer than 64. `expert_ids`: each row names 6 different experts; among the rows of one device (aligned blocks of 64 rows) no expert is named more than 9 times.
All inputs are finite; a program needn't handle non-finite values.
Results may differ from the reference program's by a relative error of at most 0.012.
Values may be sent and summed in bfloat16 or wider, within the bound.
No kernel may reach another device: no remote copies, remote signals or barrier semaphores. Data moves between devices by JAX's collectives and lax.ppermute only.
A program may use at most 128 MiB of HBM per device.

```python
import math
import jax
import jax.numpy as jnp
import numpy as np
from jax import lax

D = 2560
QUERY_HEADS = 20
KEY_VALUE_HEADS = 4
HEAD_SIZE = 128
FF_E = 1536
TOPK = 6
EXP_DEV = 1
PAGE_TOKENS = 128
LONGEST_PAGES = 32
SHORT = 64
LONGS = 6
REQ_DEV = 64
EXPERTS = 64
REQUEST_COUNT = 4096
QUERY_PER_KEY = 5
PAGES_DEV = 95
TOTAL_PAGES = 6080
CAP = 9
N_DP = 64
N_TENSOR = 4


def key_value_rule(key, salt, shape):
    noise = jnp.clip(jax.random.normal(jax.random.fold_in(key, salt), shape, jnp.float32), -6.0, 6.0)
    return noise.astype(jnp.bfloat16)


def draw_key_value_pages(key, part):
    return key_value_rule(key, 21, (2, TOTAL_PAGES, PAGE_TOKENS, KEY_VALUE_HEADS * HEAD_SIZE))


def draw_new_kv(key, part):
    return key_value_rule(key, 22, (2, REQUEST_COUNT, KEY_VALUE_HEADS * HEAD_SIZE))


def draw_query(key, part):
    base = jnp.clip(jax.random.normal(jax.random.fold_in(key, 31), (REQUEST_COUNT, QUERY_HEADS * HEAD_SIZE), jnp.float32), -6.0, 6.0)
    return base.astype(jnp.bfloat16)


def page_layout(key):
    blocks = REQUEST_COUNT // REQ_DEV
    long_blocks = jax.random.permutation(jax.random.fold_in(key, 11), blocks)[:LONGS]
    long_slots = jax.random.randint(jax.random.fold_in(key, 12), (LONGS,), 0, REQ_DEV)
    long_reqs = long_blocks * REQ_DEV + long_slots
    is_long = jnp.zeros((REQUEST_COUNT,), jnp.bool_).at[long_reqs].set(True)
    short_len = jax.random.randint(jax.random.fold_in(key, 13), (REQUEST_COUNT,), 1, SHORT)
    long_len = LONGEST_PAGES * PAGE_TOKENS - jax.random.randint(jax.random.fold_in(key, 14), (REQUEST_COUNT,), 0, PAGE_TOKENS)
    long_len = long_len.at[long_reqs[0]].set(LONGEST_PAGES * PAGE_TOKENS)
    lengths = jnp.where(is_long, long_len, short_len).astype(jnp.int32)
    needed = ((lengths + PAGE_TOKENS - 1) // PAGE_TOKENS).reshape(blocks, REQ_DEV)
    offsets = jnp.cumsum(needed, axis=1) - needed
    orders = jax.vmap(lambda subkey: jax.random.permutation(subkey, PAGES_DEV))(jax.random.split(jax.random.fold_in(key, 15), blocks))
    columns = jnp.arange(LONGEST_PAGES)
    positions = offsets[:, :, None] + jnp.minimum(columns[None, None, :], needed[:, :, None] - 1)
    local_pages = jax.vmap(lambda order, where_at: order[where_at])(orders, positions)
    table = local_pages + jnp.arange(blocks)[:, None, None] * PAGES_DEV
    return (table.reshape(REQUEST_COUNT, LONGEST_PAGES).astype(jnp.int32), lengths)


def draw_page_table(key, part):
    return page_layout(key)[0]


def draw_cache_len(key, part):
    return page_layout(key)[1]


def steps_of(stream_key, extent, cuts, low, largest):
    gain, own = 1.0, jax.random.fold_in(stream_key, 6)
    for position, blocks in cuts:
        draws = jnp.exp(jax.random.uniform(jax.random.fold_in(own, position), (blocks,), jnp.float32, low / len(cuts), largest / len(cuts)))
        gain = gain * jnp.repeat(draws, extent[position] // blocks).reshape([-1 if axis == position else 1 for axis in range(len(extent))])
    return gain


def routed_block(rng, own, number, rows, amount, top, most, skew):
    order = jax.random.permutation(rng, amount)
    crowded, usual = shares(amount, rows * top, most, skew, True), shares(amount, rows * top, most, skew, False)
    places = jnp.arange(amount)

    def named(sizes, rotation):
        used = int((sizes > 0).sum())
        fixed = max(1, used // 4)
        shifted = fixed + (places - fixed + rotation * (used - fixed)) % max(1, amount - fixed)
        return jnp.zeros((amount,), jnp.int32).at[order[jnp.where(places < fixed, places, shifted)]].set(jnp.asarray(sizes, jnp.int32))

    sizes = jnp.where(number % 4 == 0, named(crowded, number // 4), named(usual, number - number // 4 - 1))
    mixed = jax.random.permutation(jax.random.fold_in(own, 3), amount)
    donor, receiver = mixed[0:amount // 2 * 2:2], mixed[1:amount // 2 * 2:2]
    room = jnp.minimum(sizes[donor] - 1, most - sizes[receiver]) // 2
    room = jnp.where((donor == order[0]) | (receiver == order[0]) | (sizes[receiver] == 0), 0, jnp.maximum(room, 0))
    shifted = jax.random.randint(jax.random.fold_in(own, 4), (amount // 2,), 0, 1 << 20) % (room + 1)
    sizes = sizes.at[donor].add(-shifted).at[receiver].add(shifted)
    members = jnp.searchsorted(jnp.cumsum(sizes), jnp.arange(rows * top), side="right").astype(jnp.int32)
    table = members.reshape(top, rows).T
    table = table[jax.random.permutation(jax.random.fold_in(own, 1), rows)]
    rotation = jax.random.randint(jax.random.fold_in(own, 2), (rows, 1), 0, top)
    return jnp.take_along_axis(table, (jnp.arange(top)[None, :] + rotation) % top, axis=1)


def shares(count, total, limit, skew, full):
    loads = [(1 << 20) // math.isqrt(rank ** skew) + 1 for rank in range(1, count + 1)]
    largest = limit if full else min(limit, max(-(-total // count), total * loads[0] // sum(loads)))
    least = 1 if total - largest >= count - 1 else 0
    given, surplus = [largest] + [least] * (count - 1), total - largest - least * (count - 1)
    while surplus > 0:
        candidates = [i for i in range(1, count) if given[i] < largest] or [i for i in range(1, count) if given[i] < limit]
        whole, budget = sum([loads[i] for i in candidates]), surplus
        for i in candidates:
            addition = min(limit - given[i], max(1, budget * loads[i] // whole), surplus)
            given[i] = given[i] + addition
            surplus = surplus - addition
    return np.array(given)


def gaussian(stream_key, dims, scale, limit, cuts=(), kind=jnp.bfloat16):
    loudness = steps_of(stream_key, dims, cuts, -0.22, 0.18) if cuts else 1.0
    drawn = jax.random.normal(stream_key, dims, jnp.float32) * scale * loudness
    return jnp.minimum(jnp.maximum(drawn, -limit), limit).astype(kind)


def setup_inputs(seed: int = 0) -> dict:
    splits = jax.random.split(jax.random.key(seed), 13)
    query = draw_query(jax.random.fold_in(splits[12], 71), 0)
    new_kv = draw_new_kv(jax.random.fold_in(splits[12], 71), 0)
    key_value_pages = draw_key_value_pages(jax.random.fold_in(splits[12], 71), 0)
    page_table = draw_page_table(jax.random.fold_in(splits[12], 71), 0)
    cache_len = draw_cache_len(jax.random.fold_in(splits[12], 71), 0)
    residual = gaussian(splits[5], (REQUEST_COUNT, D), 1.0, 6.0, ((0, 64),))
    out_weight = gaussian(splits[6], (QUERY_HEADS * HEAD_SIZE, D), (QUERY_HEADS * HEAD_SIZE) ** -0.5, 0.125, ((0, 4),))
    norm_gain = jnp.clip(1.0 + 0.15 * jax.random.normal(splits[7], (D,), jnp.float32), 0.25, 1.75)
    expert_ids_keys = jax.random.split(jax.random.fold_in(splits[8], 1), REQUEST_COUNT // REQ_DEV)
    expert_ids_turns = jax.random.permutation(jax.random.fold_in(splits[8], 3), REQUEST_COUNT // REQ_DEV)
    expert_ids = jax.vmap(lambda own, number: routed_block(jax.random.fold_in(splits[8], 2), own, number, REQ_DEV, EXPERTS, TOPK, CAP, 2))(expert_ids_keys, expert_ids_turns).reshape((REQUEST_COUNT, TOPK))
    combine_weights = jnp.clip(jnp.exp(math.log(1.0) - 2.3025851 * jax.random.uniform(splits[9], (REQUEST_COUNT, TOPK), jnp.float32) ** steps_of(splits[9], (REQUEST_COUNT, TOPK), ((0, 64),), -0.2, 0.2)), 0.1, 1.0)
    expert_w1 = gaussian(splits[10], (EXPERTS, D, 2, FF_E), D ** -0.5, 0.125, ((0, 64), (3, 4)))
    expert_w2 = gaussian(splits[11], (EXPERTS, FF_E, D), FF_E ** -0.5, 0.15625, ((0, 64), (1, 4)))
    return {"query": query, "new_kv": new_kv, "key_value_pages": key_value_pages, "page_table": page_table, "cache_len": cache_len, "residual": residual, "out_weight": out_weight, "norm_gain": norm_gain, "expert_ids": expert_ids, "combine_weights": combine_weights, "expert_w1": expert_w1, "expert_w2": expert_w2}


def attend_request(query_vector, fresh_key, fresh_value, request_table_row, length, key_value_pages):
    scale_of_score = 1.0 / math.sqrt(HEAD_SIZE)
    keys_of_page = key_value_pages[0][request_table_row].reshape(LONGEST_PAGES * PAGE_TOKENS, KEY_VALUE_HEADS, HEAD_SIZE).astype(jnp.float32)
    values_of_page = key_value_pages[1][request_table_row].reshape(LONGEST_PAGES * PAGE_TOKENS, KEY_VALUE_HEADS, HEAD_SIZE).astype(jnp.float32)
    head_list = query_vector.reshape(KEY_VALUE_HEADS, QUERY_PER_KEY, HEAD_SIZE).astype(jnp.float32)
    scores = jnp.einsum('kgd,tkd->kgt', head_list, keys_of_page) * scale_of_score
    valid = jnp.arange(LONGEST_PAGES * PAGE_TOKENS, dtype=jnp.int32) < length
    scores = jnp.where(valid[None, None, :], scores, -1e+30)
    fresh_score = jnp.einsum('mib,mb->mi', head_list, fresh_key.reshape(KEY_VALUE_HEADS, HEAD_SIZE).astype(jnp.float32)) * scale_of_score
    row_max = jnp.maximum(lax.optimization_barrier(jnp.max(scores, axis=2)), fresh_score)
    weights = jnp.where(valid[None, None, :], jnp.exp(scores - row_max[:, :, None]), 0.0)
    weight_new = jnp.exp(fresh_score - row_max)
    denominator = lax.optimization_barrier(jnp.sum(weights, axis=2)) + weight_new
    rounded = lax.optimization_barrier(weights.astype(jnp.bfloat16)).astype(jnp.float32)
    fresh_rounded = lax.optimization_barrier(weight_new.astype(jnp.bfloat16)).astype(jnp.float32)
    weighted_numerator = jnp.einsum('kgt,tkd->kgd', rounded, values_of_page)
    weighted_numerator = weighted_numerator + fresh_rounded[:, :, None] * fresh_value.reshape(KEY_VALUE_HEADS, 1, HEAD_SIZE).astype(jnp.float32)
    return (weighted_numerator / denominator[:, :, None]).reshape(-1).astype(jnp.bfloat16)

def reference(query, new_kv, key_value_pages, page_table, cache_len, residual, out_weight, norm_gain, expert_ids, combine_weights, expert_w1, expert_w2):
    attn = lax.map(lambda packed: attend_request(packed[0], packed[1], packed[2], packed[3], packed[4], key_value_pages), (query, new_kv[0], new_kv[1], page_table, cache_len))
    hidden_state = residual.astype(jnp.float32) + jnp.dot(attn, out_weight, preferred_element_type=jnp.float32)
    mean_square = lax.optimization_barrier(jnp.mean(hidden_state * hidden_state, axis=1, keepdims=True))
    normed = (hidden_state * lax.rsqrt(mean_square + 1e-05) * norm_gain).astype(jnp.bfloat16)
    bound_rows = N_DP * EXP_DEV * CAP

    def per_expert(expert_mix, expert_index):
        hit = expert_ids == expert_index
        weight_row = lax.optimization_barrier(jnp.sum(jnp.where(hit, combine_weights, 0.0), axis=1))
        chosen = jnp.any(hit, axis=1)
        count = jnp.sum(chosen.astype(jnp.int32))
        picked = jnp.nonzero(chosen, size=bound_rows, fill_value=0)[0].astype(jnp.int32)
        live_rows = jnp.arange(bound_rows, dtype=jnp.int32) < count
        weight_sel = jnp.where(live_rows, weight_row[picked], 0.0)
        token_rows = normed[picked].astype(jnp.float32)
        first = lax.dynamic_index_in_dim(expert_w1, expert_index, 0, keepdims=False).astype(jnp.float32)
        second = lax.dynamic_index_in_dim(expert_w2, expert_index, 0, keepdims=False).astype(jnp.float32)
        gate_up = jnp.einsum('rd,dcf->rcf', token_rows, first)
        activated = jax.nn.silu(gate_up[:, 0, :]) * gate_up[:, 1, :]
        activated = lax.optimization_barrier(activated.astype(jnp.bfloat16)).astype(jnp.float32)
        grouped = jnp.einsum('rtf,tfd->rtd', activated.reshape(bound_rows, N_TENSOR, FF_E // N_TENSOR), second.reshape(N_TENSOR, FF_E // N_TENSOR, D))
        grouped = lax.optimization_barrier(grouped.astype(jnp.bfloat16)).astype(jnp.float32)
        expert_out = lax.optimization_barrier(lax.optimization_barrier(jnp.sum(grouped, axis=1)).astype(jnp.bfloat16)).astype(jnp.float32)
        expert_mix = expert_mix.at[picked].add(weight_sel[:, None] * expert_out)
        return (expert_mix, None)
    expert_mix, unused = lax.scan(per_expert, jnp.zeros((REQUEST_COUNT, D), jnp.float32), jnp.arange(EXPERTS, dtype=jnp.int32))
    return (hidden_state + expert_mix).astype(jnp.bfloat16)
```

```python
import math

import jax
import jax.numpy as jnp
from jax import lax
from jax.sharding import PartitionSpec as P

HEAD_SIZE = 128
SHORT = 64


def masked_softmax_attend(scores, valid, fresh_score, values, fresh_value):
    scores = jnp.where(valid, scores, -1e30)
    row_max = jnp.maximum(jnp.max(scores, axis=-1), fresh_score)
    weights = jnp.where(valid, jnp.exp(scores - row_max[..., None]), 0.0)
    weight_new = jnp.exp(fresh_score - row_max)
    denominator = jnp.sum(weights, axis=-1) + weight_new
    numerator = jnp.einsum(
        "...ht,...td->...hd",
        weights.astype(jnp.bfloat16),
        values,
        preferred_element_type=jnp.float32,
    )
    numerator = numerator + (
        weight_new.astype(jnp.bfloat16).astype(jnp.float32)[..., None]
        * fresh_value.astype(jnp.float32)[..., None, :]
    )
    return numerator / denominator[..., None]


def local_attention(query, new_kv, key_value_pages, page_table, cache_len):
    row_count = query.shape[0]
    pool_pages = key_value_pages.shape[1]
    page_size = key_value_pages.shape[2]
    head_dim = HEAD_SIZE
    local_heads = new_kv.shape[2] // head_dim
    group_heads = query.shape[1] // (local_heads * head_dim)
    table_width = page_table.shape[1]
    scale_of_score = 1.0 / math.sqrt(head_dim)
    local_pages = jnp.clip(page_table - lax.axis_index("dp") * pool_pages, 0, pool_pages - 1)
    heads = query.reshape(row_count, local_heads * group_heads, head_dim)
    new_keys = new_kv[0].reshape(row_count, local_heads * head_dim)
    new_values = new_kv[1].reshape(row_count, local_heads * head_dim)
    fresh_score = (
        jnp.einsum("rhd,rd->rh", heads, new_keys, preferred_element_type=jnp.float32)
        * scale_of_score
    )
    keys = key_value_pages[0].reshape(pool_pages, page_size, local_heads * head_dim)
    values = key_value_pages[1].reshape(pool_pages, page_size, local_heads * head_dim)

    first = local_pages[:, 0]
    short_keys = keys[:, :SHORT][first]
    short_values = values[:, :SHORT][first]
    short_scores = (
        jnp.einsum("rhd,rtd->rht", heads, short_keys, preferred_element_type=jnp.float32)
        * scale_of_score
    )
    short_valid = (jnp.arange(SHORT, dtype=jnp.int32)[None, :] < cache_len[:, None])[:, None, :]
    short_out = masked_softmax_attend(
        short_scores, short_valid, fresh_score, short_values, new_values
    )

    long_row = jnp.argmax(cache_len)
    long_len = cache_len[long_row]
    long_pages = local_pages[long_row]
    long_keys = keys[long_pages].reshape(table_width * page_size, local_heads * head_dim)
    long_values = values[long_pages].reshape(table_width * page_size, local_heads * head_dim)
    long_heads = heads[long_row]
    long_scores = (
        jnp.einsum("hd,td->ht", long_heads, long_keys, preferred_element_type=jnp.float32)
        * scale_of_score
    )
    long_valid = (jnp.arange(table_width * page_size, dtype=jnp.int32) < long_len)[None, :]
    long_out = masked_softmax_attend(
        long_scores, long_valid, fresh_score[long_row], long_values, new_values[long_row]
    )

    is_long = (jnp.arange(row_count, dtype=jnp.int32) == long_row) & (long_len >= SHORT)
    out = jnp.where(is_long[:, None, None], long_out[None], short_out)
    return out.reshape(row_count, -1).astype(jnp.bfloat16)


def per_device(
    query,
    new_kv,
    key_value_pages,
    page_table,
    cache_len,
    residual,
    out_weight,
    norm_gain,
    expert_ids,
    combine_weights,
    expert_w1,
    expert_w2,
):
    tensor_size = lax.axis_size("tensor")
    tensor_index = lax.axis_index("tensor")
    attn = local_attention(query, new_kv, key_value_pages, page_table, cache_len)
    row_count, model_width = residual.shape
    share_width = model_width // tensor_size
    share_start = tensor_index * share_width

    split_weight = out_weight.reshape(out_weight.shape[0], tensor_size, share_width)
    partial_proj = jnp.einsum(
        "rk,kuc->urc", attn, split_weight, preferred_element_type=jnp.float32
    )
    summed = lax.psum_scatter(partial_proj, "tensor", scatter_dimension=0, tiled=True)[0]
    residual_share = lax.dynamic_slice_in_dim(residual, share_start, share_width, 1)
    state = residual_share.astype(jnp.float32) + summed
    square_sum = lax.psum(jnp.sum(state * state, axis=1, keepdims=True), "tensor")
    mean_square = square_sum / model_width
    gain_share = lax.dynamic_slice_in_dim(norm_gain, share_start, share_width, 0)
    normed = (state * lax.rsqrt(mean_square + 1e-05) * gain_share).astype(jnp.bfloat16)

    local_experts = expert_w1.shape[0]
    top_count = expert_ids.shape[1]
    experts = local_experts * lax.axis_size("dp")
    capacity = min(
        row_count, max(3, (3 * row_count * top_count + 2 * experts - 1) // (2 * experts))
    )
    flat_ids = expert_ids.reshape(-1)
    choice_rows = flat_ids.shape[0]
    row_iota = jnp.arange(choice_rows, dtype=jnp.int32)
    choice_hot = (flat_ids[:, None] == jnp.arange(experts, dtype=jnp.int32)[None, :]).astype(
        jnp.bfloat16
    )
    strictly_lower = (row_iota[:, None] > row_iota[None, :]).astype(jnp.bfloat16)
    earlier = jnp.dot(strictly_lower, choice_hot, preferred_element_type=jnp.float32)
    slot_rank = jnp.sum(earlier * choice_hot.astype(jnp.float32), axis=1).astype(jnp.int32)
    slot_index = (flat_ids * capacity + slot_rank).reshape(row_count, top_count)
    slot_ids = jnp.arange(experts * capacity, dtype=jnp.int32)
    hit = slot_index[:, :, None] == slot_ids[None, None, :]
    placing = jnp.any(hit, axis=1).astype(jnp.bfloat16)
    mixing = jnp.sum(jnp.where(hit, combine_weights[:, :, None], 0.0), axis=1)

    outgoing = jnp.dot(placing.T, normed, preferred_element_type=jnp.float32)
    outgoing = outgoing.astype(jnp.bfloat16).reshape(experts, capacity, share_width)
    arrived = lax.all_to_all(outgoing, "dp", split_axis=0, concat_axis=0, tiled=True)
    gathered = lax.all_gather(arrived, "tensor", axis=0, tiled=False)
    split_w1 = expert_w1.reshape(tensor_size, share_width, 2, expert_w1.shape[-1])
    gate_up = jnp.einsum(
        "usnc,ucgf->sngf", gathered, split_w1, preferred_element_type=jnp.float32
    )
    activated = (jax.nn.silu(gate_up[:, :, 0, :]) * gate_up[:, :, 1, :]).astype(jnp.bfloat16)
    split_w2 = expert_w2[0].reshape(expert_w2.shape[1], tensor_size, share_width)
    partial_out = jnp.einsum(
        "snf,fuc->usnc", activated, split_w2, preferred_element_type=jnp.float32
    ).astype(jnp.bfloat16)
    partial_out = partial_out.reshape(tensor_size, experts * capacity, share_width)
    expert_sum = lax.psum_scatter(partial_out, "tensor", scatter_dimension=0, tiled=True)
    expert_sum = expert_sum.reshape(experts, capacity, share_width)
    returned_rows = lax.all_to_all(expert_sum, "dp", split_axis=0, concat_axis=0, tiled=True)
    expert_mix = jnp.dot(
        mixing,
        returned_rows.reshape(experts * capacity, share_width).astype(jnp.float32),
        precision=lax.Precision.HIGHEST,
    )
    return (state + expert_mix).astype(jnp.bfloat16)


def solution(mesh):
    return jax.shard_map(
        per_device,
        mesh=mesh,
        in_specs=(
            P("dp", "tensor"),
            P(None, "dp", "tensor"),
            P(None, "dp", None, "tensor"),
            P("dp", None),
            P("dp"),
            P("dp", None),
            P("tensor", None),
            P(),
            P("dp", None),
            P("dp", None),
            P("dp", None, None, "tensor"),
            P("dp", "tensor", None),
        ),
        out_specs=P("dp", "tensor"),
        check_vma=False,
    )
```

```python
import math

import jax
import jax.numpy as jnp
from jax import lax
from jax.experimental import pallas as pl
from jax.experimental.pallas import tpu as pltpu
from jax.sharding import PartitionSpec as P

HEAD_SIZE = 128
SHORT = 64


def attention_kernel(
    first_ref, long_ref, info_ref, q_ref, new_k_ref, new_v_ref, len_ref, kv_hbm, o_ref,
    short_k, short_v, long_k, long_v, sem,
):
    rows = q_ref.shape[0]
    head_dim = new_k_ref.shape[1]
    groups = q_ref.shape[1] // head_dim
    table_width = long_ref.shape[0]
    page_size = kv_hbm.shape[2]
    chunk = 16
    scale_of_score = 1.0 / math.sqrt(head_dim)

    def short_copy(r, which, buf):
        return pltpu.make_async_copy(
            kv_hbm.at[which, first_ref[r], pl.ds(0, SHORT), :],
            buf.at[pl.ds(r * SHORT, SHORT), :],
            sem.at[which, r],
        )

    def long_copy(j, which, buf):
        return pltpu.make_async_copy(
            kv_hbm.at[which, long_ref[j]],
            buf.at[pl.ds(j * page_size, page_size), :],
            sem.at[2 + which, j],
        )

    @pl.loop(0, rows)
    def _(r):
        short_copy(r, 0, short_k).start()
        short_copy(r, 1, short_v).start()

    @pl.loop(0, table_width)
    def _(j):
        long_copy(j, 0, long_k).start()
        long_copy(j, 1, long_v).start()

    @pl.loop(0, rows)
    def _(r):
        short_copy(r, 0, short_k).wait()
        short_copy(r, 1, short_v).wait()

    def attend(qh, keys, values, valid, new_k, new_v):
        scores = lax.dot_general(
            qh, keys, (((1,), (1,)), ((), ())), preferred_element_type=jnp.float32
        ) * scale_of_score
        fresh = jnp.sum(
            qh.astype(jnp.float32) * new_k.astype(jnp.float32), axis=1, keepdims=True
        ) * scale_of_score
        scores = jnp.where(valid, scores, -1e30)
        row_max = jnp.maximum(jnp.max(scores, axis=1, keepdims=True), fresh)
        weights = jnp.where(valid, jnp.exp(scores - row_max), 0.0)
        weight_new = jnp.exp(fresh - row_max)
        denominator = jnp.sum(weights, axis=1, keepdims=True) + weight_new
        numerator = jnp.dot(
            weights.astype(jnp.bfloat16), values, preferred_element_type=jnp.float32
        )
        numerator = numerator + (
            weight_new.astype(jnp.bfloat16).astype(jnp.float32) * new_v.astype(jnp.float32)
        )
        return (numerator / denominator).astype(o_ref.dtype)

    width = chunk * SHORT
    row = lax.broadcasted_iota(jnp.int32, (chunk, width), 0)
    col = lax.broadcasted_iota(jnp.int32, (chunk, width), 1)
    for c in range(rows // chunk):
        r0 = c * chunk
        keys = short_k[r0 * SHORT:(r0 + chunk) * SHORT, :]
        values = short_v[r0 * SHORT:(r0 + chunk) * SHORT, :]
        lengths = jnp.minimum(len_ref[r0:r0 + chunk, :], SHORT)
        valid = (col >= row * SHORT) & (col < row * SHORT + lengths)
        new_k = new_k_ref[r0:r0 + chunk, :]
        new_v = new_v_ref[r0:r0 + chunk, :]
        for h in range(groups):
            qh = q_ref[r0:r0 + chunk, h * head_dim:(h + 1) * head_dim]
            o_ref[r0:r0 + chunk, h * head_dim:(h + 1) * head_dim] = attend(
                qh, keys, values, valid, new_k, new_v
            )

    @pl.loop(0, table_width)
    def _(j):
        long_copy(j, 0, long_k).wait()
        long_copy(j, 1, long_v).wait()

    long_row = info_ref[0]
    long_len = info_ref[1]
    long_col = lax.broadcasted_iota(jnp.int32, (chunk, table_width * page_size), 1)
    long_valid = long_col < long_len
    own_row = lax.broadcasted_iota(jnp.int32, (chunk, 1), 0)
    for c in range(rows // chunk):
        r0 = c * chunk

        @pl.when((long_len >= SHORT) & (long_row >= r0) & (long_row < r0 + chunk))
        def _():
            new_k = new_k_ref[r0:r0 + chunk, :]
            new_v = new_v_ref[r0:r0 + chunk, :]
            chosen = (own_row + r0) == long_row
            for h in range(groups):
                qh = q_ref[r0:r0 + chunk, h * head_dim:(h + 1) * head_dim]
                result = attend(qh, long_k[...], long_v[...], long_valid, new_k, new_v)
                current = o_ref[r0:r0 + chunk, h * head_dim:(h + 1) * head_dim]
                o_ref[r0:r0 + chunk, h * head_dim:(h + 1) * head_dim] = jnp.where(
                    chosen, result, current
                )


def local_attention(query, new_kv, key_value_pages, page_table, cache_len):
    row_count = query.shape[0]
    pool_pages = key_value_pages.shape[1]
    page_size = key_value_pages.shape[2]
    head_dim = HEAD_SIZE
    table_width = page_table.shape[1]
    local_pages = jnp.clip(page_table - lax.axis_index("dp") * pool_pages, 0, pool_pages - 1)
    long_row = jnp.argmax(cache_len).astype(jnp.int32)
    info = jnp.stack([long_row, jnp.max(cache_len)]).astype(jnp.int32)
    first = local_pages[:, 0]
    long_pages = local_pages[long_row]
    smem = pl.BlockSpec(memory_space=pltpu.SMEM)
    vmem = pl.BlockSpec(memory_space=pltpu.VMEM)
    rows = row_count * SHORT + table_width * page_size
    return pl.pallas_call(
        attention_kernel,
        out_shape=jax.ShapeDtypeStruct(query.shape, jnp.bfloat16),
        in_specs=[smem, smem, smem, vmem, vmem, vmem, vmem, pl.BlockSpec(memory_space=pl.ANY)],
        out_specs=vmem,
        scratch_shapes=[
            pltpu.VMEM((row_count * SHORT, head_dim), key_value_pages.dtype),
            pltpu.VMEM((row_count * SHORT, head_dim), key_value_pages.dtype),
            pltpu.VMEM((table_width * page_size, head_dim), key_value_pages.dtype),
            pltpu.VMEM((table_width * page_size, head_dim), key_value_pages.dtype),
            pltpu.SemaphoreType.DMA((4, row_count)),
        ],
        cost_estimate=pl.CostEstimate(
            flops=4 * 16 * query.shape[1] * rows,
            transcendentals=16 * query.shape[1] // head_dim * rows,
            bytes_accessed=2 * 2 * head_dim * rows,
        ),
    )(
        first,
        long_pages,
        info,
        query,
        new_kv[0],
        new_kv[1],
        cache_len[:, None],
        key_value_pages,
    )


def per_device(
    query,
    new_kv,
    key_value_pages,
    page_table,
    cache_len,
    residual,
    out_weight,
    norm_gain,
    expert_ids,
    combine_weights,
    expert_w1,
    expert_w2,
):
    tensor_size = lax.axis_size("tensor")
    tensor_index = lax.axis_index("tensor")
    attn = local_attention(query, new_kv, key_value_pages, page_table, cache_len)
    row_count, model_width = residual.shape
    share_width = model_width // tensor_size
    share_start = tensor_index * share_width

    split_weight = out_weight.reshape(out_weight.shape[0], tensor_size, share_width)
    partial_proj = jnp.einsum(
        "rk,kuc->urc", attn, split_weight, preferred_element_type=jnp.float32
    )
    summed = lax.psum_scatter(partial_proj, "tensor", scatter_dimension=0, tiled=True)[0]
    residual_share = lax.dynamic_slice_in_dim(residual, share_start, share_width, 1)
    state = residual_share.astype(jnp.float32) + summed
    square_sum = lax.psum(jnp.sum(state * state, axis=1, keepdims=True), "tensor")
    mean_square = square_sum / model_width
    gain_share = lax.dynamic_slice_in_dim(norm_gain, share_start, share_width, 0)
    normed = (state * lax.rsqrt(mean_square + 1e-05) * gain_share).astype(jnp.bfloat16)

    local_experts = expert_w1.shape[0]
    top_count = expert_ids.shape[1]
    experts = local_experts * lax.axis_size("dp")
    capacity = min(
        row_count, max(3, (3 * row_count * top_count + 2 * experts - 1) // (2 * experts))
    )
    flat_ids = expert_ids.reshape(-1)
    choice_rows = flat_ids.shape[0]
    row_iota = jnp.arange(choice_rows, dtype=jnp.int32)
    choice_hot = (flat_ids[:, None] == jnp.arange(experts, dtype=jnp.int32)[None, :]).astype(
        jnp.bfloat16
    )
    strictly_lower = (row_iota[:, None] > row_iota[None, :]).astype(jnp.bfloat16)
    earlier = jnp.dot(strictly_lower, choice_hot, preferred_element_type=jnp.float32)
    slot_rank = jnp.sum(earlier * choice_hot.astype(jnp.float32), axis=1).astype(jnp.int32)
    slot_index = (flat_ids * capacity + slot_rank).reshape(row_count, top_count)
    slot_ids = jnp.arange(experts * capacity, dtype=jnp.int32)
    hit = slot_index[:, :, None] == slot_ids[None, None, :]
    placing = jnp.any(hit, axis=1).astype(jnp.bfloat16)
    mixing = jnp.sum(jnp.where(hit, combine_weights[:, :, None], 0.0), axis=1)

    outgoing = jnp.dot(placing.T, normed, preferred_element_type=jnp.float32)
    outgoing = outgoing.astype(jnp.bfloat16).reshape(experts, capacity, share_width)
    arrived = lax.all_to_all(outgoing, "dp", split_axis=0, concat_axis=0, tiled=True)
    gathered = lax.all_gather(arrived, "tensor", axis=0, tiled=False)
    split_w1 = expert_w1.reshape(tensor_size, share_width, 2, expert_w1.shape[-1])
    gate_up = jnp.einsum(
        "usnc,ucgf->sngf", gathered, split_w1, preferred_element_type=jnp.float32
    )
    activated = (jax.nn.silu(gate_up[:, :, 0, :]) * gate_up[:, :, 1, :]).astype(jnp.bfloat16)
    split_w2 = expert_w2[0].reshape(expert_w2.shape[1], tensor_size, share_width)
    partial_out = jnp.einsum(
        "snf,fuc->usnc", activated, split_w2, preferred_element_type=jnp.float32
    ).astype(jnp.bfloat16)
    partial_out = partial_out.reshape(tensor_size, experts * capacity, share_width)
    expert_sum = lax.psum_scatter(partial_out, "tensor", scatter_dimension=0, tiled=True)
    expert_sum = expert_sum.reshape(experts, capacity, share_width)
    returned_rows = lax.all_to_all(expert_sum, "dp", split_axis=0, concat_axis=0, tiled=True)
    expert_mix = jnp.dot(
        mixing,
        returned_rows.reshape(experts * capacity, share_width).astype(jnp.float32),
        precision=lax.Precision.HIGHEST,
    )
    return (state + expert_mix).astype(jnp.bfloat16)


def solution(mesh):
    return jax.shard_map(
        per_device,
        mesh=mesh,
        in_specs=(
            P("dp", "tensor"),
            P(None, "dp", "tensor"),
            P(None, "dp", None, "tensor"),
            P("dp", None),
            P("dp"),
            P("dp", None),
            P("tensor", None),
            P(),
            P("dp", None),
            P("dp", None),
            P("dp", None, None, "tensor"),
            P("dp", "tensor", None),
        ),
        out_specs=P("dp", "tensor"),
        check_vma=False,
    )
```

```python
import math

import jax
import jax.numpy as jnp
from jax import lax
from jax.experimental import pallas as pl
from jax.experimental.pallas import tpu as pltpu
from jax.sharding import PartitionSpec as P

HEAD_SIZE = 128
SHORT = 64


def attention_kernel(
    first_ref, long_ref, info_ref, q_ref, new_k_ref, new_v_ref, len_ref, kv_hbm, o_ref,
    short_k, short_v, long_k, long_v, sem,
):
    rows = q_ref.shape[0]
    head_dim = new_k_ref.shape[1]
    groups = q_ref.shape[1] // head_dim
    table_width = long_ref.shape[0]
    page_size = kv_hbm.shape[2]
    chunk = 16
    scale_of_score = 1.0 / math.sqrt(head_dim)

    def short_copy(r, which, buf):
        return pltpu.make_async_copy(
            kv_hbm.at[which, first_ref[r], pl.ds(0, SHORT), :],
            buf.at[pl.ds(r * SHORT, SHORT), :],
            sem.at[which, r],
        )

    def long_copy(j, which, buf):
        return pltpu.make_async_copy(
            kv_hbm.at[which, long_ref[j]],
            buf.at[pl.ds(j * page_size, page_size), :],
            sem.at[2 + which, j],
        )

    @pl.loop(0, rows)
    def _(r):
        short_copy(r, 0, short_k).start()
        short_copy(r, 1, short_v).start()

    @pl.loop(0, table_width)
    def _(j):
        long_copy(j, 0, long_k).start()
        long_copy(j, 1, long_v).start()

    @pl.loop(0, rows)
    def _(r):
        short_copy(r, 0, short_k).wait()
        short_copy(r, 1, short_v).wait()

    def attend(qh, keys, values, valid, new_k, new_v):
        scores = lax.dot_general(
            qh, keys, (((1,), (1,)), ((), ())), preferred_element_type=jnp.float32
        ) * scale_of_score
        fresh = jnp.sum(
            qh.astype(jnp.float32) * new_k.astype(jnp.float32), axis=1, keepdims=True
        ) * scale_of_score
        scores = jnp.where(valid, scores, -1e30)
        row_max = jnp.maximum(jnp.max(scores, axis=1, keepdims=True), fresh)
        weights = jnp.where(valid, jnp.exp(scores - row_max), 0.0)
        weight_new = jnp.exp(fresh - row_max)
        denominator = jnp.sum(weights, axis=1, keepdims=True) + weight_new
        numerator = jnp.dot(
            weights.astype(jnp.bfloat16), values, preferred_element_type=jnp.float32
        )
        numerator = numerator + (
            weight_new.astype(jnp.bfloat16).astype(jnp.float32) * new_v.astype(jnp.float32)
        )
        return (numerator / denominator).astype(o_ref.dtype)

    width = chunk * SHORT
    row = lax.broadcasted_iota(jnp.int32, (chunk, width), 0)
    col = lax.broadcasted_iota(jnp.int32, (chunk, width), 1)
    for c in range(rows // chunk):
        r0 = c * chunk
        keys = short_k[r0 * SHORT:(r0 + chunk) * SHORT, :]
        values = short_v[r0 * SHORT:(r0 + chunk) * SHORT, :]
        lengths = jnp.minimum(len_ref[r0:r0 + chunk, :], SHORT)
        valid = (col >= row * SHORT) & (col < row * SHORT + lengths)
        new_k = new_k_ref[r0:r0 + chunk, :]
        new_v = new_v_ref[r0:r0 + chunk, :]
        for h in range(groups):
            qh = q_ref[r0:r0 + chunk, h * head_dim:(h + 1) * head_dim]
            o_ref[r0:r0 + chunk, h * head_dim:(h + 1) * head_dim] = attend(
                qh, keys, values, valid, new_k, new_v
            )

    @pl.loop(0, table_width)
    def _(j):
        long_copy(j, 0, long_k).wait()
        long_copy(j, 1, long_v).wait()

    long_row = info_ref[0]
    long_len = info_ref[1]
    long_col = lax.broadcasted_iota(jnp.int32, (chunk, table_width * page_size), 1)
    long_valid = long_col < long_len
    own_row = lax.broadcasted_iota(jnp.int32, (chunk, 1), 0)
    for c in range(rows // chunk):
        r0 = c * chunk

        @pl.when((long_len >= SHORT) & (long_row >= r0) & (long_row < r0 + chunk))
        def _():
            new_k = new_k_ref[r0:r0 + chunk, :]
            new_v = new_v_ref[r0:r0 + chunk, :]
            chosen = (own_row + r0) == long_row
            for h in range(groups):
                qh = q_ref[r0:r0 + chunk, h * head_dim:(h + 1) * head_dim]
                result = attend(qh, long_k[...], long_v[...], long_valid, new_k, new_v)
                current = o_ref[r0:r0 + chunk, h * head_dim:(h + 1) * head_dim]
                o_ref[r0:r0 + chunk, h * head_dim:(h + 1) * head_dim] = jnp.where(
                    chosen, result, current
                )


def local_attention(query, new_kv, key_value_pages, page_table, cache_len):
    row_count = query.shape[0]
    pool_pages = key_value_pages.shape[1]
    page_size = key_value_pages.shape[2]
    head_dim = HEAD_SIZE
    table_width = page_table.shape[1]
    local_pages = jnp.clip(page_table - lax.axis_index("dp") * pool_pages, 0, pool_pages - 1)
    long_row = jnp.argmax(cache_len).astype(jnp.int32)
    info = jnp.stack([long_row, jnp.max(cache_len)]).astype(jnp.int32)
    first = local_pages[:, 0]
    long_pages = local_pages[long_row]
    smem = pl.BlockSpec(memory_space=pltpu.SMEM)
    vmem = pl.BlockSpec(memory_space=pltpu.VMEM)
    rows = row_count * SHORT + table_width * page_size
    return pl.pallas_call(
        attention_kernel,
        out_shape=jax.ShapeDtypeStruct(query.shape, jnp.bfloat16),
        in_specs=[smem, smem, smem, vmem, vmem, vmem, vmem, pl.BlockSpec(memory_space=pl.ANY)],
        out_specs=vmem,
        scratch_shapes=[
            pltpu.VMEM((row_count * SHORT, head_dim), key_value_pages.dtype),
            pltpu.VMEM((row_count * SHORT, head_dim), key_value_pages.dtype),
            pltpu.VMEM((table_width * page_size, head_dim), key_value_pages.dtype),
            pltpu.VMEM((table_width * page_size, head_dim), key_value_pages.dtype),
            pltpu.SemaphoreType.DMA((4, row_count)),
        ],
        cost_estimate=pl.CostEstimate(
            flops=4 * 16 * query.shape[1] * rows,
            transcendentals=16 * query.shape[1] // head_dim * rows,
            bytes_accessed=2 * 2 * head_dim * rows,
        ),
    )(
        first,
        long_pages,
        info,
        query,
        new_kv[0],
        new_kv[1],
        cache_len[:, None],
        key_value_pages,
    )


def per_device(
    query,
    new_kv,
    key_value_pages,
    page_table,
    cache_len,
    residual,
    out_weight,
    norm_gain,
    expert_ids,
    combine_weights,
    expert_w1,
    expert_w2,
):
    tensor_size = lax.axis_size("tensor")
    tensor_index = lax.axis_index("tensor")
    attn = local_attention(query, new_kv, key_value_pages, page_table, cache_len)
    row_count, model_width = residual.shape
    share_width = model_width // tensor_size
    share_start = tensor_index * share_width

    split_weight = out_weight.reshape(out_weight.shape[0], tensor_size, share_width)
    partial_proj = jnp.einsum(
        "rk,kuc->urc", attn, split_weight, preferred_element_type=jnp.float32
    )
    summed = lax.psum_scatter(partial_proj, "tensor", scatter_dimension=0, tiled=True)[0]
    residual_share = lax.dynamic_slice_in_dim(residual, share_start, share_width, 1)
    state = residual_share.astype(jnp.float32) + summed
    square_sum = lax.psum(jnp.sum(state * state, axis=1, keepdims=True), "tensor")
    mean_square = square_sum / model_width
    gain_share = lax.dynamic_slice_in_dim(norm_gain, share_start, share_width, 0)
    normed = (state * lax.rsqrt(mean_square + 1e-05) * gain_share).astype(jnp.bfloat16)

    local_experts = expert_w1.shape[0]
    top_count = expert_ids.shape[1]
    experts = local_experts * lax.axis_size("dp")
    capacity = min(
        row_count, max(3, (3 * row_count * top_count + 2 * experts - 1) // (2 * experts))
    )
    flat_ids = expert_ids.reshape(-1)
    choice_rows = flat_ids.shape[0]
    row_iota = jnp.arange(choice_rows, dtype=jnp.int32)
    choice_hot = (flat_ids[:, None] == jnp.arange(experts, dtype=jnp.int32)[None, :]).astype(
        jnp.bfloat16
    )
    strictly_lower = (row_iota[:, None] > row_iota[None, :]).astype(jnp.bfloat16)
    earlier = jnp.dot(strictly_lower, choice_hot, preferred_element_type=jnp.float32)
    slot_rank = jnp.sum(earlier * choice_hot.astype(jnp.float32), axis=1).astype(jnp.int32)
    slot_index = (flat_ids * capacity + slot_rank).reshape(row_count, top_count)
    slot_ids = jnp.arange(experts * capacity, dtype=jnp.int32)
    hit = slot_index[:, :, None] == slot_ids[None, None, :]
    placing = jnp.any(hit, axis=1).astype(jnp.bfloat16)
    mixing = jnp.sum(jnp.where(hit, combine_weights[:, :, None], 0.0), axis=1)

    outgoing = jnp.dot(placing.T, normed, preferred_element_type=jnp.float32)
    outgoing = outgoing.astype(jnp.bfloat16).reshape(experts, capacity, share_width)
    mixing = mixing.reshape(row_count, experts, capacity)
    split_w1 = expert_w1.reshape(tensor_size, share_width, 2, expert_w1.shape[-1])
    split_w2 = expert_w2[0].reshape(expert_w2.shape[1], tensor_size, share_width)

    expert_mix = None
    bounds = [0, (capacity + 1) // 2, capacity]
    for lo, hi in zip(bounds[:-1], bounds[1:]):
        slots = hi - lo
        arrived = lax.all_to_all(
            outgoing[:, lo:hi], "dp", split_axis=0, concat_axis=0, tiled=True
        )
        gathered = lax.all_gather(arrived, "tensor", axis=0, tiled=False)
        gate_up = jnp.einsum(
            "usnc,ucgf->sngf", gathered, split_w1, preferred_element_type=jnp.float32
        )
        activated = (jax.nn.silu(gate_up[:, :, 0, :]) * gate_up[:, :, 1, :]).astype(
            jnp.bfloat16
        )
        partial_out = jnp.einsum(
            "snf,fuc->usnc", activated, split_w2, preferred_element_type=jnp.float32
        ).astype(jnp.bfloat16)
        partial_out = partial_out.reshape(tensor_size, experts * slots, share_width)
        expert_sum = lax.psum_scatter(partial_out, "tensor", scatter_dimension=0, tiled=True)
        expert_sum = expert_sum.reshape(experts, slots, share_width)
        returned_rows = lax.all_to_all(
            expert_sum, "dp", split_axis=0, concat_axis=0, tiled=True
        )
        part_mix = jnp.dot(
            mixing[:, :, lo:hi].reshape(row_count, experts * slots),
            returned_rows.reshape(experts * slots, share_width).astype(jnp.float32),
            precision=lax.Precision.HIGHEST,
        )
        expert_mix = part_mix if expert_mix is None else expert_mix + part_mix
    return (state + expert_mix).astype(jnp.bfloat16)


def solution(mesh):
    return jax.shard_map(
        per_device,
        mesh=mesh,
        in_specs=(
            P("dp", "tensor"),
            P(None, "dp", "tensor"),
            P(None, "dp", None, "tensor"),
            P("dp", None),
            P("dp"),
            P("dp", None),
            P("tensor", None),
            P(),
            P("dp", None),
            P("dp", None),
            P("dp", None, None, "tensor"),
            P("dp", "tensor", None),
        ),
        out_specs=P("dp", "tensor"),
        check_vma=False,
    )
```

```python
import math

import jax
import jax.numpy as jnp
from jax import lax
from jax.experimental import pallas as pl
from jax.experimental.pallas import tpu as pltpu
from jax.sharding import PartitionSpec as P

HEAD_SIZE = 128
SHORT = 64


def attention_kernel(
    first_ref, long_ref, info_ref, q_ref, new_k_ref, new_v_ref, len_ref, kv_hbm, o_ref,
    short_k, short_v, long_k, long_v, sem,
):
    rows = q_ref.shape[0]
    head_dim = new_k_ref.shape[1]
    groups = q_ref.shape[1] // head_dim
    table_width = long_ref.shape[0]
    page_size = kv_hbm.shape[2]
    chunk = 16
    scale_of_score = 1.0 / math.sqrt(head_dim)

    def short_copy(r, which, buf):
        return pltpu.make_async_copy(
            kv_hbm.at[which, first_ref[r], pl.ds(0, SHORT), :],
            buf.at[pl.ds(r * SHORT, SHORT), :],
            sem.at[which, r],
        )

    def long_copy(j, which, buf):
        return pltpu.make_async_copy(
            kv_hbm.at[which, long_ref[j]],
            buf.at[pl.ds(j * page_size, page_size), :],
            sem.at[2 + which, j],
        )

    @pl.loop(0, rows)
    def _(r):
        short_copy(r, 0, short_k).start()
        short_copy(r, 1, short_v).start()

    @pl.loop(0, table_width)
    def _(j):
        long_copy(j, 0, long_k).start()
        long_copy(j, 1, long_v).start()

    @pl.loop(0, rows)
    def _(r):
        short_copy(r, 0, short_k).wait()
        short_copy(r, 1, short_v).wait()

    def attend(qh, keys, values, valid, new_k, new_v):
        scores = lax.dot_general(
            qh, keys, (((1,), (1,)), ((), ())), preferred_element_type=jnp.float32
        ) * scale_of_score
        fresh = jnp.sum(
            qh.astype(jnp.float32) * new_k.astype(jnp.float32), axis=1, keepdims=True
        ) * scale_of_score
        scores = jnp.where(valid, scores, -1e30)
        row_max = jnp.maximum(jnp.max(scores, axis=1, keepdims=True), fresh)
        weights = jnp.where(valid, jnp.exp(scores - row_max), 0.0)
        weight_new = jnp.exp(fresh - row_max)
        denominator = jnp.sum(weights, axis=1, keepdims=True) + weight_new
        numerator = jnp.dot(
            weights.astype(jnp.bfloat16), values, preferred_element_type=jnp.float32
        )
        numerator = numerator + (
            weight_new.astype(jnp.bfloat16).astype(jnp.float32) * new_v.astype(jnp.float32)
        )
        return (numerator / denominator).astype(o_ref.dtype)

    width = chunk * SHORT
    row = lax.broadcasted_iota(jnp.int32, (chunk, width), 0)
    col = lax.broadcasted_iota(jnp.int32, (chunk, width), 1)

    @pl.loop(0, rows // chunk)
    def _(c):
        r0 = pl.multiple_of(c * chunk, chunk)
        k0 = pl.multiple_of(c * width, width)
        keys = short_k[pl.ds(k0, width), :]
        values = short_v[pl.ds(k0, width), :]
        lengths = jnp.minimum(len_ref[pl.ds(r0, chunk), :], SHORT)
        valid = (col >= row * SHORT) & (col < row * SHORT + lengths)
        new_k = new_k_ref[pl.ds(r0, chunk), :]
        new_v = new_v_ref[pl.ds(r0, chunk), :]
        for h in range(groups):
            qh = q_ref[pl.ds(r0, chunk), h * head_dim:(h + 1) * head_dim]
            o_ref[pl.ds(r0, chunk), h * head_dim:(h + 1) * head_dim] = attend(
                qh, keys, values, valid, new_k, new_v
            )

    @pl.loop(0, table_width)
    def _(j):
        long_copy(j, 0, long_k).wait()
        long_copy(j, 1, long_v).wait()

    long_row = info_ref[0]
    long_len = info_ref[1]
    long_col = lax.broadcasted_iota(jnp.int32, (chunk, table_width * page_size), 1)
    long_valid = long_col < long_len
    own_row = lax.broadcasted_iota(jnp.int32, (chunk, 1), 0)

    @pl.when(long_len >= SHORT)
    def _():
        r0 = pl.multiple_of((long_row // chunk) * chunk, chunk)
        new_k = new_k_ref[pl.ds(r0, chunk), :]
        new_v = new_v_ref[pl.ds(r0, chunk), :]
        chosen = (own_row + r0) == long_row
        for h in range(groups):
            qh = q_ref[pl.ds(r0, chunk), h * head_dim:(h + 1) * head_dim]
            result = attend(qh, long_k[...], long_v[...], long_valid, new_k, new_v)
            current = o_ref[pl.ds(r0, chunk), h * head_dim:(h + 1) * head_dim]
            o_ref[pl.ds(r0, chunk), h * head_dim:(h + 1) * head_dim] = jnp.where(
                chosen, result, current
            )


def local_attention(query, new_kv, key_value_pages, page_table, cache_len):
    row_count = query.shape[0]
    pool_pages = key_value_pages.shape[1]
    page_size = key_value_pages.shape[2]
    head_dim = HEAD_SIZE
    table_width = page_table.shape[1]
    local_pages = jnp.clip(page_table - lax.axis_index("dp") * pool_pages, 0, pool_pages - 1)
    long_row = jnp.argmax(cache_len).astype(jnp.int32)
    info = jnp.stack([long_row, jnp.max(cache_len)]).astype(jnp.int32)
    first = local_pages[:, 0]
    long_pages = local_pages[long_row]
    smem = pl.BlockSpec(memory_space=pltpu.SMEM)
    vmem = pl.BlockSpec(memory_space=pltpu.VMEM)
    rows = row_count * SHORT + table_width * page_size
    return pl.pallas_call(
        attention_kernel,
        out_shape=jax.ShapeDtypeStruct(query.shape, jnp.bfloat16),
        in_specs=[smem, smem, smem, vmem, vmem, vmem, vmem, pl.BlockSpec(memory_space=pl.ANY)],
        out_specs=vmem,
        scratch_shapes=[
            pltpu.VMEM((row_count * SHORT, head_dim), key_value_pages.dtype),
            pltpu.VMEM((row_count * SHORT, head_dim), key_value_pages.dtype),
            pltpu.VMEM((table_width * page_size, head_dim), key_value_pages.dtype),
            pltpu.VMEM((table_width * page_size, head_dim), key_value_pages.dtype),
            pltpu.SemaphoreType.DMA((4, row_count)),
        ],
        cost_estimate=pl.CostEstimate(
            flops=4 * 16 * query.shape[1] * rows,
            transcendentals=16 * query.shape[1] // head_dim * rows,
            bytes_accessed=2 * 2 * head_dim * rows,
        ),
    )(
        first,
        long_pages,
        info,
        query,
        new_kv[0],
        new_kv[1],
        cache_len[:, None],
        key_value_pages,
    )


def ring_shift(x, shift, axis_name, size):
    return lax.ppermute(x, axis_name, [(i, (i + shift) % size) for i in range(size)])


def ring_reduce_scatter(blocks, axis_name, size, index):
    total = lax.dynamic_index_in_dim(blocks, index, 0, keepdims=False).astype(jnp.float32)
    for shift in range(1, size):
        outgoing = lax.dynamic_index_in_dim(blocks, (index + shift) % size, 0, keepdims=False)
        total = total + ring_shift(outgoing, shift, axis_name, size).astype(jnp.float32)
    return total


def ring_all_gather(x, axis_name, size):
    return [x] + [ring_shift(x, shift, axis_name, size) for shift in range(1, size)]


def per_device(
    query,
    new_kv,
    key_value_pages,
    page_table,
    cache_len,
    residual,
    out_weight,
    norm_gain,
    expert_ids,
    combine_weights,
    expert_w1,
    expert_w2,
):
    tensor_size = lax.axis_size("tensor")
    tensor_index = lax.axis_index("tensor")
    attn = local_attention(query, new_kv, key_value_pages, page_table, cache_len)
    row_count, model_width = residual.shape
    share_width = model_width // tensor_size
    share_start = tensor_index * share_width

    split_weight = out_weight.reshape(out_weight.shape[0], tensor_size, share_width)
    partial_proj = jnp.einsum(
        "rk,kuc->urc", attn, split_weight, preferred_element_type=jnp.float32
    )
    summed = ring_reduce_scatter(partial_proj, "tensor", tensor_size, tensor_index)
    residual_share = lax.dynamic_slice_in_dim(residual, share_start, share_width, 1)
    state = residual_share.astype(jnp.float32) + summed
    square_sum = sum(ring_all_gather(jnp.sum(state * state, axis=1, keepdims=True), "tensor", tensor_size))
    mean_square = square_sum / model_width
    gain_share = lax.dynamic_slice_in_dim(norm_gain, share_start, share_width, 0)
    normed = (state * lax.rsqrt(mean_square + 1e-05) * gain_share).astype(jnp.bfloat16)

    local_experts = expert_w1.shape[0]
    top_count = expert_ids.shape[1]
    experts = local_experts * lax.axis_size("dp")
    capacity = min(
        row_count, max(3, (3 * row_count * top_count + 2 * experts - 1) // (2 * experts))
    )
    flat_ids = expert_ids.reshape(-1)
    choice_rows = flat_ids.shape[0]
    row_iota = jnp.arange(choice_rows, dtype=jnp.int32)
    choice_hot = (flat_ids[:, None] == jnp.arange(experts, dtype=jnp.int32)[None, :]).astype(
        jnp.bfloat16
    )
    strictly_lower = (row_iota[:, None] > row_iota[None, :]).astype(jnp.bfloat16)
    earlier = jnp.dot(strictly_lower, choice_hot, preferred_element_type=jnp.float32)
    slot_rank = jnp.sum(earlier * choice_hot.astype(jnp.float32), axis=1).astype(jnp.int32)
    slot_index = (flat_ids * capacity + slot_rank).reshape(row_count, top_count)
    slot_ids = jnp.arange(experts * capacity, dtype=jnp.int32)
    hit = slot_index[:, :, None] == slot_ids[None, None, :]
    placing = jnp.any(hit, axis=1).astype(jnp.bfloat16)
    mixing = jnp.sum(jnp.where(hit, combine_weights[:, :, None], 0.0), axis=1)

    outgoing = jnp.dot(placing.T, normed, preferred_element_type=jnp.float32)
    outgoing = outgoing.astype(jnp.bfloat16).reshape(experts, capacity, share_width)
    mixing = mixing.reshape(row_count, experts, capacity)
    split_w1 = expert_w1.reshape(tensor_size, share_width, 2, expert_w1.shape[-1])
    split_w2 = expert_w2[0].reshape(expert_w2.shape[1], tensor_size, share_width)

    expert_mix = None
    bounds = [0, (capacity + 1) // 2, capacity]
    for lo, hi in zip(bounds[:-1], bounds[1:]):
        slots = hi - lo
        arrived = lax.all_to_all(
            outgoing[:, lo:hi], "dp", split_axis=0, concat_axis=0, tiled=True
        )
        pieces = ring_all_gather(arrived, "tensor", tensor_size)
        gate_up = None
        for shift, piece in enumerate(pieces):
            weight = lax.dynamic_index_in_dim(
                split_w1, (tensor_index - shift) % tensor_size, 0, keepdims=False
            )
            term = jnp.einsum("snc,cgf->sngf", piece, weight, preferred_element_type=jnp.float32)
            gate_up = term if gate_up is None else gate_up + term
        activated = (jax.nn.silu(gate_up[:, :, 0, :]) * gate_up[:, :, 1, :]).astype(
            jnp.bfloat16
        )
        partial_out = jnp.einsum(
            "snf,fuc->usnc", activated, split_w2, preferred_element_type=jnp.float32
        ).astype(jnp.bfloat16)
        expert_sum = ring_reduce_scatter(partial_out, "tensor", tensor_size, tensor_index)
        expert_sum = expert_sum.astype(jnp.bfloat16)
        returned_rows = lax.all_to_all(
            expert_sum, "dp", split_axis=0, concat_axis=0, tiled=True
        )
        part_mix = jnp.dot(
            mixing[:, :, lo:hi].reshape(row_count, experts * slots),
            returned_rows.reshape(experts * slots, share_width).astype(jnp.float32),
            precision=lax.Precision.HIGHEST,
        )
        expert_mix = part_mix if expert_mix is None else expert_mix + part_mix
    return (state + expert_mix).astype(jnp.bfloat16)


def solution(mesh):
    return jax.shard_map(
        per_device,
        mesh=mesh,
        in_specs=(
            P("dp", "tensor"),
            P(None, "dp", "tensor"),
            P(None, "dp", None, "tensor"),
            P("dp", None),
            P("dp"),
            P("dp", None),
            P("tensor", None),
            P(),
            P("dp", None),
            P("dp", None),
            P("dp", None, None, "tensor"),
            P("dp", "tensor", None),
        ),
        out_specs=P("dp", "tensor"),
        check_vma=False,
    )
```

```python
import math

import jax
import jax.numpy as jnp
from jax import lax
from jax.experimental import pallas as pl
from jax.experimental.pallas import tpu as pltpu
from jax.sharding import PartitionSpec as P

HEAD_SIZE = 128
SHORT = 64


def attention_kernel(
    table_ref, len_ref, base_ref, q_ref, new_k_ref, new_v_ref, kv_hbm, o_ref,
    short_k, short_v, long_k, long_v, sem,
):
    rows = q_ref.shape[0]
    head_dim = new_k_ref.shape[1]
    groups = q_ref.shape[1] // head_dim
    table_width = table_ref.shape[1]
    pool_pages = kv_hbm.shape[1]
    page_size = kv_hbm.shape[2]
    chunk = 16
    scale_of_score = 1.0 / math.sqrt(head_dim)
    base = base_ref[0]

    def local_page(r, j):
        return jnp.minimum(jnp.maximum(table_ref[r, j] - base, 0), pool_pages - 1)

    def longest(r, carry):
        best_row, best_len = carry
        length = len_ref[r]
        better = length > best_len
        return jnp.where(better, r, best_row), jnp.where(better, length, best_len)

    long_row, long_len = lax.fori_loop(0, rows, longest, (jnp.int32(0), len_ref[0]))

    def short_copy(r, which, buf):
        return pltpu.make_async_copy(
            kv_hbm.at[which, local_page(r, 0), pl.ds(0, SHORT), :],
            buf.at[pl.ds(r * SHORT, SHORT), :],
            sem.at[which, r],
        )

    def long_copy(j, which, buf):
        return pltpu.make_async_copy(
            kv_hbm.at[which, local_page(long_row, j)],
            buf.at[pl.ds(j * page_size, page_size), :],
            sem.at[2 + which, j],
        )

    @pl.loop(0, rows)
    def _(r):
        short_copy(r, 0, short_k).start()
        short_copy(r, 1, short_v).start()

    @pl.loop(0, table_width)
    def _(j):
        long_copy(j, 0, long_k).start()
        long_copy(j, 1, long_v).start()

    @pl.loop(0, rows)
    def _(r):
        short_copy(r, 0, short_k).wait()
        short_copy(r, 1, short_v).wait()

    def attend(qh, keys, values, valid, new_k, new_v):
        scores = lax.dot_general(
            qh, keys, (((1,), (1,)), ((), ())), preferred_element_type=jnp.float32
        ) * scale_of_score
        fresh = jnp.sum(
            qh.astype(jnp.float32) * new_k.astype(jnp.float32), axis=1, keepdims=True
        ) * scale_of_score
        scores = jnp.where(valid, scores, -1e30)
        row_max = jnp.maximum(jnp.max(scores, axis=1, keepdims=True), fresh)
        weights = jnp.where(valid, jnp.exp(scores - row_max), 0.0)
        weight_new = jnp.exp(fresh - row_max)
        denominator = jnp.sum(weights, axis=1, keepdims=True) + weight_new
        numerator = jnp.dot(
            weights.astype(jnp.bfloat16), values, preferred_element_type=jnp.float32
        )
        numerator = numerator + (
            weight_new.astype(jnp.bfloat16).astype(jnp.float32) * new_v.astype(jnp.float32)
        )
        return (numerator / denominator).astype(o_ref.dtype)

    width = chunk * SHORT
    row = lax.broadcasted_iota(jnp.int32, (chunk, width), 0)
    col = lax.broadcasted_iota(jnp.int32, (chunk, width), 1)

    @pl.loop(0, rows // chunk)
    def _(c):
        r0 = pl.multiple_of(c * chunk, chunk)
        k0 = pl.multiple_of(c * width, width)
        keys = short_k[pl.ds(k0, width), :]
        values = short_v[pl.ds(k0, width), :]
        lengths = jnp.zeros((chunk, 1), jnp.int32)
        for i in range(chunk):
            lengths = jnp.where(row[:, :1] == i, jnp.minimum(len_ref[r0 + i], SHORT), lengths)
        valid = (col >= row * SHORT) & (col < row * SHORT + lengths)
        new_k = new_k_ref[pl.ds(r0, chunk), :]
        new_v = new_v_ref[pl.ds(r0, chunk), :]
        for h in range(groups):
            qh = q_ref[pl.ds(r0, chunk), h * head_dim:(h + 1) * head_dim]
            o_ref[pl.ds(r0, chunk), h * head_dim:(h + 1) * head_dim] = attend(
                qh, keys, values, valid, new_k, new_v
            )

    @pl.loop(0, table_width)
    def _(j):
        long_copy(j, 0, long_k).wait()
        long_copy(j, 1, long_v).wait()

    long_col = lax.broadcasted_iota(jnp.int32, (chunk, table_width * page_size), 1)
    long_valid = long_col < long_len
    own_row = lax.broadcasted_iota(jnp.int32, (chunk, 1), 0)

    @pl.when(long_len >= SHORT)
    def _():
        r0 = pl.multiple_of((long_row // chunk) * chunk, chunk)
        new_k = new_k_ref[pl.ds(r0, chunk), :]
        new_v = new_v_ref[pl.ds(r0, chunk), :]
        chosen = (own_row + r0) == long_row
        for h in range(groups):
            qh = q_ref[pl.ds(r0, chunk), h * head_dim:(h + 1) * head_dim]
            result = attend(qh, long_k[...], long_v[...], long_valid, new_k, new_v)
            current = o_ref[pl.ds(r0, chunk), h * head_dim:(h + 1) * head_dim]
            o_ref[pl.ds(r0, chunk), h * head_dim:(h + 1) * head_dim] = jnp.where(
                chosen, result, current
            )


def local_attention(query, new_kv, key_value_pages, page_table, cache_len):
    row_count = query.shape[0]
    pool_pages = key_value_pages.shape[1]
    page_size = key_value_pages.shape[2]
    head_dim = HEAD_SIZE
    table_width = page_table.shape[1]
    base = jnp.full((1,), lax.axis_index("dp") * pool_pages, jnp.int32)
    smem = pl.BlockSpec(memory_space=pltpu.SMEM)
    vmem = pl.BlockSpec(memory_space=pltpu.VMEM)
    rows = row_count * SHORT + table_width * page_size
    return pl.pallas_call(
        attention_kernel,
        out_shape=jax.ShapeDtypeStruct(query.shape, jnp.bfloat16),
        in_specs=[smem, smem, smem, vmem, vmem, vmem, pl.BlockSpec(memory_space=pl.ANY)],
        out_specs=vmem,
        scratch_shapes=[
            pltpu.VMEM((row_count * SHORT, head_dim), key_value_pages.dtype),
            pltpu.VMEM((row_count * SHORT, head_dim), key_value_pages.dtype),
            pltpu.VMEM((table_width * page_size, head_dim), key_value_pages.dtype),
            pltpu.VMEM((table_width * page_size, head_dim), key_value_pages.dtype),
            pltpu.SemaphoreType.DMA((4, row_count)),
        ],
        cost_estimate=pl.CostEstimate(
            flops=4 * 16 * query.shape[1] * rows,
            transcendentals=16 * query.shape[1] // head_dim * rows,
            bytes_accessed=2 * 2 * head_dim * rows,
        ),
    )(page_table, cache_len, base, query, new_kv[0], new_kv[1], key_value_pages)


def ring_shift(x, shift, axis_name, size):
    return lax.ppermute(x, axis_name, [(i, (i + shift) % size) for i in range(size)])


def ring_reduce_scatter(blocks, axis_name, size, index):
    total = lax.dynamic_index_in_dim(blocks, index, 0, keepdims=False).astype(jnp.float32)
    for shift in range(1, size):
        outgoing = lax.dynamic_index_in_dim(blocks, (index + shift) % size, 0, keepdims=False)
        total = total + ring_shift(outgoing, shift, axis_name, size).astype(jnp.float32)
    return total


def ring_all_gather(x, axis_name, size):
    return [x] + [ring_shift(x, shift, axis_name, size) for shift in range(1, size)]


def per_device(
    query,
    new_kv,
    key_value_pages,
    page_table,
    cache_len,
    residual,
    out_weight,
    norm_gain,
    expert_ids,
    combine_weights,
    expert_w1,
    expert_w2,
):
    tensor_size = lax.axis_size("tensor")
    tensor_index = lax.axis_index("tensor")
    attn = local_attention(query, new_kv, key_value_pages, page_table, cache_len)
    row_count, model_width = residual.shape
    share_width = model_width // tensor_size
    share_start = tensor_index * share_width

    split_weight = out_weight.reshape(out_weight.shape[0], tensor_size, share_width)
    partial_proj = jnp.einsum(
        "rk,kuc->urc", attn, split_weight, preferred_element_type=jnp.float32
    )
    summed = ring_reduce_scatter(partial_proj, "tensor", tensor_size, tensor_index)
    residual_share = lax.dynamic_slice_in_dim(residual, share_start, share_width, 1)
    state = residual_share.astype(jnp.float32) + summed
    square_sum = sum(ring_all_gather(jnp.sum(state * state, axis=1, keepdims=True), "tensor", tensor_size))
    mean_square = square_sum / model_width
    gain_share = lax.dynamic_slice_in_dim(norm_gain, share_start, share_width, 0)
    normed = (state * lax.rsqrt(mean_square + 1e-05) * gain_share).astype(jnp.bfloat16)

    local_experts = expert_w1.shape[0]
    top_count = expert_ids.shape[1]
    experts = local_experts * lax.axis_size("dp")
    capacity = min(
        row_count, max(3, (3 * row_count * top_count + 2 * experts - 1) // (2 * experts))
    )
    flat_ids = expert_ids.reshape(-1)
    choice_rows = flat_ids.shape[0]
    row_iota = jnp.arange(choice_rows, dtype=jnp.int32)
    choice_hot = (flat_ids[:, None] == jnp.arange(experts, dtype=jnp.int32)[None, :]).astype(
        jnp.bfloat16
    )
    strictly_lower = (row_iota[:, None] > row_iota[None, :]).astype(jnp.bfloat16)
    earlier = jnp.dot(strictly_lower, choice_hot, preferred_element_type=jnp.float32)
    slot_rank = jnp.sum(earlier * choice_hot.astype(jnp.float32), axis=1).astype(jnp.int32)
    slot_index = (flat_ids * capacity + slot_rank).reshape(row_count, top_count)
    slot_ids = jnp.arange(experts * capacity, dtype=jnp.int32)
    hit = slot_index[:, :, None] == slot_ids[None, None, :]
    placing = jnp.any(hit, axis=1).astype(jnp.bfloat16)
    mixing = jnp.sum(jnp.where(hit, combine_weights[:, :, None], 0.0), axis=1)

    outgoing = jnp.dot(placing.T, normed, preferred_element_type=jnp.float32)
    outgoing = outgoing.astype(jnp.bfloat16).reshape(experts, capacity, share_width)
    mixing = mixing.reshape(row_count, experts, capacity)
    split_w1 = expert_w1.reshape(tensor_size, share_width, 2, expert_w1.shape[-1])
    split_w2 = expert_w2[0].reshape(expert_w2.shape[1], tensor_size, share_width)

    expert_mix = None
    bounds = [0, (capacity + 1) // 2, capacity]
    for lo, hi in zip(bounds[:-1], bounds[1:]):
        slots = hi - lo
        arrived = lax.all_to_all(
            outgoing[:, lo:hi], "dp", split_axis=0, concat_axis=0, tiled=True
        )
        pieces = ring_all_gather(arrived, "tensor", tensor_size)
        gate_up = None
        for shift, piece in enumerate(pieces):
            weight = lax.dynamic_index_in_dim(
                split_w1, (tensor_index - shift) % tensor_size, 0, keepdims=False
            )
            term = jnp.einsum("snc,cgf->sngf", piece, weight, preferred_element_type=jnp.float32)
            gate_up = term if gate_up is None else gate_up + term
        activated = (jax.nn.silu(gate_up[:, :, 0, :]) * gate_up[:, :, 1, :]).astype(
            jnp.bfloat16
        )
        partial_out = jnp.einsum(
            "snf,fuc->usnc", activated, split_w2, preferred_element_type=jnp.float32
        ).astype(jnp.bfloat16)
        expert_sum = ring_reduce_scatter(partial_out, "tensor", tensor_size, tensor_index)
        expert_sum = expert_sum.astype(jnp.bfloat16)
        returned_rows = lax.all_to_all(
            expert_sum, "dp", split_axis=0, concat_axis=0, tiled=True
        )
        part_mix = jnp.dot(
            mixing[:, :, lo:hi].reshape(row_count, experts * slots),
            returned_rows.reshape(experts * slots, share_width).astype(jnp.float32),
            precision=lax.Precision.HIGHEST,
        )
        expert_mix = part_mix if expert_mix is None else expert_mix + part_mix
    return (state + expert_mix).astype(jnp.bfloat16)


def solution(mesh):
    return jax.shard_map(
        per_device,
        mesh=mesh,
        in_specs=(
            P("dp", "tensor"),
            P(None, "dp", "tensor"),
            P(None, "dp", None, "tensor"),
            P("dp", None),
            P("dp"),
            P("dp", None),
            P("tensor", None),
            P(),
            P("dp", None),
            P("dp", None),
            P("dp", None, None, "tensor"),
            P("dp", "tensor", None),
        ),
        out_specs=P("dp", "tensor"),
        check_vma=False,
    )
```

```python
import math

import jax
import jax.numpy as jnp
from jax import lax
from jax.experimental import pallas as pl
from jax.experimental.pallas import tpu as pltpu
from jax.sharding import PartitionSpec as P

HEAD_SIZE = 128
SHORT = 64


def attention_kernel(
    table_ref, len_ref, base_ref, q_ref, new_k_ref, new_v_ref, kv_hbm, o_ref,
    short_k, short_v, long_k, long_v, sem,
):
    rows = q_ref.shape[0]
    head_dim = new_k_ref.shape[1]
    groups = q_ref.shape[1] // head_dim
    table_width = table_ref.shape[1]
    pool_pages = kv_hbm.shape[1]
    page_size = kv_hbm.shape[2]
    chunk = 16
    scale_of_score = 1.0 / math.sqrt(head_dim)
    base = base_ref[0]

    def local_page(r, j):
        return jnp.minimum(jnp.maximum(table_ref[r, j] - base, 0), pool_pages - 1)

    def longest(r, carry):
        best_row, best_len = carry
        length = len_ref[r]
        better = length > best_len
        return jnp.where(better, r, best_row), jnp.where(better, length, best_len)

    long_row, long_len = lax.fori_loop(0, rows, longest, (jnp.int32(0), len_ref[0]))

    def short_copy(r, which, buf):
        return pltpu.make_async_copy(
            kv_hbm.at[which, local_page(r, 0), pl.ds(0, SHORT), :],
            buf.at[pl.ds(r * SHORT, SHORT), :],
            sem.at[which, r],
        )

    def long_copy(j, which, buf):
        return pltpu.make_async_copy(
            kv_hbm.at[which, local_page(long_row, j)],
            buf.at[pl.ds(j * page_size, page_size), :],
            sem.at[2 + which, j],
        )

    @pl.loop(0, rows)
    def _(r):
        short_copy(r, 0, short_k).start()
        short_copy(r, 1, short_v).start()

    @pl.loop(0, table_width)
    def _(j):
        long_copy(j, 0, long_k).start()
        long_copy(j, 1, long_v).start()

    @pl.loop(0, rows)
    def _(r):
        short_copy(r, 0, short_k).wait()
        short_copy(r, 1, short_v).wait()

    def attend(qh, keys, values, valid, new_k, new_v):
        scores = lax.dot_general(
            qh, keys, (((1,), (1,)), ((), ())), preferred_element_type=jnp.float32
        ) * scale_of_score
        fresh = jnp.sum(
            qh.astype(jnp.float32) * new_k.astype(jnp.float32), axis=1, keepdims=True
        ) * scale_of_score
        scores = jnp.where(valid, scores, -1e30)
        row_max = jnp.maximum(jnp.max(scores, axis=1, keepdims=True), fresh)
        weights = jnp.where(valid, jnp.exp(scores - row_max), 0.0)
        weight_new = jnp.exp(fresh - row_max)
        denominator = jnp.sum(weights, axis=1, keepdims=True) + weight_new
        numerator = jnp.dot(
            weights.astype(jnp.bfloat16), values, preferred_element_type=jnp.float32
        )
        numerator = numerator + (
            weight_new.astype(jnp.bfloat16).astype(jnp.float32) * new_v.astype(jnp.float32)
        )
        return (numerator / denominator).astype(o_ref.dtype)

    width = chunk * SHORT
    row = lax.broadcasted_iota(jnp.int32, (chunk, width), 0)
    col = lax.broadcasted_iota(jnp.int32, (chunk, width), 1)

    @pl.loop(0, rows // chunk)
    def _(c):
        r0 = pl.multiple_of(c * chunk, chunk)
        k0 = pl.multiple_of(c * width, width)
        keys = short_k[pl.ds(k0, width), :]
        values = short_v[pl.ds(k0, width), :]
        lengths = jnp.zeros((chunk, 1), jnp.int32)
        for i in range(chunk):
            lengths = jnp.where(row[:, :1] == i, jnp.minimum(len_ref[r0 + i], SHORT), lengths)
        valid = (col >= row * SHORT) & (col < row * SHORT + lengths)
        new_k = new_k_ref[pl.ds(r0, chunk), :]
        new_v = new_v_ref[pl.ds(r0, chunk), :]
        for h in range(groups):
            qh = q_ref[pl.ds(r0, chunk), h * head_dim:(h + 1) * head_dim]
            o_ref[pl.ds(r0, chunk), h * head_dim:(h + 1) * head_dim] = attend(
                qh, keys, values, valid, new_k, new_v
            )

    @pl.loop(0, table_width)
    def _(j):
        long_copy(j, 0, long_k).wait()
        long_copy(j, 1, long_v).wait()

    long_col = lax.broadcasted_iota(jnp.int32, (chunk, table_width * page_size), 1)
    long_valid = long_col < long_len
    own_row = lax.broadcasted_iota(jnp.int32, (chunk, 1), 0)

    @pl.when(long_len >= SHORT)
    def _():
        r0 = pl.multiple_of((long_row // chunk) * chunk, chunk)
        new_k = new_k_ref[pl.ds(r0, chunk), :]
        new_v = new_v_ref[pl.ds(r0, chunk), :]
        chosen = (own_row + r0) == long_row
        for h in range(groups):
            qh = q_ref[pl.ds(r0, chunk), h * head_dim:(h + 1) * head_dim]
            result = attend(qh, long_k[...], long_v[...], long_valid, new_k, new_v)
            current = o_ref[pl.ds(r0, chunk), h * head_dim:(h + 1) * head_dim]
            o_ref[pl.ds(r0, chunk), h * head_dim:(h + 1) * head_dim] = jnp.where(
                chosen, result, current
            )


def local_attention(query, new_kv, key_value_pages, page_table, cache_len):
    row_count = query.shape[0]
    pool_pages = key_value_pages.shape[1]
    page_size = key_value_pages.shape[2]
    head_dim = HEAD_SIZE
    table_width = page_table.shape[1]
    base = jnp.full((1,), lax.axis_index("dp") * pool_pages, jnp.int32)
    smem = pl.BlockSpec(memory_space=pltpu.SMEM)
    vmem = pl.BlockSpec(memory_space=pltpu.VMEM)
    rows = row_count * SHORT + table_width * page_size
    return pl.pallas_call(
        attention_kernel,
        out_shape=jax.ShapeDtypeStruct(query.shape, jnp.bfloat16),
        in_specs=[smem, smem, smem, vmem, vmem, vmem, pl.BlockSpec(memory_space=pl.ANY)],
        out_specs=vmem,
        scratch_shapes=[
            pltpu.VMEM((row_count * SHORT, head_dim), key_value_pages.dtype),
            pltpu.VMEM((row_count * SHORT, head_dim), key_value_pages.dtype),
            pltpu.VMEM((table_width * page_size, head_dim), key_value_pages.dtype),
            pltpu.VMEM((table_width * page_size, head_dim), key_value_pages.dtype),
            pltpu.SemaphoreType.DMA((4, row_count)),
        ],
        cost_estimate=pl.CostEstimate(
            flops=4 * 16 * query.shape[1] * rows,
            transcendentals=16 * query.shape[1] // head_dim * rows,
            bytes_accessed=2 * 2 * head_dim * rows,
        ),
    )(page_table, cache_len, base, query, new_kv[0], new_kv[1], key_value_pages)


def ring_shift(x, shift, axis_name, size):
    return lax.ppermute(x, axis_name, [(i, (i + shift) % size) for i in range(size)])


def ring_reduce_scatter(blocks, axis_name, size, index):
    total = lax.dynamic_index_in_dim(blocks, index, 0, keepdims=False).astype(jnp.float32)
    for shift in range(1, size):
        outgoing = lax.dynamic_index_in_dim(blocks, (index + shift) % size, 0, keepdims=False)
        total = total + ring_shift(outgoing, shift, axis_name, size).astype(jnp.float32)
    return total


def ring_all_gather(x, axis_name, size):
    return [x] + [ring_shift(x, shift, axis_name, size) for shift in range(1, size)]


def dense_all_to_all(x, axis_name):
    lanes = 128
    flat = x.reshape(x.shape[0], x.shape[1] * x.shape[2] // lanes, lanes)
    moved = lax.all_to_all(flat, axis_name, split_axis=0, concat_axis=0, tiled=True)
    return moved.reshape(x.shape)


def per_device(
    query,
    new_kv,
    key_value_pages,
    page_table,
    cache_len,
    residual,
    out_weight,
    norm_gain,
    expert_ids,
    combine_weights,
    expert_w1,
    expert_w2,
):
    tensor_size = lax.axis_size("tensor")
    tensor_index = lax.axis_index("tensor")
    attn = local_attention(query, new_kv, key_value_pages, page_table, cache_len)
    row_count, model_width = residual.shape
    share_width = model_width // tensor_size
    share_start = tensor_index * share_width

    split_weight = out_weight.reshape(out_weight.shape[0], tensor_size, share_width)
    partial_proj = jnp.einsum(
        "rk,kuc->urc", attn, split_weight, preferred_element_type=jnp.float32
    )
    summed = ring_reduce_scatter(partial_proj, "tensor", tensor_size, tensor_index)
    residual_share = lax.dynamic_slice_in_dim(residual, share_start, share_width, 1)
    state = residual_share.astype(jnp.float32) + summed
    square_sum = sum(ring_all_gather(jnp.sum(state * state, axis=1, keepdims=True), "tensor", tensor_size))
    mean_square = square_sum / model_width
    gain_share = lax.dynamic_slice_in_dim(norm_gain, share_start, share_width, 0)
    normed = (state * lax.rsqrt(mean_square + 1e-05) * gain_share).astype(jnp.bfloat16)

    local_experts = expert_w1.shape[0]
    top_count = expert_ids.shape[1]
    experts = local_experts * lax.axis_size("dp")
    capacity = min(
        row_count, max(3, (3 * row_count * top_count + 2 * experts - 1) // (2 * experts))
    )
    flat_ids = expert_ids.reshape(-1)
    choice_rows = flat_ids.shape[0]
    row_iota = jnp.arange(choice_rows, dtype=jnp.int32)
    choice_hot = (flat_ids[:, None] == jnp.arange(experts, dtype=jnp.int32)[None, :]).astype(
        jnp.bfloat16
    )
    strictly_lower = (row_iota[:, None] > row_iota[None, :]).astype(jnp.bfloat16)
    earlier = jnp.dot(strictly_lower, choice_hot, preferred_element_type=jnp.float32)
    slot_rank = jnp.sum(earlier * choice_hot.astype(jnp.float32), axis=1).astype(jnp.int32)
    slot_index = (flat_ids * capacity + slot_rank).reshape(row_count, top_count)
    slot_ids = jnp.arange(experts * capacity, dtype=jnp.int32)
    hit = slot_index[:, :, None] == slot_ids[None, None, :]
    placing = jnp.any(hit, axis=1).astype(jnp.bfloat16)
    mixing = jnp.sum(jnp.where(hit, combine_weights[:, :, None], 0.0), axis=1)

    outgoing = jnp.dot(placing.T, normed, preferred_element_type=jnp.float32)
    outgoing = outgoing.astype(jnp.bfloat16).reshape(experts, capacity, share_width)
    mixing = mixing.reshape(row_count, experts, capacity)
    split_w1 = expert_w1.reshape(tensor_size, share_width, 2, expert_w1.shape[-1])
    split_w2 = expert_w2[0].reshape(expert_w2.shape[1], tensor_size, share_width)

    expert_mix = None
    streams = 3
    bounds = [capacity * i // streams for i in range(streams + 1)]
    for lo, hi in zip(bounds[:-1], bounds[1:]):
        slots = hi - lo
        arrived = dense_all_to_all(outgoing[:, lo:hi], "dp")
        pieces = ring_all_gather(arrived, "tensor", tensor_size)
        gate_up = None
        for shift, piece in enumerate(pieces):
            weight = lax.dynamic_index_in_dim(
                split_w1, (tensor_index - shift) % tensor_size, 0, keepdims=False
            )
            term = jnp.einsum("snc,cgf->sngf", piece, weight, preferred_element_type=jnp.float32)
            gate_up = term if gate_up is None else gate_up + term
        activated = (jax.nn.silu(gate_up[:, :, 0, :]) * gate_up[:, :, 1, :]).astype(
            jnp.bfloat16
        )
        partial_out = jnp.einsum(
            "snf,fuc->usnc", activated, split_w2, preferred_element_type=jnp.float32
        ).astype(jnp.bfloat16)
        expert_sum = ring_reduce_scatter(partial_out, "tensor", tensor_size, tensor_index)
        expert_sum = expert_sum.astype(jnp.bfloat16)
        returned_rows = dense_all_to_all(expert_sum, "dp")
        part_mix = jnp.dot(
            mixing[:, :, lo:hi].reshape(row_count, experts * slots),
            returned_rows.reshape(experts * slots, share_width).astype(jnp.float32),
            precision=lax.Precision.HIGHEST,
        )
        expert_mix = part_mix if expert_mix is None else expert_mix + part_mix
    return (state + expert_mix).astype(jnp.bfloat16)


def solution(mesh):
    return jax.shard_map(
        per_device,
        mesh=mesh,
        in_specs=(
            P("dp", "tensor"),
            P(None, "dp", "tensor"),
            P(None, "dp", None, "tensor"),
            P("dp", None),
            P("dp"),
            P("dp", None),
            P("tensor", None),
            P(),
            P("dp", None),
            P("dp", None),
            P("dp", None, None, "tensor"),
            P("dp", "tensor", None),
        ),
        out_specs=P("dp", "tensor"),
        check_vma=False,
    )
```

```python
import math

import jax
import jax.numpy as jnp
from jax import lax
from jax.experimental import pallas as pl
from jax.experimental.pallas import tpu as pltpu
from jax.sharding import PartitionSpec as P

HEAD_SIZE = 128
SHORT = 64


def attention_kernel(
    table_ref, len_ref, base_ref, q_ref, new_k_ref, new_v_ref, kv_hbm, o_ref,
    short_k, short_v, long_k, long_v, sem,
):
    rows = q_ref.shape[0]
    head_dim = new_k_ref.shape[1]
    groups = q_ref.shape[1] // head_dim
    table_width = table_ref.shape[1]
    pool_pages = kv_hbm.shape[1]
    page_size = kv_hbm.shape[2]
    chunk = 16
    scale_of_score = 1.0 / math.sqrt(head_dim)
    base = base_ref[0]

    def local_page(r, j):
        return jnp.minimum(jnp.maximum(table_ref[r, j] - base, 0), pool_pages - 1)

    def longest(r, carry):
        best_row, best_len = carry
        length = len_ref[r]
        better = length > best_len
        return jnp.where(better, r, best_row), jnp.where(better, length, best_len)

    long_row, long_len = lax.fori_loop(0, rows, longest, (jnp.int32(0), len_ref[0]))

    def short_copy(r, which, buf):
        return pltpu.make_async_copy(
            kv_hbm.at[which, local_page(r, 0), pl.ds(0, SHORT), :],
            buf.at[pl.ds(r * SHORT, SHORT), :],
            sem.at[which, r],
        )

    def long_copy(j, which, buf):
        return pltpu.make_async_copy(
            kv_hbm.at[which, local_page(long_row, j)],
            buf.at[pl.ds(j * page_size, page_size), :],
            sem.at[2 + which, j],
        )

    @pl.loop(0, rows)
    def _(r):
        short_copy(r, 0, short_k).start()
        short_copy(r, 1, short_v).start()

    @pl.loop(0, table_width)
    def _(j):
        long_copy(j, 0, long_k).start()
        long_copy(j, 1, long_v).start()

    @pl.loop(0, rows)
    def _(r):
        short_copy(r, 0, short_k).wait()
        short_copy(r, 1, short_v).wait()

    def attend(qh, keys, values, valid, new_k, new_v):
        scores = lax.dot_general(
            qh, keys, (((1,), (1,)), ((), ())), preferred_element_type=jnp.float32
        ) * scale_of_score
        fresh = jnp.sum(
            qh.astype(jnp.float32) * new_k.astype(jnp.float32), axis=1, keepdims=True
        ) * scale_of_score
        scores = jnp.where(valid, scores, -1e30)
        row_max = jnp.maximum(jnp.max(scores, axis=1, keepdims=True), fresh)
        weights = jnp.where(valid, jnp.exp(scores - row_max), 0.0)
        weight_new = jnp.exp(fresh - row_max)
        denominator = jnp.sum(weights, axis=1, keepdims=True) + weight_new
        numerator = jnp.dot(
            weights.astype(jnp.bfloat16), values, preferred_element_type=jnp.float32
        )
        numerator = numerator + (
            weight_new.astype(jnp.bfloat16).astype(jnp.float32) * new_v.astype(jnp.float32)
        )
        return (numerator / denominator).astype(o_ref.dtype)

    width = chunk * SHORT
    row = lax.broadcasted_iota(jnp.int32, (chunk, width), 0)
    col = lax.broadcasted_iota(jnp.int32, (chunk, width), 1)

    @pl.loop(0, rows // chunk)
    def _(c):
        r0 = pl.multiple_of(c * chunk, chunk)
        k0 = pl.multiple_of(c * width, width)
        keys = short_k[pl.ds(k0, width), :]
        values = short_v[pl.ds(k0, width), :]
        lengths = jnp.zeros((chunk, 1), jnp.int32)
        for i in range(chunk):
            lengths = jnp.where(row[:, :1] == i, jnp.minimum(len_ref[r0 + i], SHORT), lengths)
        valid = (col >= row * SHORT) & (col < row * SHORT + lengths)
        new_k = new_k_ref[pl.ds(r0, chunk), :]
        new_v = new_v_ref[pl.ds(r0, chunk), :]
        for h in range(groups):
            qh = q_ref[pl.ds(r0, chunk), h * head_dim:(h + 1) * head_dim]
            o_ref[pl.ds(r0, chunk), h * head_dim:(h + 1) * head_dim] = attend(
                qh, keys, values, valid, new_k, new_v
            )

    @pl.loop(0, table_width)
    def _(j):
        long_copy(j, 0, long_k).wait()
        long_copy(j, 1, long_v).wait()

    long_col = lax.broadcasted_iota(jnp.int32, (chunk, table_width * page_size), 1)
    long_valid = long_col < long_len
    own_row = lax.broadcasted_iota(jnp.int32, (chunk, 1), 0)

    @pl.when(long_len >= SHORT)
    def _():
        r0 = pl.multiple_of((long_row // chunk) * chunk, chunk)
        new_k = new_k_ref[pl.ds(r0, chunk), :]
        new_v = new_v_ref[pl.ds(r0, chunk), :]
        chosen = (own_row + r0) == long_row
        for h in range(groups):
            qh = q_ref[pl.ds(r0, chunk), h * head_dim:(h + 1) * head_dim]
            result = attend(qh, long_k[...], long_v[...], long_valid, new_k, new_v)
            current = o_ref[pl.ds(r0, chunk), h * head_dim:(h + 1) * head_dim]
            o_ref[pl.ds(r0, chunk), h * head_dim:(h + 1) * head_dim] = jnp.where(
                chosen, result, current
            )


def local_attention(query, new_kv, key_value_pages, page_table, cache_len):
    row_count = query.shape[0]
    pool_pages = key_value_pages.shape[1]
    page_size = key_value_pages.shape[2]
    head_dim = HEAD_SIZE
    table_width = page_table.shape[1]
    base = jnp.full((1,), lax.axis_index("dp") * pool_pages, jnp.int32)
    smem = pl.BlockSpec(memory_space=pltpu.SMEM)
    vmem = pl.BlockSpec(memory_space=pltpu.VMEM)
    rows = row_count * SHORT + table_width * page_size
    return pl.pallas_call(
        attention_kernel,
        out_shape=jax.ShapeDtypeStruct(query.shape, jnp.bfloat16),
        in_specs=[smem, smem, smem, vmem, vmem, vmem, pl.BlockSpec(memory_space=pl.ANY)],
        out_specs=vmem,
        scratch_shapes=[
            pltpu.VMEM((row_count * SHORT, head_dim), key_value_pages.dtype),
            pltpu.VMEM((row_count * SHORT, head_dim), key_value_pages.dtype),
            pltpu.VMEM((table_width * page_size, head_dim), key_value_pages.dtype),
            pltpu.VMEM((table_width * page_size, head_dim), key_value_pages.dtype),
            pltpu.SemaphoreType.DMA((4, row_count)),
        ],
        cost_estimate=pl.CostEstimate(
            flops=4 * 16 * query.shape[1] * rows,
            transcendentals=16 * query.shape[1] // head_dim * rows,
            bytes_accessed=2 * 2 * head_dim * rows,
        ),
    )(page_table, cache_len, base, query, new_kv[0], new_kv[1], key_value_pages)


def ring_shift(x, shift, axis_name, size):
    return lax.ppermute(x, axis_name, [(i, (i + shift) % size) for i in range(size)])


def ring_reduce_scatter(blocks, axis_name, size, index):
    total = lax.dynamic_index_in_dim(blocks, index, 0, keepdims=False).astype(jnp.float32)
    for shift in range(1, size):
        outgoing = lax.dynamic_index_in_dim(blocks, (index + shift) % size, 0, keepdims=False)
        total = total + ring_shift(outgoing, shift, axis_name, size).astype(jnp.float32)
    return total


def ring_all_gather(x, axis_name, size):
    return [x] + [ring_shift(x, shift, axis_name, size) for shift in range(1, size)]


def dense_all_to_all(x, axis_name):
    lanes = 128
    flat = x.reshape(x.shape[0], x.shape[1] * x.shape[2] // lanes, lanes)
    moved = lax.all_to_all(flat, axis_name, split_axis=0, concat_axis=0, tiled=True)
    return moved.reshape(x.shape)


def per_device(
    query,
    new_kv,
    key_value_pages,
    page_table,
    cache_len,
    residual,
    out_weight,
    norm_gain,
    expert_ids,
    combine_weights,
    expert_w1,
    expert_w2,
):
    tensor_size = lax.axis_size("tensor")
    tensor_index = lax.axis_index("tensor")
    attn = local_attention(query, new_kv, key_value_pages, page_table, cache_len)
    row_count, model_width = residual.shape
    share_width = model_width // tensor_size
    share_start = tensor_index * share_width

    split_weight = out_weight.reshape(out_weight.shape[0], tensor_size, share_width)
    partial_proj = jnp.einsum(
        "rk,kuc->urc", attn, split_weight, preferred_element_type=jnp.float32
    )
    summed = ring_reduce_scatter(partial_proj, "tensor", tensor_size, tensor_index)
    residual_share = lax.dynamic_slice_in_dim(residual, share_start, share_width, 1)
    state = residual_share.astype(jnp.float32) + summed
    square_sum = sum(ring_all_gather(jnp.sum(state * state, axis=1, keepdims=True), "tensor", tensor_size))
    mean_square = square_sum / model_width
    gain_share = lax.dynamic_slice_in_dim(norm_gain, share_start, share_width, 0)
    normed = (state * lax.rsqrt(mean_square + 1e-05) * gain_share).astype(jnp.bfloat16)

    local_experts = expert_w1.shape[0]
    top_count = expert_ids.shape[1]
    experts = local_experts * lax.axis_size("dp")
    capacity = min(
        row_count, max(3, (3 * row_count * top_count + 2 * experts - 1) // (2 * experts))
    )
    flat_ids = expert_ids.reshape(-1)
    choice_rows = flat_ids.shape[0]
    row_iota = jnp.arange(choice_rows, dtype=jnp.int32)
    choice_hot = (flat_ids[:, None] == jnp.arange(experts, dtype=jnp.int32)[None, :]).astype(
        jnp.bfloat16
    )
    strictly_lower = (row_iota[:, None] > row_iota[None, :]).astype(jnp.bfloat16)
    earlier = jnp.dot(strictly_lower, choice_hot, preferred_element_type=jnp.float32)
    slot_rank = jnp.sum(earlier * choice_hot.astype(jnp.float32), axis=1).astype(jnp.int32)
    slot_index = (flat_ids * capacity + slot_rank).reshape(row_count, top_count)
    slot_ids = jnp.arange(experts * capacity, dtype=jnp.int32)
    hit = slot_index[:, :, None] == slot_ids[None, None, :]
    placing = jnp.any(hit, axis=1).astype(jnp.bfloat16)
    mixing = jnp.sum(jnp.where(hit, combine_weights[:, :, None], 0.0), axis=1)

    outgoing = jnp.dot(placing.T, normed, preferred_element_type=jnp.float32)
    outgoing = outgoing.astype(jnp.bfloat16).reshape(experts, capacity, share_width)
    mixing = mixing.reshape(row_count, experts, capacity)
    split_w1 = expert_w1.reshape(tensor_size, share_width, 2, expert_w1.shape[-1])
    split_w2 = expert_w2[0].reshape(expert_w2.shape[1], tensor_size, share_width)

    expert_mix = None
    streams = 1
    bounds = [capacity * i // streams for i in range(streams + 1)]
    for lo, hi in zip(bounds[:-1], bounds[1:]):
        slots = hi - lo
        arrived = dense_all_to_all(outgoing[:, lo:hi], "dp")
        pieces = ring_all_gather(arrived, "tensor", tensor_size)
        gate_up = None
        for shift, piece in enumerate(pieces):
            weight = lax.dynamic_index_in_dim(
                split_w1, (tensor_index - shift) % tensor_size, 0, keepdims=False
            )
            term = jnp.einsum("snc,cgf->sngf", piece, weight, preferred_element_type=jnp.float32)
            gate_up = term if gate_up is None else gate_up + term
        activated = (jax.nn.silu(gate_up[:, :, 0, :]) * gate_up[:, :, 1, :]).astype(
            jnp.bfloat16
        )
        partial_out = jnp.einsum(
            "snf,fuc->usnc", activated, split_w2, preferred_element_type=jnp.float32
        ).astype(jnp.bfloat16)
        expert_sum = ring_reduce_scatter(partial_out, "tensor", tensor_size, tensor_index)
        expert_sum = expert_sum.astype(jnp.bfloat16)
        returned_rows = dense_all_to_all(expert_sum, "dp")
        part_mix = jnp.dot(
            mixing[:, :, lo:hi].reshape(row_count, experts * slots),
            returned_rows.reshape(experts * slots, share_width).astype(jnp.float32),
            precision=lax.Precision.HIGHEST,
        )
        expert_mix = part_mix if expert_mix is None else expert_mix + part_mix
    return (state + expert_mix).astype(jnp.bfloat16)


def solution(mesh):
    return jax.shard_map(
        per_device,
        mesh=mesh,
        in_specs=(
            P("dp", "tensor"),
            P(None, "dp", "tensor"),
            P(None, "dp", None, "tensor"),
            P("dp", None),
            P("dp"),
            P("dp", None),
            P("tensor", None),
            P(),
            P("dp", None),
            P("dp", None),
            P("dp", None, None, "tensor"),
            P("dp", "tensor", None),
        ),
        out_specs=P("dp", "tensor"),
        check_vma=False,
    )
```

```python
import math

import jax
import jax.numpy as jnp
from jax import lax
from jax.experimental import pallas as pl
from jax.experimental.pallas import tpu as pltpu
from jax.sharding import PartitionSpec as P

HEAD_SIZE = 128
SHORT = 64


def attention_kernel(
    table_ref, len_ref, base_ref, q_ref, new_k_ref, new_v_ref, kv_hbm, o_ref,
    short_k, short_v, long_k, long_v, sem,
):
    rows = q_ref.shape[0]
    head_dim = new_k_ref.shape[1]
    groups = q_ref.shape[1] // head_dim
    table_width = table_ref.shape[1]
    pool_pages = kv_hbm.shape[1]
    page_size = kv_hbm.shape[2]
    chunk = 16
    scale_of_score = 1.0 / math.sqrt(head_dim)
    base = base_ref[0]

    def local_page(r, j):
        return jnp.minimum(jnp.maximum(table_ref[r, j] - base, 0), pool_pages - 1)

    def longest(r, carry):
        best_row, best_len = carry
        length = len_ref[r]
        better = length > best_len
        return jnp.where(better, r, best_row), jnp.where(better, length, best_len)

    long_row, long_len = lax.fori_loop(0, rows, longest, (jnp.int32(0), len_ref[0]))

    def short_copy(r, which, buf):
        return pltpu.make_async_copy(
            kv_hbm.at[which, local_page(r, 0), pl.ds(0, SHORT), :],
            buf.at[pl.ds(r * SHORT, SHORT), :],
            sem.at[which, r],
        )

    def long_copy(j, which, buf):
        return pltpu.make_async_copy(
            kv_hbm.at[which, local_page(long_row, j)],
            buf.at[pl.ds(j * page_size, page_size), :],
            sem.at[2 + which, j],
        )

    @pl.loop(0, rows)
    def _(r):
        short_copy(r, 0, short_k).start()
        short_copy(r, 1, short_v).start()

    @pl.loop(0, table_width)
    def _(j):
        long_copy(j, 0, long_k).start()
        long_copy(j, 1, long_v).start()

    @pl.loop(0, rows)
    def _(r):
        short_copy(r, 0, short_k).wait()
        short_copy(r, 1, short_v).wait()

    def attend(qh, keys, values, valid, new_k, new_v):
        scores = lax.dot_general(
            qh, keys, (((1,), (1,)), ((), ())), preferred_element_type=jnp.float32
        ) * scale_of_score
        fresh = jnp.sum(
            qh.astype(jnp.float32) * new_k.astype(jnp.float32), axis=1, keepdims=True
        ) * scale_of_score
        scores = jnp.where(valid, scores, -1e30)
        row_max = jnp.maximum(jnp.max(scores, axis=1, keepdims=True), fresh)
        weights = jnp.where(valid, jnp.exp(scores - row_max), 0.0)
        weight_new = jnp.exp(fresh - row_max)
        denominator = jnp.sum(weights, axis=1, keepdims=True) + weight_new
        numerator = jnp.dot(
            weights.astype(jnp.bfloat16), values, preferred_element_type=jnp.float32
        )
        numerator = numerator + (
            weight_new.astype(jnp.bfloat16).astype(jnp.float32) * new_v.astype(jnp.float32)
        )
        return (numerator / denominator).astype(o_ref.dtype)

    width = chunk * SHORT
    row = lax.broadcasted_iota(jnp.int32, (chunk, width), 0)
    col = lax.broadcasted_iota(jnp.int32, (chunk, width), 1)

    @pl.loop(0, rows // chunk)
    def _(c):
        r0 = pl.multiple_of(c * chunk, chunk)
        k0 = pl.multiple_of(c * width, width)
        keys = short_k[pl.ds(k0, width), :]
        values = short_v[pl.ds(k0, width), :]
        lengths = jnp.zeros((chunk, 1), jnp.int32)
        for i in range(chunk):
            lengths = jnp.where(row[:, :1] == i, jnp.minimum(len_ref[r0 + i], SHORT), lengths)
        valid = (col >= row * SHORT) & (col < row * SHORT + lengths)
        new_k = new_k_ref[pl.ds(r0, chunk), :]
        new_v = new_v_ref[pl.ds(r0, chunk), :]
        for h in range(groups):
            qh = q_ref[pl.ds(r0, chunk), h * head_dim:(h + 1) * head_dim]
            o_ref[pl.ds(r0, chunk), h * head_dim:(h + 1) * head_dim] = attend(
                qh, keys, values, valid, new_k, new_v
            )

    @pl.loop(0, table_width)
    def _(j):
        long_copy(j, 0, long_k).wait()
        long_copy(j, 1, long_v).wait()

    long_col = lax.broadcasted_iota(jnp.int32, (chunk, table_width * page_size), 1)
    long_valid = long_col < long_len
    own_row = lax.broadcasted_iota(jnp.int32, (chunk, 1), 0)

    @pl.when(long_len >= SHORT)
    def _():
        r0 = pl.multiple_of((long_row // chunk) * chunk, chunk)
        new_k = new_k_ref[pl.ds(r0, chunk), :]
        new_v = new_v_ref[pl.ds(r0, chunk), :]
        chosen = (own_row + r0) == long_row
        for h in range(groups):
            qh = q_ref[pl.ds(r0, chunk), h * head_dim:(h + 1) * head_dim]
            result = attend(qh, long_k[...], long_v[...], long_valid, new_k, new_v)
            current = o_ref[pl.ds(r0, chunk), h * head_dim:(h + 1) * head_dim]
            o_ref[pl.ds(r0, chunk), h * head_dim:(h + 1) * head_dim] = jnp.where(
                chosen, result, current
            )


def local_attention(query, new_kv, key_value_pages, page_table, cache_len):
    row_count = query.shape[0]
    pool_pages = key_value_pages.shape[1]
    page_size = key_value_pages.shape[2]
    head_dim = HEAD_SIZE
    table_width = page_table.shape[1]
    base = jnp.full((1,), lax.axis_index("dp") * pool_pages, jnp.int32)
    smem = pl.BlockSpec(memory_space=pltpu.SMEM)
    vmem = pl.BlockSpec(memory_space=pltpu.VMEM)
    rows = row_count * SHORT + table_width * page_size
    return pl.pallas_call(
        attention_kernel,
        out_shape=jax.ShapeDtypeStruct(query.shape, jnp.bfloat16),
        in_specs=[smem, smem, smem, vmem, vmem, vmem, pl.BlockSpec(memory_space=pl.ANY)],
        out_specs=vmem,
        scratch_shapes=[
            pltpu.VMEM((row_count * SHORT, head_dim), key_value_pages.dtype),
            pltpu.VMEM((row_count * SHORT, head_dim), key_value_pages.dtype),
            pltpu.VMEM((table_width * page_size, head_dim), key_value_pages.dtype),
            pltpu.VMEM((table_width * page_size, head_dim), key_value_pages.dtype),
            pltpu.SemaphoreType.DMA((4, row_count)),
        ],
        cost_estimate=pl.CostEstimate(
            flops=4 * 16 * query.shape[1] * rows,
            transcendentals=16 * query.shape[1] // head_dim * rows,
            bytes_accessed=2 * 2 * head_dim * rows,
        ),
    )(page_table, cache_len, base, query, new_kv[0], new_kv[1], key_value_pages)


def ring_shift(x, shift, axis_name, size):
    return lax.ppermute(x, axis_name, [(i, (i + shift) % size) for i in range(size)])


def ring_reduce_scatter(blocks, axis_name, size, index):
    total = lax.dynamic_index_in_dim(blocks, index, 0, keepdims=False).astype(jnp.float32)
    for shift in range(1, size):
        outgoing = lax.dynamic_index_in_dim(blocks, (index + shift) % size, 0, keepdims=False)
        total = total + ring_shift(outgoing, shift, axis_name, size).astype(jnp.float32)
    return total


def ring_all_gather(x, axis_name, size):
    return [x] + [ring_shift(x, shift, axis_name, size) for shift in range(1, size)]


def dense_all_to_all(x, axis_name):
    lanes = 128
    flat = x.reshape(x.shape[0], x.shape[1] * x.shape[2] // lanes, lanes)
    moved = lax.all_to_all(flat, axis_name, split_axis=0, concat_axis=0, tiled=True)
    return moved.reshape(x.shape)


def per_device(
    query,
    new_kv,
    key_value_pages,
    page_table,
    cache_len,
    residual,
    out_weight,
    norm_gain,
    expert_ids,
    combine_weights,
    expert_w1,
    expert_w2,
):
    tensor_size = lax.axis_size("tensor")
    tensor_index = lax.axis_index("tensor")
    attn = local_attention(query, new_kv, key_value_pages, page_table, cache_len)
    row_count, model_width = residual.shape
    share_width = model_width // tensor_size
    share_start = tensor_index * share_width

    split_weight = out_weight.reshape(out_weight.shape[0], tensor_size, share_width)
    partial_proj = jnp.einsum(
        "rk,kuc->urc", attn, split_weight, preferred_element_type=jnp.float32
    )
    summed = ring_reduce_scatter(partial_proj, "tensor", tensor_size, tensor_index)
    residual_share = lax.dynamic_slice_in_dim(residual, share_start, share_width, 1)
    state = residual_share.astype(jnp.float32) + summed
    square_sum = sum(ring_all_gather(jnp.sum(state * state, axis=1, keepdims=True), "tensor", tensor_size))
    mean_square = square_sum / model_width
    gain_share = lax.dynamic_slice_in_dim(norm_gain, share_start, share_width, 0)
    normed = (state * lax.rsqrt(mean_square + 1e-05) * gain_share).astype(jnp.bfloat16)

    local_experts = expert_w1.shape[0]
    top_count = expert_ids.shape[1]
    experts = local_experts * lax.axis_size("dp")
    capacity = min(
        row_count, max(3, (3 * row_count * top_count + 2 * experts - 1) // (2 * experts))
    )
    flat_ids = expert_ids.reshape(-1)
    choice_rows = flat_ids.shape[0]
    row_iota = jnp.arange(choice_rows, dtype=jnp.int32)
    choice_hot = (flat_ids[:, None] == jnp.arange(experts, dtype=jnp.int32)[None, :]).astype(
        jnp.bfloat16
    )
    strictly_lower = (row_iota[:, None] > row_iota[None, :]).astype(jnp.bfloat16)
    earlier = jnp.dot(strictly_lower, choice_hot, preferred_element_type=jnp.float32)
    slot_rank = jnp.sum(earlier * choice_hot.astype(jnp.float32), axis=1).astype(jnp.int32)
    slot_index = (flat_ids * capacity + slot_rank).reshape(row_count, top_count)
    slot_ids = jnp.arange(experts * capacity, dtype=jnp.int32)
    hit = slot_index[:, :, None] == slot_ids[None, None, :]
    placing = jnp.any(hit, axis=1).astype(jnp.bfloat16)
    mixing = jnp.sum(jnp.where(hit, combine_weights[:, :, None], 0.0), axis=1)

    outgoing = jnp.dot(placing.T, normed, preferred_element_type=jnp.float32)
    outgoing = outgoing.astype(jnp.bfloat16).reshape(experts, capacity, share_width)
    mixing = mixing.reshape(row_count, experts, capacity)
    split_w1 = expert_w1.reshape(tensor_size, share_width, 2, expert_w1.shape[-1])
    split_w2 = expert_w2[0].reshape(expert_w2.shape[1], tensor_size, share_width)

    expert_mix = None
    bounds = [0, capacity // 3, capacity]
    for lo, hi in zip(bounds[:-1], bounds[1:]):
        slots = hi - lo
        arrived = dense_all_to_all(outgoing[:, lo:hi], "dp")
        pieces = ring_all_gather(arrived, "tensor", tensor_size)
        gate_up = None
        for shift, piece in enumerate(pieces):
            weight = lax.dynamic_index_in_dim(
                split_w1, (tensor_index - shift) % tensor_size, 0, keepdims=False
            )
            term = jnp.einsum("snc,cgf->sngf", piece, weight, preferred_element_type=jnp.float32)
            gate_up = term if gate_up is None else gate_up + term
        activated = (jax.nn.silu(gate_up[:, :, 0, :]) * gate_up[:, :, 1, :]).astype(
            jnp.bfloat16
        )
        partial_out = jnp.einsum(
            "snf,fuc->usnc", activated, split_w2, preferred_element_type=jnp.float32
        ).astype(jnp.bfloat16)
        expert_sum = ring_reduce_scatter(partial_out, "tensor", tensor_size, tensor_index)
        expert_sum = expert_sum.astype(jnp.bfloat16)
        returned_rows = dense_all_to_all(expert_sum, "dp")
        part_mix = jnp.dot(
            mixing[:, :, lo:hi].reshape(row_count, experts * slots),
            returned_rows.reshape(experts * slots, share_width).astype(jnp.float32),
            precision=lax.Precision.HIGHEST,
        )
        expert_mix = part_mix if expert_mix is None else expert_mix + part_mix
    return (state + expert_mix).astype(jnp.bfloat16)


def solution(mesh):
    return jax.shard_map(
        per_device,
        mesh=mesh,
        in_specs=(
            P("dp", "tensor"),
            P(None, "dp", "tensor"),
            P(None, "dp", None, "tensor"),
            P("dp", None),
            P("dp"),
            P("dp", None),
            P("tensor", None),
            P(),
            P("dp", None),
            P("dp", None),
            P("dp", None, None, "tensor"),
            P("dp", "tensor", None),
        ),
        out_specs=P("dp", "tensor"),
        check_vma=False,
    )
```

```python
import math

import jax
import jax.numpy as jnp
from jax import lax
from jax.experimental import pallas as pl
from jax.experimental.pallas import tpu as pltpu
from jax.sharding import PartitionSpec as P

HEAD_SIZE = 128
SHORT = 64


def attention_kernel(
    table_ref, len_ref, base_ref, q_ref, new_k_ref, new_v_ref, kv_hbm, o_ref,
    short_k, short_v, long_k, long_v, sem,
):
    rows = q_ref.shape[0]
    head_dim = new_k_ref.shape[1]
    groups = q_ref.shape[1] // head_dim
    table_width = table_ref.shape[1]
    pool_pages = kv_hbm.shape[1]
    page_size = kv_hbm.shape[2]
    chunk = 16
    scale_of_score = 1.0 / math.sqrt(head_dim)
    base = base_ref[0]

    def local_page(r, j):
        return jnp.minimum(jnp.maximum(table_ref[r, j] - base, 0), pool_pages - 1)

    def longest(r, carry):
        best_row, best_len = carry
        length = len_ref[r]
        better = length > best_len
        return jnp.where(better, r, best_row), jnp.where(better, length, best_len)

    long_row, long_len = lax.fori_loop(0, rows, longest, (jnp.int32(0), len_ref[0]))

    def short_copy(r, which, buf):
        return pltpu.make_async_copy(
            kv_hbm.at[which, local_page(r, 0), pl.ds(0, SHORT), :],
            buf.at[pl.ds(r * SHORT, SHORT), :],
            sem.at[which, r],
        )

    def long_copy(j, which, buf):
        return pltpu.make_async_copy(
            kv_hbm.at[which, local_page(long_row, j)],
            buf.at[pl.ds(j * page_size, page_size), :],
            sem.at[2 + which, j],
        )

    @pl.loop(0, rows)
    def _(r):
        short_copy(r, 0, short_k).start()
        short_copy(r, 1, short_v).start()

    @pl.loop(0, table_width)
    def _(j):
        long_copy(j, 0, long_k).start()
        long_copy(j, 1, long_v).start()

    @pl.loop(0, rows)
    def _(r):
        short_copy(r, 0, short_k).wait()
        short_copy(r, 1, short_v).wait()

    def attend(qh, keys, values, valid, new_k, new_v):
        scores = lax.dot_general(
            qh, keys, (((1,), (1,)), ((), ())), preferred_element_type=jnp.float32
        ) * scale_of_score
        fresh = jnp.sum(
            qh.astype(jnp.float32) * new_k.astype(jnp.float32), axis=1, keepdims=True
        ) * scale_of_score
        scores = jnp.where(valid, scores, -1e30)
        row_max = jnp.maximum(jnp.max(scores, axis=1, keepdims=True), fresh)
        weights = jnp.where(valid, jnp.exp(scores - row_max), 0.0)
        weight_new = jnp.exp(fresh - row_max)
        denominator = jnp.sum(weights, axis=1, keepdims=True) + weight_new
        numerator = jnp.dot(
            weights.astype(jnp.bfloat16), values, preferred_element_type=jnp.float32
        )
        numerator = numerator + (
            weight_new.astype(jnp.bfloat16).astype(jnp.float32) * new_v.astype(jnp.float32)
        )
        return (numerator / denominator).astype(o_ref.dtype)

    width = chunk * SHORT
    row = lax.broadcasted_iota(jnp.int32, (chunk, width), 0)
    col = lax.broadcasted_iota(jnp.int32, (chunk, width), 1)

    @pl.loop(0, rows // chunk)
    def _(c):
        r0 = pl.multiple_of(c * chunk, chunk)
        k0 = pl.multiple_of(c * width, width)
        keys = short_k[pl.ds(k0, width), :]
        values = short_v[pl.ds(k0, width), :]
        lengths = jnp.zeros((chunk, 1), jnp.int32)
        for i in range(chunk):
            lengths = jnp.where(row[:, :1] == i, jnp.minimum(len_ref[r0 + i], SHORT), lengths)
        valid = (col >= row * SHORT) & (col < row * SHORT + lengths)
        new_k = new_k_ref[pl.ds(r0, chunk), :]
        new_v = new_v_ref[pl.ds(r0, chunk), :]
        for h in range(groups):
            qh = q_ref[pl.ds(r0, chunk), h * head_dim:(h + 1) * head_dim]
            o_ref[pl.ds(r0, chunk), h * head_dim:(h + 1) * head_dim] = attend(
                qh, keys, values, valid, new_k, new_v
            )

    @pl.loop(0, table_width)
    def _(j):
        long_copy(j, 0, long_k).wait()
        long_copy(j, 1, long_v).wait()

    long_col = lax.broadcasted_iota(jnp.int32, (chunk, table_width * page_size), 1)
    long_valid = long_col < long_len
    own_row = lax.broadcasted_iota(jnp.int32, (chunk, 1), 0)

    @pl.when(long_len >= SHORT)
    def _():
        r0 = pl.multiple_of((long_row // chunk) * chunk, chunk)
        new_k = new_k_ref[pl.ds(r0, chunk), :]
        new_v = new_v_ref[pl.ds(r0, chunk), :]
        chosen = (own_row + r0) == long_row
        for h in range(groups):
            qh = q_ref[pl.ds(r0, chunk), h * head_dim:(h + 1) * head_dim]
            result = attend(qh, long_k[...], long_v[...], long_valid, new_k, new_v)
            current = o_ref[pl.ds(r0, chunk), h * head_dim:(h + 1) * head_dim]
            o_ref[pl.ds(r0, chunk), h * head_dim:(h + 1) * head_dim] = jnp.where(
                chosen, result, current
            )


def local_attention(query, new_kv, key_value_pages, page_table, cache_len):
    row_count = query.shape[0]
    pool_pages = key_value_pages.shape[1]
    page_size = key_value_pages.shape[2]
    head_dim = HEAD_SIZE
    table_width = page_table.shape[1]
    base = jnp.full((1,), lax.axis_index("dp") * pool_pages, jnp.int32)
    smem = pl.BlockSpec(memory_space=pltpu.SMEM)
    vmem = pl.BlockSpec(memory_space=pltpu.VMEM)
    rows = row_count * SHORT + table_width * page_size
    return pl.pallas_call(
        attention_kernel,
        out_shape=jax.ShapeDtypeStruct(query.shape, jnp.bfloat16),
        in_specs=[smem, smem, smem, vmem, vmem, vmem, pl.BlockSpec(memory_space=pl.ANY)],
        out_specs=vmem,
        scratch_shapes=[
            pltpu.VMEM((row_count * SHORT, head_dim), key_value_pages.dtype),
            pltpu.VMEM((row_count * SHORT, head_dim), key_value_pages.dtype),
            pltpu.VMEM((table_width * page_size, head_dim), key_value_pages.dtype),
            pltpu.VMEM((table_width * page_size, head_dim), key_value_pages.dtype),
            pltpu.SemaphoreType.DMA((4, row_count)),
        ],
        cost_estimate=pl.CostEstimate(
            flops=4 * 16 * query.shape[1] * rows,
            transcendentals=16 * query.shape[1] // head_dim * rows,
            bytes_accessed=2 * 2 * head_dim * rows,
        ),
    )(page_table, cache_len, base, query, new_kv[0], new_kv[1], key_value_pages)


def ring_shift(x, shift, axis_name, size):
    return lax.ppermute(x, axis_name, [(i, (i + shift) % size) for i in range(size)])


def ring_reduce_scatter(blocks, axis_name, size, index):
    total = lax.dynamic_index_in_dim(blocks, index, 0, keepdims=False).astype(jnp.float32)
    for shift in range(1, size):
        outgoing = lax.dynamic_index_in_dim(blocks, (index + shift) % size, 0, keepdims=False)
        total = total + ring_shift(outgoing, shift, axis_name, size).astype(jnp.float32)
    return total


def ring_all_gather(x, axis_name, size):
    return [x] + [ring_shift(x, shift, axis_name, size) for shift in range(1, size)]


def dense_all_to_all(x, axis_name):
    lanes = 128
    flat = x.reshape(x.shape[0], x.shape[1] * x.shape[2] // lanes, lanes)
    moved = lax.all_to_all(flat, axis_name, split_axis=0, concat_axis=0, tiled=True)
    return moved.reshape(x.shape)


def ring_all_gather_two_step(x, axis_name, size, index):
    half = x.shape[0] // 2
    from_left = ring_shift(x, 1, axis_name, size)
    from_right = ring_shift(x, size - 1, axis_name, size)
    far = jnp.concatenate(
        [
            ring_shift(from_left[:half], 1, axis_name, size),
            ring_shift(from_right[half:], size - 1, axis_name, size),
        ],
        axis=0,
    )
    return [x, from_left, far, from_right]


def ring_reduce_scatter_two_step(blocks, axis_name, size, index):
    def block(shift):
        return lax.dynamic_index_in_dim(blocks, (index + shift) % size, 0, keepdims=False)

    far = block(2)
    half = far.shape[0] // 2
    to_left_far = ring_shift(far[:half], 1, axis_name, size)
    to_right_far = ring_shift(far[half:], size - 1, axis_name, size)
    from_left = ring_shift(block(1), 1, axis_name, size).astype(jnp.float32)
    from_right = ring_shift(block(size - 1), size - 1, axis_name, size).astype(jnp.float32)
    far_first = ring_shift(to_left_far, 1, axis_name, size).astype(jnp.float32)
    far_second = ring_shift(to_right_far, size - 1, axis_name, size).astype(jnp.float32)
    total = block(0).astype(jnp.float32) + from_left + from_right
    return total + jnp.concatenate([far_first, far_second], axis=0)


def per_device(
    query,
    new_kv,
    key_value_pages,
    page_table,
    cache_len,
    residual,
    out_weight,
    norm_gain,
    expert_ids,
    combine_weights,
    expert_w1,
    expert_w2,
):
    tensor_size = lax.axis_size("tensor")
    tensor_index = lax.axis_index("tensor")
    attn = local_attention(query, new_kv, key_value_pages, page_table, cache_len)
    row_count, model_width = residual.shape
    share_width = model_width // tensor_size
    share_start = tensor_index * share_width

    split_weight = out_weight.reshape(out_weight.shape[0], tensor_size, share_width)
    partial_proj = jnp.einsum(
        "rk,kuc->urc", attn, split_weight, preferred_element_type=jnp.float32
    )
    summed = ring_reduce_scatter(partial_proj, "tensor", tensor_size, tensor_index)
    residual_share = lax.dynamic_slice_in_dim(residual, share_start, share_width, 1)
    state = residual_share.astype(jnp.float32) + summed
    square_sum = sum(ring_all_gather(jnp.sum(state * state, axis=1, keepdims=True), "tensor", tensor_size))
    mean_square = square_sum / model_width
    gain_share = lax.dynamic_slice_in_dim(norm_gain, share_start, share_width, 0)
    normed = (state * lax.rsqrt(mean_square + 1e-05) * gain_share).astype(jnp.bfloat16)

    local_experts = expert_w1.shape[0]
    top_count = expert_ids.shape[1]
    experts = local_experts * lax.axis_size("dp")
    capacity = min(
        row_count, max(3, (3 * row_count * top_count + 2 * experts - 1) // (2 * experts))
    )
    flat_ids = expert_ids.reshape(-1)
    choice_rows = flat_ids.shape[0]
    row_iota = jnp.arange(choice_rows, dtype=jnp.int32)
    choice_hot = (flat_ids[:, None] == jnp.arange(experts, dtype=jnp.int32)[None, :]).astype(
        jnp.bfloat16
    )
    strictly_lower = (row_iota[:, None] > row_iota[None, :]).astype(jnp.bfloat16)
    earlier = jnp.dot(strictly_lower, choice_hot, preferred_element_type=jnp.float32)
    slot_rank = jnp.sum(earlier * choice_hot.astype(jnp.float32), axis=1).astype(jnp.int32)
    slot_index = (flat_ids * capacity + slot_rank).reshape(row_count, top_count)
    slot_ids = jnp.arange(experts * capacity, dtype=jnp.int32)
    hit = slot_index[:, :, None] == slot_ids[None, None, :]
    placing = jnp.any(hit, axis=1).astype(jnp.bfloat16)
    mixing = jnp.sum(jnp.where(hit, combine_weights[:, :, None], 0.0), axis=1)

    outgoing = jnp.dot(placing.T, normed, preferred_element_type=jnp.float32)
    outgoing = outgoing.astype(jnp.bfloat16).reshape(experts, capacity, share_width)
    mixing = mixing.reshape(row_count, experts, capacity)
    split_w1 = expert_w1.reshape(tensor_size, share_width, 2, expert_w1.shape[-1])
    split_w2 = expert_w2[0].reshape(expert_w2.shape[1], tensor_size, share_width)

    expert_mix = None
    streams = 1
    bounds = [capacity * i // streams for i in range(streams + 1)]
    for lo, hi in zip(bounds[:-1], bounds[1:]):
        slots = hi - lo
        arrived = dense_all_to_all(outgoing[:, lo:hi], "dp")
        pieces = ring_all_gather_two_step(arrived, "tensor", tensor_size, tensor_index)
        gate_up = None
        for shift, piece in enumerate(pieces):
            weight = lax.dynamic_index_in_dim(
                split_w1, (tensor_index - shift) % tensor_size, 0, keepdims=False
            )
            term = jnp.einsum("snc,cgf->sngf", piece, weight, preferred_element_type=jnp.float32)
            gate_up = term if gate_up is None else gate_up + term
        activated = (jax.nn.silu(gate_up[:, :, 0, :]) * gate_up[:, :, 1, :]).astype(
            jnp.bfloat16
        )
        partial_out = jnp.einsum(
            "snf,fuc->usnc", activated, split_w2, preferred_element_type=jnp.float32
        ).astype(jnp.bfloat16)
        expert_sum = ring_reduce_scatter_two_step(
            partial_out, "tensor", tensor_size, tensor_index
        )
        expert_sum = expert_sum.astype(jnp.bfloat16)
        returned_rows = dense_all_to_all(expert_sum, "dp")
        part_mix = jnp.dot(
            mixing[:, :, lo:hi].reshape(row_count, experts * slots),
            returned_rows.reshape(experts * slots, share_width).astype(jnp.float32),
            precision=lax.Precision.HIGHEST,
        )
        expert_mix = part_mix if expert_mix is None else expert_mix + part_mix
    return (state + expert_mix).astype(jnp.bfloat16)


def solution(mesh):
    return jax.shard_map(
        per_device,
        mesh=mesh,
        in_specs=(
            P("dp", "tensor"),
            P(None, "dp", "tensor"),
            P(None, "dp", None, "tensor"),
            P("dp", None),
            P("dp"),
            P("dp", None),
            P("tensor", None),
            P(),
            P("dp", None),
            P("dp", None),
            P("dp", None, None, "tensor"),
            P("dp", "tensor", None),
        ),
        out_specs=P("dp", "tensor"),
        check_vma=False,
    )
```

```python
import math

import jax
import jax.numpy as jnp
from jax import lax
from jax.experimental import pallas as pl
from jax.experimental.pallas import tpu as pltpu
from jax.sharding import PartitionSpec as P

HEAD_SIZE = 128
SHORT = 64


def attention_kernel(
    table_ref, len_ref, base_ref, q_ref, new_k_ref, new_v_ref, kv_hbm, o_ref,
    short_k, short_v, long_k, long_v, sem,
):
    rows = q_ref.shape[0]
    head_dim = new_k_ref.shape[1]
    groups = q_ref.shape[1] // head_dim
    table_width = table_ref.shape[1]
    pool_pages = kv_hbm.shape[1]
    page_size = kv_hbm.shape[2]
    chunk = 16
    scale_of_score = 1.0 / math.sqrt(head_dim)
    base = base_ref[0]

    def local_page(r, j):
        return jnp.minimum(jnp.maximum(table_ref[r, j] - base, 0), pool_pages - 1)

    def longest(r, carry):
        best_row, best_len = carry
        length = len_ref[r]
        better = length > best_len
        return jnp.where(better, r, best_row), jnp.where(better, length, best_len)

    long_row, long_len = lax.fori_loop(0, rows, longest, (jnp.int32(0), len_ref[0]))

    def short_copy(r, which, buf):
        return pltpu.make_async_copy(
            kv_hbm.at[which, local_page(r, 0), pl.ds(0, SHORT), :],
            buf.at[pl.ds(r * SHORT, SHORT), :],
            sem.at[which, r],
        )

    def long_copy(j, which, buf):
        return pltpu.make_async_copy(
            kv_hbm.at[which, local_page(long_row, j)],
            buf.at[pl.ds(j * page_size, page_size), :],
            sem.at[2 + which, j],
        )

    @pl.loop(0, rows)
    def _(r):
        short_copy(r, 0, short_k).start()
        short_copy(r, 1, short_v).start()

    @pl.loop(0, table_width)
    def _(j):
        long_copy(j, 0, long_k).start()
        long_copy(j, 1, long_v).start()

    @pl.loop(0, rows)
    def _(r):
        short_copy(r, 0, short_k).wait()
        short_copy(r, 1, short_v).wait()

    def attend(qh, keys, values, valid, new_k, new_v):
        scores = lax.dot_general(
            qh, keys, (((1,), (1,)), ((), ())), preferred_element_type=jnp.float32
        ) * scale_of_score
        fresh = jnp.sum(
            qh.astype(jnp.float32) * new_k.astype(jnp.float32), axis=1, keepdims=True
        ) * scale_of_score
        scores = jnp.where(valid, scores, -1e30)
        row_max = jnp.maximum(jnp.max(scores, axis=1, keepdims=True), fresh)
        weights = jnp.where(valid, jnp.exp(scores - row_max), 0.0)
        weight_new = jnp.exp(fresh - row_max)
        denominator = jnp.sum(weights, axis=1, keepdims=True) + weight_new
        numerator = jnp.dot(
            weights.astype(jnp.bfloat16), values, preferred_element_type=jnp.float32
        )
        numerator = numerator + (
            weight_new.astype(jnp.bfloat16).astype(jnp.float32) * new_v.astype(jnp.float32)
        )
        return (numerator / denominator).astype(o_ref.dtype)

    width = chunk * SHORT
    row = lax.broadcasted_iota(jnp.int32, (chunk, width), 0)
    col = lax.broadcasted_iota(jnp.int32, (chunk, width), 1)

    @pl.loop(0, rows // chunk)
    def _(c):
        r0 = pl.multiple_of(c * chunk, chunk)
        k0 = pl.multiple_of(c * width, width)
        keys = short_k[pl.ds(k0, width), :]
        values = short_v[pl.ds(k0, width), :]
        lengths = jnp.zeros((chunk, 1), jnp.int32)
        for i in range(chunk):
            lengths = jnp.where(row[:, :1] == i, jnp.minimum(len_ref[r0 + i], SHORT), lengths)
        valid = (col >= row * SHORT) & (col < row * SHORT + lengths)
        new_k = new_k_ref[pl.ds(r0, chunk), :]
        new_v = new_v_ref[pl.ds(r0, chunk), :]
        for h in range(groups):
            qh = q_ref[pl.ds(r0, chunk), h * head_dim:(h + 1) * head_dim]
            o_ref[pl.ds(r0, chunk), h * head_dim:(h + 1) * head_dim] = attend(
                qh, keys, values, valid, new_k, new_v
            )

    @pl.loop(0, table_width)
    def _(j):
        long_copy(j, 0, long_k).wait()
        long_copy(j, 1, long_v).wait()

    long_col = lax.broadcasted_iota(jnp.int32, (chunk, table_width * page_size), 1)
    long_valid = long_col < long_len
    own_row = lax.broadcasted_iota(jnp.int32, (chunk, 1), 0)

    @pl.when(long_len >= SHORT)
    def _():
        r0 = pl.multiple_of((long_row // chunk) * chunk, chunk)
        new_k = new_k_ref[pl.ds(r0, chunk), :]
        new_v = new_v_ref[pl.ds(r0, chunk), :]
        chosen = (own_row + r0) == long_row
        for h in range(groups):
            qh = q_ref[pl.ds(r0, chunk), h * head_dim:(h + 1) * head_dim]
            result = attend(qh, long_k[...], long_v[...], long_valid, new_k, new_v)
            current = o_ref[pl.ds(r0, chunk), h * head_dim:(h + 1) * head_dim]
            o_ref[pl.ds(r0, chunk), h * head_dim:(h + 1) * head_dim] = jnp.where(
                chosen, result, current
            )


def local_attention(query, new_kv, key_value_pages, page_table, cache_len):
    row_count = query.shape[0]
    pool_pages = key_value_pages.shape[1]
    page_size = key_value_pages.shape[2]
    head_dim = HEAD_SIZE
    table_width = page_table.shape[1]
    base = jnp.full((1,), lax.axis_index("dp") * pool_pages, jnp.int32)
    smem = pl.BlockSpec(memory_space=pltpu.SMEM)
    vmem = pl.BlockSpec(memory_space=pltpu.VMEM)
    rows = row_count * SHORT + table_width * page_size
    return pl.pallas_call(
        attention_kernel,
        out_shape=jax.ShapeDtypeStruct(query.shape, jnp.bfloat16),
        in_specs=[smem, smem, smem, vmem, vmem, vmem, pl.BlockSpec(memory_space=pl.ANY)],
        out_specs=vmem,
        scratch_shapes=[
            pltpu.VMEM((row_count * SHORT, head_dim), key_value_pages.dtype),
            pltpu.VMEM((row_count * SHORT, head_dim), key_value_pages.dtype),
            pltpu.VMEM((table_width * page_size, head_dim), key_value_pages.dtype),
            pltpu.VMEM((table_width * page_size, head_dim), key_value_pages.dtype),
            pltpu.SemaphoreType.DMA((4, row_count)),
        ],
        cost_estimate=pl.CostEstimate(
            flops=4 * 16 * query.shape[1] * rows,
            transcendentals=16 * query.shape[1] // head_dim * rows,
            bytes_accessed=2 * 2 * head_dim * rows,
        ),
    )(page_table, cache_len, base, query, new_kv[0], new_kv[1], key_value_pages)


def ring_shift(x, shift, axis_name, size):
    return lax.ppermute(x, axis_name, [(i, (i + shift) % size) for i in range(size)])


def ring_reduce_scatter(blocks, axis_name, size, index):
    total = lax.dynamic_index_in_dim(blocks, index, 0, keepdims=False).astype(jnp.float32)
    for shift in range(1, size):
        outgoing = lax.dynamic_index_in_dim(blocks, (index + shift) % size, 0, keepdims=False)
        total = total + ring_shift(outgoing, shift, axis_name, size).astype(jnp.float32)
    return total


def ring_all_gather(x, axis_name, size):
    return [x] + [ring_shift(x, shift, axis_name, size) for shift in range(1, size)]


def dense_all_to_all(x, axis_name):
    lanes = 128
    flat = x.reshape(x.shape[0], x.shape[1] * x.shape[2] // lanes, lanes)
    moved = lax.all_to_all(flat, axis_name, split_axis=0, concat_axis=0, tiled=True)
    return moved.reshape(x.shape)


def ring_all_gather_two_step(x, axis_name, size, index):
    half = x.shape[0] // 2
    from_left = ring_shift(x, 1, axis_name, size)
    from_right = ring_shift(x, size - 1, axis_name, size)
    far = jnp.concatenate(
        [
            ring_shift(from_left[:half], 1, axis_name, size),
            ring_shift(from_right[half:], size - 1, axis_name, size),
        ],
        axis=0,
    )
    return [x, from_left, far, from_right]


def ring_reduce_scatter_two_step(blocks, axis_name, size, index):
    def block(shift):
        return lax.dynamic_index_in_dim(blocks, (index + shift) % size, 0, keepdims=False)

    far = block(2)
    half = far.shape[0] // 2
    to_left_far = ring_shift(far[:half], 1, axis_name, size)
    to_right_far = ring_shift(far[half:], size - 1, axis_name, size)
    from_left = ring_shift(block(1), 1, axis_name, size).astype(jnp.float32)
    from_right = ring_shift(block(size - 1), size - 1, axis_name, size).astype(jnp.float32)
    far_first = ring_shift(to_left_far, 1, axis_name, size).astype(jnp.float32)
    far_second = ring_shift(to_right_far, size - 1, axis_name, size).astype(jnp.float32)
    total = block(0).astype(jnp.float32) + from_left + from_right
    return total + jnp.concatenate([far_first, far_second], axis=0)


def per_device(
    query,
    new_kv,
    key_value_pages,
    page_table,
    cache_len,
    residual,
    out_weight,
    norm_gain,
    expert_ids,
    combine_weights,
    expert_w1,
    expert_w2,
):
    tensor_size = lax.axis_size("tensor")
    tensor_index = lax.axis_index("tensor")
    attn = local_attention(query, new_kv, key_value_pages, page_table, cache_len)
    row_count, model_width = residual.shape
    share_width = model_width // tensor_size
    share_start = tensor_index * share_width

    split_weight = out_weight.reshape(out_weight.shape[0], tensor_size, share_width)
    partial_proj = jnp.einsum(
        "rk,kuc->urc", attn, split_weight, preferred_element_type=jnp.float32
    )
    summed = ring_reduce_scatter(partial_proj, "tensor", tensor_size, tensor_index)
    residual_share = lax.dynamic_slice_in_dim(residual, share_start, share_width, 1)
    state = residual_share.astype(jnp.float32) + summed
    square_sum = sum(ring_all_gather(jnp.sum(state * state, axis=1, keepdims=True), "tensor", tensor_size))
    mean_square = square_sum / model_width
    gain_share = lax.dynamic_slice_in_dim(norm_gain, share_start, share_width, 0)
    normed = (state * lax.rsqrt(mean_square + 1e-05) * gain_share).astype(jnp.bfloat16)

    local_experts = expert_w1.shape[0]
    top_count = expert_ids.shape[1]
    experts = local_experts * lax.axis_size("dp")
    capacity = min(
        row_count, max(3, (3 * row_count * top_count + 2 * experts - 1) // (2 * experts))
    )
    flat_ids = expert_ids.reshape(-1)
    choice_rows = flat_ids.shape[0]
    row_iota = jnp.arange(choice_rows, dtype=jnp.int32)
    choice_hot = (flat_ids[:, None] == jnp.arange(experts, dtype=jnp.int32)[None, :]).astype(
        jnp.bfloat16
    )
    strictly_lower = (row_iota[:, None] > row_iota[None, :]).astype(jnp.bfloat16)
    earlier = jnp.dot(strictly_lower, choice_hot, preferred_element_type=jnp.float32)
    slot_rank = jnp.sum(earlier * choice_hot.astype(jnp.float32), axis=1).astype(jnp.int32)
    slot_index = (flat_ids * capacity + slot_rank).reshape(row_count, top_count)
    slot_ids = jnp.arange(experts * capacity, dtype=jnp.int32)
    hit = slot_index[:, :, None] == slot_ids[None, None, :]
    placing = jnp.any(hit, axis=1).astype(jnp.bfloat16)
    mixing = jnp.sum(jnp.where(hit, combine_weights[:, :, None], 0.0), axis=1)

    outgoing = jnp.dot(placing.T, normed, preferred_element_type=jnp.float32)
    outgoing = outgoing.astype(jnp.bfloat16).reshape(experts, capacity, share_width)
    mixing = mixing.reshape(row_count, experts, capacity)
    split_w1 = expert_w1.reshape(tensor_size, share_width, 2, expert_w1.shape[-1])
    split_w2 = expert_w2[0].reshape(expert_w2.shape[1], tensor_size, share_width)

    expert_mix = None
    streams = 1
    bounds = [capacity * i // streams for i in range(streams + 1)]
    for lo, hi in zip(bounds[:-1], bounds[1:]):
        slots = hi - lo
        arrived = dense_all_to_all(outgoing[:, lo:hi], "dp")
        pieces = ring_all_gather_two_step(arrived, "tensor", tensor_size, tensor_index)
        gate_up = None
        for shift, piece in enumerate(pieces):
            weight = lax.dynamic_index_in_dim(
                split_w1, (tensor_index - shift) % tensor_size, 0, keepdims=False
            )
            term = jnp.einsum("snc,cgf->sngf", piece, weight, preferred_element_type=jnp.float32)
            gate_up = term if gate_up is None else gate_up + term
        activated = (jax.nn.silu(gate_up[:, :, 0, :]) * gate_up[:, :, 1, :]).astype(
            jnp.bfloat16
        )
        partial_out = jnp.einsum(
            "snf,fuc->usnc", activated, split_w2, preferred_element_type=jnp.float32
        ).astype(jnp.bfloat16)
        for first, last in ((0, capacity // 3), (capacity // 3, capacity)):
            expert_sum = ring_reduce_scatter_two_step(
                partial_out[:, :, first:last], "tensor", tensor_size, tensor_index
            )
            expert_sum = expert_sum.astype(jnp.bfloat16)
            returned_rows = dense_all_to_all(expert_sum, "dp")
            part_mix = jnp.dot(
                mixing[:, :, lo + first:lo + last].reshape(row_count, experts * (last - first)),
                returned_rows.reshape(experts * (last - first), share_width).astype(jnp.float32),
                precision=lax.Precision.HIGHEST,
            )
            expert_mix = part_mix if expert_mix is None else expert_mix + part_mix
    return (state + expert_mix).astype(jnp.bfloat16)


def solution(mesh):
    return jax.shard_map(
        per_device,
        mesh=mesh,
        in_specs=(
            P("dp", "tensor"),
            P(None, "dp", "tensor"),
            P(None, "dp", None, "tensor"),
            P("dp", None),
            P("dp"),
            P("dp", None),
            P("tensor", None),
            P(),
            P("dp", None),
            P("dp", None),
            P("dp", None, None, "tensor"),
            P("dp", "tensor", None),
        ),
        out_specs=P("dp", "tensor"),
        check_vma=False,
    )
```

```python
import math

import jax
import jax.numpy as jnp
from jax import lax
from jax.experimental import pallas as pl
from jax.experimental.pallas import tpu as pltpu
from jax.sharding import PartitionSpec as P

HEAD_SIZE = 128
SHORT = 64


def attention_kernel(
    table_ref, len_ref, base_ref, q_ref, new_kv_ref, kv_hbm, o_ref,
    short_k, short_v, long_k, long_v, sem,
):
    rows = q_ref.shape[0]
    head_dim = new_kv_ref.shape[2]
    groups = q_ref.shape[1] // head_dim
    table_width = table_ref.shape[1]
    pool_pages = kv_hbm.shape[1]
    page_size = kv_hbm.shape[2]
    chunk = 16
    scale_of_score = 1.0 / math.sqrt(head_dim)
    base = base_ref[0]

    def local_page(r, j):
        return jnp.minimum(jnp.maximum(table_ref[r, j] - base, 0), pool_pages - 1)

    def longest(r, carry):
        best_row, best_len = carry
        length = len_ref[r]
        better = length > best_len
        return jnp.where(better, r, best_row), jnp.where(better, length, best_len)

    long_row, long_len = lax.fori_loop(0, rows, longest, (jnp.int32(0), len_ref[0]))

    def short_copy(r, which, buf):
        return pltpu.make_async_copy(
            kv_hbm.at[which, local_page(r, 0), pl.ds(0, SHORT), :],
            buf.at[pl.ds(r * SHORT, SHORT), :],
            sem.at[which, r],
        )

    def long_copy(j, which, buf):
        return pltpu.make_async_copy(
            kv_hbm.at[which, local_page(long_row, j)],
            buf.at[pl.ds(j * page_size, page_size), :],
            sem.at[2 + which, j],
        )

    @pl.loop(0, rows)
    def _(r):
        short_copy(r, 0, short_k).start()
        short_copy(r, 1, short_v).start()

    @pl.loop(0, table_width)
    def _(j):
        long_copy(j, 0, long_k).start()
        long_copy(j, 1, long_v).start()

    def attend(qh, keys, values, valid, new_k, new_v):
        scores = lax.dot_general(
            qh, keys, (((1,), (1,)), ((), ())), preferred_element_type=jnp.float32
        ) * scale_of_score
        fresh = jnp.sum(
            qh.astype(jnp.float32) * new_k.astype(jnp.float32), axis=1, keepdims=True
        ) * scale_of_score
        scores = jnp.where(valid, scores, -1e30)
        row_max = jnp.maximum(jnp.max(scores, axis=1, keepdims=True), fresh)
        weights = jnp.where(valid, jnp.exp(scores - row_max), 0.0)
        weight_new = jnp.exp(fresh - row_max)
        denominator = jnp.sum(weights, axis=1, keepdims=True) + weight_new
        numerator = jnp.dot(
            weights.astype(jnp.bfloat16), values, preferred_element_type=jnp.float32
        )
        numerator = numerator + (
            weight_new.astype(jnp.bfloat16).astype(jnp.float32) * new_v.astype(jnp.float32)
        )
        return (numerator / denominator).astype(o_ref.dtype)

    width = chunk * SHORT
    row = lax.broadcasted_iota(jnp.int32, (chunk, width), 0)
    col = lax.broadcasted_iota(jnp.int32, (chunk, width), 1)

    @pl.loop(0, rows // chunk)
    def _(c):
        r0 = pl.multiple_of(c * chunk, chunk)
        k0 = pl.multiple_of(c * width, width)

        @pl.loop(0, chunk)
        def _(i):
            short_copy(r0 + i, 0, short_k).wait()
            short_copy(r0 + i, 1, short_v).wait()

        keys = short_k[pl.ds(k0, width), :]
        values = short_v[pl.ds(k0, width), :]
        lengths = jnp.zeros((chunk, 1), jnp.int32)
        for i in range(chunk):
            lengths = jnp.where(row[:, :1] == i, jnp.minimum(len_ref[r0 + i], SHORT), lengths)
        valid = (col >= row * SHORT) & (col < row * SHORT + lengths)
        new_k = new_kv_ref[0, pl.ds(r0, chunk), :]
        new_v = new_kv_ref[1, pl.ds(r0, chunk), :]
        for h in range(groups):
            qh = q_ref[pl.ds(r0, chunk), h * head_dim:(h + 1) * head_dim]
            o_ref[pl.ds(r0, chunk), h * head_dim:(h + 1) * head_dim] = attend(
                qh, keys, values, valid, new_k, new_v
            )

    @pl.loop(0, table_width)
    def _(j):
        long_copy(j, 0, long_k).wait()
        long_copy(j, 1, long_v).wait()

    long_col = lax.broadcasted_iota(jnp.int32, (chunk, table_width * page_size), 1)
    long_valid = long_col < long_len
    own_row = lax.broadcasted_iota(jnp.int32, (chunk, 1), 0)

    @pl.when(long_len >= SHORT)
    def _():
        r0 = pl.multiple_of((long_row // chunk) * chunk, chunk)
        new_k = new_kv_ref[0, pl.ds(r0, chunk), :]
        new_v = new_kv_ref[1, pl.ds(r0, chunk), :]
        chosen = (own_row + r0) == long_row
        for h in range(groups):
            qh = q_ref[pl.ds(r0, chunk), h * head_dim:(h + 1) * head_dim]
            result = attend(qh, long_k[...], long_v[...], long_valid, new_k, new_v)
            current = o_ref[pl.ds(r0, chunk), h * head_dim:(h + 1) * head_dim]
            o_ref[pl.ds(r0, chunk), h * head_dim:(h + 1) * head_dim] = jnp.where(
                chosen, result, current
            )


def local_attention(query, new_kv, key_value_pages, page_table, cache_len):
    row_count = query.shape[0]
    pool_pages = key_value_pages.shape[1]
    page_size = key_value_pages.shape[2]
    head_dim = HEAD_SIZE
    table_width = page_table.shape[1]
    base = jnp.full((1,), lax.axis_index("dp") * pool_pages, jnp.int32)
    smem = pl.BlockSpec(memory_space=pltpu.SMEM)
    vmem = pl.BlockSpec(memory_space=pltpu.VMEM)
    rows = row_count * SHORT + table_width * page_size
    return pl.pallas_call(
        attention_kernel,
        out_shape=jax.ShapeDtypeStruct(query.shape, jnp.bfloat16),
        in_specs=[smem, smem, smem, vmem, vmem, pl.BlockSpec(memory_space=pl.ANY)],
        out_specs=vmem,
        scratch_shapes=[
            pltpu.VMEM((row_count * SHORT, head_dim), key_value_pages.dtype),
            pltpu.VMEM((row_count * SHORT, head_dim), key_value_pages.dtype),
            pltpu.VMEM((table_width * page_size, head_dim), key_value_pages.dtype),
            pltpu.VMEM((table_width * page_size, head_dim), key_value_pages.dtype),
            pltpu.SemaphoreType.DMA((4, row_count)),
        ],
        cost_estimate=pl.CostEstimate(
            flops=4 * 16 * query.shape[1] * rows,
            transcendentals=16 * query.shape[1] // head_dim * rows,
            bytes_accessed=2 * 2 * head_dim * rows,
        ),
    )(page_table, cache_len, base, query, new_kv, key_value_pages)


def ring_shift(x, shift, axis_name, size):
    return lax.ppermute(x, axis_name, [(i, (i + shift) % size) for i in range(size)])


def ring_reduce_scatter(blocks, axis_name, size, index):
    total = lax.dynamic_index_in_dim(blocks, index, 0, keepdims=False).astype(jnp.float32)
    for shift in range(1, size):
        outgoing = lax.dynamic_index_in_dim(blocks, (index + shift) % size, 0, keepdims=False)
        total = total + ring_shift(outgoing, shift, axis_name, size).astype(jnp.float32)
    return total


def ring_all_gather(x, axis_name, size):
    return [x] + [ring_shift(x, shift, axis_name, size) for shift in range(1, size)]


def dense_all_to_all(x, axis_name):
    lanes = 128
    flat = x.reshape(x.shape[0], x.shape[1] * x.shape[2] // lanes, lanes)
    moved = lax.all_to_all(flat, axis_name, split_axis=0, concat_axis=0, tiled=True)
    return moved.reshape(x.shape)


def ring_all_gather_two_step(x, axis_name, size, index):
    half = x.shape[0] // 2
    from_left = ring_shift(x, 1, axis_name, size)
    from_right = ring_shift(x, size - 1, axis_name, size)
    far = jnp.concatenate(
        [
            ring_shift(from_left[:half], 1, axis_name, size),
            ring_shift(from_right[half:], size - 1, axis_name, size),
        ],
        axis=0,
    )
    return [x, from_left, far, from_right]


def ring_reduce_scatter_two_step(blocks, axis_name, size, index):
    def block(shift):
        return lax.dynamic_index_in_dim(blocks, (index + shift) % size, 0, keepdims=False)

    far = block(2)
    half = far.shape[0] // 2
    to_left_far = ring_shift(far[:half], 1, axis_name, size)
    to_right_far = ring_shift(far[half:], size - 1, axis_name, size)
    from_left = ring_shift(block(1), 1, axis_name, size).astype(jnp.float32)
    from_right = ring_shift(block(size - 1), size - 1, axis_name, size).astype(jnp.float32)
    far_first = ring_shift(to_left_far, 1, axis_name, size).astype(jnp.float32)
    far_second = ring_shift(to_right_far, size - 1, axis_name, size).astype(jnp.float32)
    total = block(0).astype(jnp.float32) + from_left + from_right
    return total + jnp.concatenate([far_first, far_second], axis=0)


def per_device(
    query,
    new_kv,
    key_value_pages,
    page_table,
    cache_len,
    residual,
    out_weight,
    norm_gain,
    expert_ids,
    combine_weights,
    expert_w1,
    expert_w2,
):
    tensor_size = lax.axis_size("tensor")
    tensor_index = lax.axis_index("tensor")
    attn = local_attention(query, new_kv, key_value_pages, page_table, cache_len)
    row_count, model_width = residual.shape
    share_width = model_width // tensor_size
    share_start = tensor_index * share_width

    split_weight = out_weight.reshape(out_weight.shape[0], tensor_size, share_width)
    partial_proj = jnp.einsum(
        "rk,kuc->urc", attn, split_weight, preferred_element_type=jnp.float32
    )
    summed = ring_reduce_scatter(partial_proj, "tensor", tensor_size, tensor_index)
    residual_share = lax.dynamic_slice_in_dim(residual, share_start, share_width, 1)
    state = residual_share.astype(jnp.float32) + summed
    square_sum = sum(ring_all_gather(jnp.sum(state * state, axis=1, keepdims=True), "tensor", tensor_size))
    mean_square = square_sum / model_width
    gain_share = lax.dynamic_slice_in_dim(norm_gain, share_start, share_width, 0)
    normed = (state * lax.rsqrt(mean_square + 1e-05) * gain_share).astype(jnp.bfloat16)

    local_experts = expert_w1.shape[0]
    top_count = expert_ids.shape[1]
    experts = local_experts * lax.axis_size("dp")
    capacity = min(
        row_count, max(3, (3 * row_count * top_count + 2 * experts - 1) // (2 * experts))
    )
    flat_ids = expert_ids.reshape(-1)
    choice_rows = flat_ids.shape[0]
    row_iota = jnp.arange(choice_rows, dtype=jnp.int32)
    choice_hot = (flat_ids[:, None] == jnp.arange(experts, dtype=jnp.int32)[None, :]).astype(
        jnp.bfloat16
    )
    strictly_lower = (row_iota[:, None] > row_iota[None, :]).astype(jnp.bfloat16)
    earlier = jnp.dot(strictly_lower, choice_hot, preferred_element_type=jnp.float32)
    slot_rank = jnp.sum(earlier * choice_hot.astype(jnp.float32), axis=1).astype(jnp.int32)
    slot_index = (flat_ids * capacity + slot_rank).reshape(row_count, top_count)
    slot_ids = jnp.arange(experts * capacity, dtype=jnp.int32)
    hit = slot_index[:, :, None] == slot_ids[None, None, :]
    placing = jnp.any(hit, axis=1).astype(jnp.bfloat16)
    mixing = jnp.sum(jnp.where(hit, combine_weights[:, :, None], 0.0), axis=1)

    outgoing = jnp.dot(placing.T, normed, preferred_element_type=jnp.float32)
    outgoing = outgoing.astype(jnp.bfloat16).reshape(experts, capacity, share_width)
    mixing = mixing.reshape(row_count, experts, capacity)
    split_w1 = expert_w1.reshape(tensor_size, share_width, 2, expert_w1.shape[-1])
    split_w2 = expert_w2[0].reshape(expert_w2.shape[1], tensor_size, share_width)

    expert_mix = None
    streams = 1
    bounds = [capacity * i // streams for i in range(streams + 1)]
    for lo, hi in zip(bounds[:-1], bounds[1:]):
        slots = hi - lo
        arrived = dense_all_to_all(outgoing[:, lo:hi], "dp")
        pieces = ring_all_gather_two_step(arrived, "tensor", tensor_size, tensor_index)
        gate_up = None
        for shift, piece in enumerate(pieces):
            weight = lax.dynamic_index_in_dim(
                split_w1, (tensor_index - shift) % tensor_size, 0, keepdims=False
            )
            term = jnp.einsum("snc,cgf->sngf", piece, weight, preferred_element_type=jnp.float32)
            gate_up = term if gate_up is None else gate_up + term
        activated = (jax.nn.silu(gate_up[:, :, 0, :]) * gate_up[:, :, 1, :]).astype(
            jnp.bfloat16
        )
        partial_out = jnp.einsum(
            "snf,fuc->usnc", activated, split_w2, preferred_element_type=jnp.float32
        ).astype(jnp.bfloat16)
        expert_sum = ring_reduce_scatter_two_step(
            partial_out, "tensor", tensor_size, tensor_index
        )
        expert_sum = expert_sum.astype(jnp.bfloat16)
        returned_rows = dense_all_to_all(expert_sum, "dp")
        part_mix = jnp.dot(
            mixing[:, :, lo:hi].reshape(row_count, experts * slots),
            returned_rows.reshape(experts * slots, share_width).astype(jnp.float32),
            precision=lax.Precision.HIGHEST,
        )
        expert_mix = part_mix if expert_mix is None else expert_mix + part_mix
    return (state + expert_mix).astype(jnp.bfloat16)


def solution(mesh):
    return jax.shard_map(
        per_device,
        mesh=mesh,
        in_specs=(
            P("dp", "tensor"),
            P(None, "dp", "tensor"),
            P(None, "dp", None, "tensor"),
            P("dp", None),
            P("dp"),
            P("dp", None),
            P("tensor", None),
            P(),
            P("dp", None),
            P("dp", None),
            P("dp", None, None, "tensor"),
            P("dp", "tensor", None),
        ),
        out_specs=P("dp", "tensor"),
        check_vma=False,
    )
```

```python
import math

import jax
import jax.numpy as jnp
from jax import lax
from jax.experimental import pallas as pl
from jax.experimental.pallas import tpu as pltpu
from jax.sharding import PartitionSpec as P

HEAD_SIZE = 128
SHORT = 64


def attention_kernel(
    table_ref, len_ref, base_ref, q_ref, new_kv_ref, kv_hbm, o_ref,
    short_k, short_v, long_k, long_v, sem,
):
    rows = q_ref.shape[0]
    head_dim = new_kv_ref.shape[2]
    groups = q_ref.shape[1] // head_dim
    table_width = table_ref.shape[1]
    pool_pages = kv_hbm.shape[1]
    page_size = kv_hbm.shape[2]
    chunk = 16
    scale_of_score = 1.0 / math.sqrt(head_dim)
    base = base_ref[0]

    def local_page(r, j):
        return jnp.minimum(jnp.maximum(table_ref[r, j] - base, 0), pool_pages - 1)

    def longest(r, carry):
        best_row, best_len = carry
        length = len_ref[r]
        better = length > best_len
        return jnp.where(better, r, best_row), jnp.where(better, length, best_len)

    long_row, long_len = lax.fori_loop(0, rows, longest, (jnp.int32(0), len_ref[0]))

    def short_copy(r, which, buf):
        return pltpu.make_async_copy(
            kv_hbm.at[which, local_page(r, 0), pl.ds(0, SHORT), :],
            buf.at[pl.ds(r * SHORT, SHORT), :],
            sem.at[which, r],
        )

    def long_copy(j, which, buf):
        return pltpu.make_async_copy(
            kv_hbm.at[which, local_page(long_row, j)],
            buf.at[pl.ds(j * page_size, page_size), :],
            sem.at[2 + which, j],
        )

    @pl.loop(0, rows)
    def _(r):
        short_copy(r, 0, short_k).start()
        short_copy(r, 1, short_v).start()

    @pl.loop(0, table_width)
    def _(j):
        long_copy(j, 0, long_k).start()
        long_copy(j, 1, long_v).start()

    def attend(qh, keys, values, valid, new_k, new_v):
        scores = lax.dot_general(
            qh, keys, (((1,), (1,)), ((), ())), preferred_element_type=jnp.float32
        ) * scale_of_score
        fresh = jnp.sum(
            qh.astype(jnp.float32) * new_k.astype(jnp.float32), axis=1, keepdims=True
        ) * scale_of_score
        scores = jnp.where(valid, scores, -1e30)
        row_max = jnp.maximum(jnp.max(scores, axis=1, keepdims=True), fresh)
        weights = jnp.where(valid, jnp.exp(scores - row_max), 0.0)
        weight_new = jnp.exp(fresh - row_max)
        denominator = jnp.sum(weights, axis=1, keepdims=True) + weight_new
        numerator = jnp.dot(
            weights.astype(jnp.bfloat16), values, preferred_element_type=jnp.float32
        )
        numerator = numerator + (
            weight_new.astype(jnp.bfloat16).astype(jnp.float32) * new_v.astype(jnp.float32)
        )
        return (numerator / denominator).astype(o_ref.dtype)

    width = chunk * SHORT
    row = lax.broadcasted_iota(jnp.int32, (chunk, width), 0)
    col = lax.broadcasted_iota(jnp.int32, (chunk, width), 1)

    @pl.loop(0, rows // chunk)
    def _(c):
        r0 = pl.multiple_of(c * chunk, chunk)
        k0 = pl.multiple_of(c * width, width)

        @pl.loop(0, chunk)
        def _(i):
            short_copy(r0 + i, 0, short_k).wait()
            short_copy(r0 + i, 1, short_v).wait()

        keys = short_k[pl.ds(k0, width), :]
        values = short_v[pl.ds(k0, width), :]
        lengths = jnp.zeros((chunk, 1), jnp.int32)
        for i in range(chunk):
            lengths = jnp.where(row[:, :1] == i, jnp.minimum(len_ref[r0 + i], SHORT), lengths)
        valid = (col >= row * SHORT) & (col < row * SHORT + lengths)
        new_k = new_kv_ref[0, pl.ds(r0, chunk), :]
        new_v = new_kv_ref[1, pl.ds(r0, chunk), :]
        for h in range(groups):
            qh = q_ref[pl.ds(r0, chunk), h * head_dim:(h + 1) * head_dim]
            o_ref[pl.ds(r0, chunk), h * head_dim:(h + 1) * head_dim] = attend(
                qh, keys, values, valid, new_k, new_v
            )

    @pl.loop(0, table_width)
    def _(j):
        long_copy(j, 0, long_k).wait()
        long_copy(j, 1, long_v).wait()

    long_col = lax.broadcasted_iota(jnp.int32, (chunk, table_width * page_size), 1)
    long_valid = long_col < long_len
    own_row = lax.broadcasted_iota(jnp.int32, (chunk, 1), 0)

    @pl.when(long_len >= SHORT)
    def _():
        r0 = pl.multiple_of((long_row // chunk) * chunk, chunk)
        new_k = new_kv_ref[0, pl.ds(r0, chunk), :]
        new_v = new_kv_ref[1, pl.ds(r0, chunk), :]
        chosen = (own_row + r0) == long_row
        for h in range(groups):
            qh = q_ref[pl.ds(r0, chunk), h * head_dim:(h + 1) * head_dim]
            result = attend(qh, long_k[...], long_v[...], long_valid, new_k, new_v)
            current = o_ref[pl.ds(r0, chunk), h * head_dim:(h + 1) * head_dim]
            o_ref[pl.ds(r0, chunk), h * head_dim:(h + 1) * head_dim] = jnp.where(
                chosen, result, current
            )


def local_attention(query, new_kv, key_value_pages, page_table, cache_len):
    row_count = query.shape[0]
    pool_pages = key_value_pages.shape[1]
    page_size = key_value_pages.shape[2]
    head_dim = HEAD_SIZE
    table_width = page_table.shape[1]
    base = jnp.full((1,), lax.axis_index("dp") * pool_pages, jnp.int32)
    smem = pl.BlockSpec(memory_space=pltpu.SMEM)
    vmem = pl.BlockSpec(memory_space=pltpu.VMEM)
    rows = row_count * SHORT + table_width * page_size
    return pl.pallas_call(
        attention_kernel,
        out_shape=jax.ShapeDtypeStruct(query.shape, jnp.bfloat16),
        in_specs=[smem, smem, smem, vmem, vmem, pl.BlockSpec(memory_space=pl.ANY)],
        out_specs=vmem,
        scratch_shapes=[
            pltpu.VMEM((row_count * SHORT, head_dim), key_value_pages.dtype),
            pltpu.VMEM((row_count * SHORT, head_dim), key_value_pages.dtype),
            pltpu.VMEM((table_width * page_size, head_dim), key_value_pages.dtype),
            pltpu.VMEM((table_width * page_size, head_dim), key_value_pages.dtype),
            pltpu.SemaphoreType.DMA((4, row_count)),
        ],
        cost_estimate=pl.CostEstimate(
            flops=4 * 16 * query.shape[1] * rows,
            transcendentals=16 * query.shape[1] // head_dim * rows,
            bytes_accessed=2 * 2 * head_dim * rows,
        ),
    )(page_table, cache_len, base, query, new_kv, key_value_pages)


def ring_shift(x, shift, axis_name, size):
    return lax.ppermute(x, axis_name, [(i, (i + shift) % size) for i in range(size)])


def ring_reduce_scatter(blocks, axis_name, size, index):
    total = lax.dynamic_index_in_dim(blocks, index, 0, keepdims=False).astype(jnp.float32)
    for shift in range(1, size):
        outgoing = lax.dynamic_index_in_dim(blocks, (index + shift) % size, 0, keepdims=False)
        total = total + ring_shift(outgoing, shift, axis_name, size).astype(jnp.float32)
    return total


def ring_all_gather(x, axis_name, size):
    return [x] + [ring_shift(x, shift, axis_name, size) for shift in range(1, size)]


def dense_all_to_all(x, axis_name):
    lanes = 128
    flat = x.reshape(x.shape[0], x.shape[1] * x.shape[2] // lanes, lanes)
    moved = lax.all_to_all(flat, axis_name, split_axis=0, concat_axis=0, tiled=True)
    return moved.reshape(x.shape)


def ring_all_gather_two_step(x, axis_name, size, index):
    half = x.shape[0] // 2
    from_left = ring_shift(x, 1, axis_name, size)
    from_right = ring_shift(x, size - 1, axis_name, size)
    far = jnp.concatenate(
        [
            ring_shift(from_left[:half], 1, axis_name, size),
            ring_shift(from_right[half:], size - 1, axis_name, size),
        ],
        axis=0,
    )
    return [x, from_left, far, from_right]


def ring_reduce_scatter_two_step(blocks, axis_name, size, index):
    def block(shift):
        return lax.dynamic_index_in_dim(blocks, (index + shift) % size, 0, keepdims=False)

    far = block(2)
    half = far.shape[0] // 2
    to_left_far = ring_shift(far[:half], 1, axis_name, size)
    to_right_far = ring_shift(far[half:], size - 1, axis_name, size)
    from_left = ring_shift(block(1), 1, axis_name, size).astype(jnp.float32)
    from_right = ring_shift(block(size - 1), size - 1, axis_name, size).astype(jnp.float32)
    far_first = ring_shift(to_left_far, 1, axis_name, size).astype(jnp.float32)
    far_second = ring_shift(to_right_far, size - 1, axis_name, size).astype(jnp.float32)
    total = block(0).astype(jnp.float32) + from_left + from_right
    return total + jnp.concatenate([far_first, far_second], axis=0)


def per_device(
    query,
    new_kv,
    key_value_pages,
    page_table,
    cache_len,
    residual,
    out_weight,
    norm_gain,
    expert_ids,
    combine_weights,
    expert_w1,
    expert_w2,
):
    tensor_size = lax.axis_size("tensor")
    tensor_index = lax.axis_index("tensor")
    attn = local_attention(query, new_kv, key_value_pages, page_table, cache_len)
    row_count, model_width = residual.shape
    share_width = model_width // tensor_size
    share_start = tensor_index * share_width

    split_weight = out_weight.reshape(out_weight.shape[0], tensor_size, share_width)
    partial_proj = jnp.einsum(
        "rk,kuc->urc", attn, split_weight, preferred_element_type=jnp.float32
    )
    summed = ring_reduce_scatter(partial_proj, "tensor", tensor_size, tensor_index)
    residual_share = lax.dynamic_slice_in_dim(residual, share_start, share_width, 1)
    state = residual_share.astype(jnp.float32) + summed
    own_square = jnp.sum(state * state, axis=1, keepdims=True)
    square_from_left = ring_shift(own_square, 1, "tensor", tensor_size)
    square_from_right = ring_shift(own_square, tensor_size - 1, "tensor", tensor_size)
    square_far = ring_shift(square_from_left, 1, "tensor", tensor_size)
    square_sum = own_square + square_from_left + square_far + square_from_right
    mean_square = square_sum / model_width
    gain_share = lax.dynamic_slice_in_dim(norm_gain, share_start, share_width, 0)
    normed = (state * lax.rsqrt(mean_square + 1e-05) * gain_share).astype(jnp.bfloat16)

    local_experts = expert_w1.shape[0]
    top_count = expert_ids.shape[1]
    experts = local_experts * lax.axis_size("dp")
    capacity = min(
        row_count, max(3, (3 * row_count * top_count + 2 * experts - 1) // (2 * experts))
    )
    flat_ids = expert_ids.reshape(-1)
    choice_rows = flat_ids.shape[0]
    row_iota = jnp.arange(choice_rows, dtype=jnp.int32)
    choice_hot = (flat_ids[:, None] == jnp.arange(experts, dtype=jnp.int32)[None, :]).astype(
        jnp.bfloat16
    )
    strictly_lower = (row_iota[:, None] > row_iota[None, :]).astype(jnp.bfloat16)
    earlier = jnp.dot(strictly_lower, choice_hot, preferred_element_type=jnp.float32)
    slot_rank = jnp.sum(earlier * choice_hot.astype(jnp.float32), axis=1).astype(jnp.int32)
    slot_index = (flat_ids * capacity + slot_rank).reshape(row_count, top_count)
    slot_ids = jnp.arange(experts * capacity, dtype=jnp.int32)
    hit = slot_index[:, :, None] == slot_ids[None, None, :]
    placing = jnp.any(hit, axis=1).astype(jnp.bfloat16)
    mixing = jnp.sum(jnp.where(hit, combine_weights[:, :, None], 0.0), axis=1)

    outgoing = jnp.dot(placing.T, normed, preferred_element_type=jnp.float32)
    outgoing = outgoing.astype(jnp.bfloat16).reshape(experts, capacity, share_width)
    mixing = mixing.reshape(row_count, experts, capacity)
    split_w1 = expert_w1.reshape(tensor_size, share_width, 2, expert_w1.shape[-1])
    split_w2 = expert_w2[0].reshape(expert_w2.shape[1], tensor_size, share_width)

    expert_mix = None
    streams = 1
    bounds = [capacity * i // streams for i in range(streams + 1)]
    for lo, hi in zip(bounds[:-1], bounds[1:]):
        slots = hi - lo
        arrived = dense_all_to_all(outgoing[:, lo:hi], "dp")
        pieces = ring_all_gather_two_step(arrived, "tensor", tensor_size, tensor_index)
        gate_up = None
        for shift, piece in enumerate(pieces):
            weight = lax.dynamic_index_in_dim(
                split_w1, (tensor_index - shift) % tensor_size, 0, keepdims=False
            )
            term = jnp.einsum("snc,cgf->sngf", piece, weight, preferred_element_type=jnp.float32)
            gate_up = term if gate_up is None else gate_up + term
        activated = (jax.nn.silu(gate_up[:, :, 0, :]) * gate_up[:, :, 1, :]).astype(
            jnp.bfloat16
        )
        partial_out = jnp.einsum(
            "snf,fuc->usnc", activated, split_w2, preferred_element_type=jnp.float32
        ).astype(jnp.bfloat16)
        expert_sum = ring_reduce_scatter_two_step(
            partial_out, "tensor", tensor_size, tensor_index
        )
        expert_sum = expert_sum.astype(jnp.bfloat16)
        returned_rows = dense_all_to_all(expert_sum, "dp")
        part_mix = jnp.dot(
            mixing[:, :, lo:hi].reshape(row_count, experts * slots),
            returned_rows.reshape(experts * slots, share_width).astype(jnp.float32),
            precision=lax.Precision.HIGHEST,
        )
        expert_mix = part_mix if expert_mix is None else expert_mix + part_mix
    return (state + expert_mix).astype(jnp.bfloat16)


def solution(mesh):
    return jax.shard_map(
        per_device,
        mesh=mesh,
        in_specs=(
            P("dp", "tensor"),
            P(None, "dp", "tensor"),
            P(None, "dp", None, "tensor"),
            P("dp", None),
            P("dp"),
            P("dp", None),
            P("tensor", None),
            P(),
            P("dp", None),
            P("dp", None),
            P("dp", None, None, "tensor"),
            P("dp", "tensor", None),
        ),
        out_specs=P("dp", "tensor"),
        check_vma=False,
    )
```

```python
import math

import jax
import jax.numpy as jnp
from jax import lax
from jax.experimental import pallas as pl
from jax.experimental.pallas import tpu as pltpu
from jax.sharding import PartitionSpec as P

HEAD_SIZE = 128
SHORT = 64


def attention_kernel(
    table_ref, len_ref, base_ref, q_ref, new_kv_ref, kv_hbm, o_ref,
    short_k, short_v, long_k, long_v, sem,
):
    rows = q_ref.shape[0]
    head_dim = new_kv_ref.shape[2]
    groups = q_ref.shape[1] // head_dim
    table_width = table_ref.shape[1]
    pool_pages = kv_hbm.shape[1]
    page_size = kv_hbm.shape[2]
    chunk = 16
    scale_of_score = 1.0 / math.sqrt(head_dim)
    base = base_ref[0]

    def local_page(r, j):
        return jnp.minimum(jnp.maximum(table_ref[r, j] - base, 0), pool_pages - 1)

    def longest(r, carry):
        best_row, best_len = carry
        length = len_ref[r]
        better = length > best_len
        return jnp.where(better, r, best_row), jnp.where(better, length, best_len)

    long_row, long_len = lax.fori_loop(0, rows, longest, (jnp.int32(0), len_ref[0]))

    def short_copy(r, which, buf):
        return pltpu.make_async_copy(
            kv_hbm.at[which, local_page(r, 0), pl.ds(0, SHORT), :],
            buf.at[pl.ds(r * SHORT, SHORT), :],
            sem.at[which, r],
        )

    def long_copy(j, which, buf):
        return pltpu.make_async_copy(
            kv_hbm.at[which, local_page(long_row, j)],
            buf.at[pl.ds(j * page_size, page_size), :],
            sem.at[2 + which, j],
        )

    @pl.loop(0, rows)
    def _(r):
        short_copy(r, 0, short_k).start()
        short_copy(r, 1, short_v).start()

    @pl.loop(0, table_width)
    def _(j):
        long_copy(j, 0, long_k).start()
        long_copy(j, 1, long_v).start()

    def attend(qh, keys, values, valid, new_k, new_v):
        scores = lax.dot_general(
            qh, keys, (((1,), (1,)), ((), ())), preferred_element_type=jnp.float32
        ) * scale_of_score
        fresh = jnp.sum(
            qh.astype(jnp.float32) * new_k.astype(jnp.float32), axis=1, keepdims=True
        ) * scale_of_score
        scores = jnp.where(valid, scores, -1e30)
        row_max = jnp.maximum(jnp.max(scores, axis=1, keepdims=True), fresh)
        weights = jnp.where(valid, jnp.exp(scores - row_max), 0.0)
        weight_new = jnp.exp(fresh - row_max)
        denominator = jnp.sum(weights, axis=1, keepdims=True) + weight_new
        numerator = jnp.dot(
            weights.astype(jnp.bfloat16), values, preferred_element_type=jnp.float32
        )
        numerator = numerator + (
            weight_new.astype(jnp.bfloat16).astype(jnp.float32) * new_v.astype(jnp.float32)
        )
        return (numerator / denominator).astype(o_ref.dtype)

    width = chunk * SHORT
    row = lax.broadcasted_iota(jnp.int32, (chunk, width), 0)
    col = lax.broadcasted_iota(jnp.int32, (chunk, width), 1)

    @pl.loop(0, rows // chunk)
    def _(c):
        r0 = pl.multiple_of(c * chunk, chunk)
        k0 = pl.multiple_of(c * width, width)

        @pl.loop(0, chunk)
        def _(i):
            short_copy(r0 + i, 0, short_k).wait()
            short_copy(r0 + i, 1, short_v).wait()

        keys = short_k[pl.ds(k0, width), :]
        values = short_v[pl.ds(k0, width), :]
        lengths = jnp.zeros((chunk, 1), jnp.int32)
        for i in range(chunk):
            lengths = jnp.where(row[:, :1] == i, jnp.minimum(len_ref[r0 + i], SHORT), lengths)
        valid = (col >= row * SHORT) & (col < row * SHORT + lengths)
        new_k = new_kv_ref[0, pl.ds(r0, chunk), :]
        new_v = new_kv_ref[1, pl.ds(r0, chunk), :]
        for h in range(groups):
            qh = q_ref[pl.ds(r0, chunk), h * head_dim:(h + 1) * head_dim]
            o_ref[pl.ds(r0, chunk), h * head_dim:(h + 1) * head_dim] = attend(
                qh, keys, values, valid, new_k, new_v
            )

    @pl.loop(0, table_width)
    def _(j):
        long_copy(j, 0, long_k).wait()
        long_copy(j, 1, long_v).wait()

    long_col = lax.broadcasted_iota(jnp.int32, (chunk, table_width * page_size), 1)
    long_valid = long_col < long_len
    own_row = lax.broadcasted_iota(jnp.int32, (chunk, 1), 0)

    @pl.when(long_len >= SHORT)
    def _():
        r0 = pl.multiple_of((long_row // chunk) * chunk, chunk)
        new_k = new_kv_ref[0, pl.ds(r0, chunk), :]
        new_v = new_kv_ref[1, pl.ds(r0, chunk), :]
        chosen = (own_row + r0) == long_row
        for h in range(groups):
            qh = q_ref[pl.ds(r0, chunk), h * head_dim:(h + 1) * head_dim]
            result = attend(qh, long_k[...], long_v[...], long_valid, new_k, new_v)
            current = o_ref[pl.ds(r0, chunk), h * head_dim:(h + 1) * head_dim]
            o_ref[pl.ds(r0, chunk), h * head_dim:(h + 1) * head_dim] = jnp.where(
                chosen, result, current
            )


def local_attention(query, new_kv, key_value_pages, page_table, cache_len):
    row_count = query.shape[0]
    pool_pages = key_value_pages.shape[1]
    page_size = key_value_pages.shape[2]
    head_dim = HEAD_SIZE
    table_width = page_table.shape[1]
    base = jnp.full((1,), lax.axis_index("dp") * pool_pages, jnp.int32)
    smem = pl.BlockSpec(memory_space=pltpu.SMEM)
    vmem = pl.BlockSpec(memory_space=pltpu.VMEM)
    rows = row_count * SHORT + table_width * page_size
    return pl.pallas_call(
        attention_kernel,
        out_shape=jax.ShapeDtypeStruct(query.shape, jnp.bfloat16),
        in_specs=[smem, smem, smem, vmem, vmem, pl.BlockSpec(memory_space=pl.ANY)],
        out_specs=vmem,
        scratch_shapes=[
            pltpu.VMEM((row_count * SHORT, head_dim), key_value_pages.dtype),
            pltpu.VMEM((row_count * SHORT, head_dim), key_value_pages.dtype),
            pltpu.VMEM((table_width * page_size, head_dim), key_value_pages.dtype),
            pltpu.VMEM((table_width * page_size, head_dim), key_value_pages.dtype),
            pltpu.SemaphoreType.DMA((4, row_count)),
        ],
        cost_estimate=pl.CostEstimate(
            flops=4 * 16 * query.shape[1] * rows,
            transcendentals=16 * query.shape[1] // head_dim * rows,
            bytes_accessed=2 * 2 * head_dim * rows,
        ),
    )(page_table, cache_len, base, query, new_kv, key_value_pages)


def ring_shift(x, shift, axis_name, size):
    return lax.ppermute(x, axis_name, [(i, (i + shift) % size) for i in range(size)])


def ring_reduce_scatter(blocks, axis_name, size, index):
    total = lax.dynamic_index_in_dim(blocks, index, 0, keepdims=False).astype(jnp.float32)
    for shift in range(1, size):
        outgoing = lax.dynamic_index_in_dim(blocks, (index + shift) % size, 0, keepdims=False)
        total = total + ring_shift(outgoing, shift, axis_name, size).astype(jnp.float32)
    return total


def ring_all_gather(x, axis_name, size):
    return [x] + [ring_shift(x, shift, axis_name, size) for shift in range(1, size)]


def dense_all_to_all(x, axis_name):
    lanes = 128
    flat = x.reshape(x.shape[0], x.shape[1] * x.shape[2] // lanes, lanes)
    moved = lax.all_to_all(flat, axis_name, split_axis=0, concat_axis=0, tiled=True)
    return moved.reshape(x.shape)


def ring_all_gather_two_step(x, axis_name, size, index):
    half = x.shape[0] // 2
    from_left = ring_shift(x, 1, axis_name, size)
    from_right = ring_shift(x, size - 1, axis_name, size)
    far = jnp.concatenate(
        [
            ring_shift(from_left[:half], 1, axis_name, size),
            ring_shift(from_right[half:], size - 1, axis_name, size),
        ],
        axis=0,
    )
    return [x, from_left, far, from_right]


def ring_reduce_scatter_two_step(blocks, axis_name, size, index):
    def block(shift):
        return lax.dynamic_index_in_dim(blocks, (index + shift) % size, 0, keepdims=False)

    far = block(2)
    half = far.shape[0] // 2
    to_left_far = ring_shift(far[:half], 1, axis_name, size)
    to_right_far = ring_shift(far[half:], size - 1, axis_name, size)
    from_left = ring_shift(block(1), 1, axis_name, size).astype(jnp.float32)
    from_right = ring_shift(block(size - 1), size - 1, axis_name, size).astype(jnp.float32)
    far_first = ring_shift(to_left_far, 1, axis_name, size).astype(jnp.float32)
    far_second = ring_shift(to_right_far, size - 1, axis_name, size).astype(jnp.float32)
    total = block(0).astype(jnp.float32) + from_left + from_right
    return total + jnp.concatenate([far_first, far_second], axis=0)


def per_device(
    query,
    new_kv,
    key_value_pages,
    page_table,
    cache_len,
    residual,
    out_weight,
    norm_gain,
    expert_ids,
    combine_weights,
    expert_w1,
    expert_w2,
):
    tensor_size = lax.axis_size("tensor")
    tensor_index = lax.axis_index("tensor")
    attn = local_attention(query, new_kv, key_value_pages, page_table, cache_len)
    row_count, model_width = residual.shape
    share_width = model_width // tensor_size
    share_start = tensor_index * share_width

    split_weight = out_weight.reshape(out_weight.shape[0], tensor_size, share_width)
    partial_proj = jnp.einsum(
        "rk,kuc->urc", attn, split_weight, preferred_element_type=jnp.float32
    )
    summed = ring_reduce_scatter_two_step(partial_proj, "tensor", tensor_size, tensor_index)
    residual_share = lax.dynamic_slice_in_dim(residual, share_start, share_width, 1)
    state = residual_share.astype(jnp.float32) + summed
    square_sum = sum(ring_all_gather(jnp.sum(state * state, axis=1, keepdims=True), "tensor", tensor_size))
    mean_square = square_sum / model_width
    gain_share = lax.dynamic_slice_in_dim(norm_gain, share_start, share_width, 0)
    normed = (state * lax.rsqrt(mean_square + 1e-05) * gain_share).astype(jnp.bfloat16)

    local_experts = expert_w1.shape[0]
    top_count = expert_ids.shape[1]
    experts = local_experts * lax.axis_size("dp")
    capacity = min(
        row_count, max(3, (3 * row_count * top_count + 2 * experts - 1) // (2 * experts))
    )
    flat_ids = expert_ids.reshape(-1)
    choice_rows = flat_ids.shape[0]
    row_iota = jnp.arange(choice_rows, dtype=jnp.int32)
    choice_hot = (flat_ids[:, None] == jnp.arange(experts, dtype=jnp.int32)[None, :]).astype(
        jnp.bfloat16
    )
    strictly_lower = (row_iota[:, None] > row_iota[None, :]).astype(jnp.bfloat16)
    earlier = jnp.dot(strictly_lower, choice_hot, preferred_element_type=jnp.float32)
    slot_rank = jnp.sum(earlier * choice_hot.astype(jnp.float32), axis=1).astype(jnp.int32)
    slot_index = (flat_ids * capacity + slot_rank).reshape(row_count, top_count)
    slot_ids = jnp.arange(experts * capacity, dtype=jnp.int32)
    hit = slot_index[:, :, None] == slot_ids[None, None, :]
    placing = jnp.any(hit, axis=1).astype(jnp.bfloat16)
    mixing = jnp.sum(jnp.where(hit, combine_weights[:, :, None], 0.0), axis=1)

    outgoing = jnp.dot(placing.T, normed, preferred_element_type=jnp.float32)
    outgoing = outgoing.astype(jnp.bfloat16).reshape(experts, capacity, share_width)
    mixing = mixing.reshape(row_count, experts, capacity)
    split_w1 = expert_w1.reshape(tensor_size, share_width, 2, expert_w1.shape[-1])
    split_w2 = expert_w2[0].reshape(expert_w2.shape[1], tensor_size, share_width)

    expert_mix = None
    streams = 1
    bounds = [capacity * i // streams for i in range(streams + 1)]
    for lo, hi in zip(bounds[:-1], bounds[1:]):
        slots = hi - lo
        arrived = dense_all_to_all(outgoing[:, lo:hi], "dp")
        pieces = ring_all_gather_two_step(arrived, "tensor", tensor_size, tensor_index)
        gate_up = None
        for shift, piece in enumerate(pieces):
            weight = lax.dynamic_index_in_dim(
                split_w1, (tensor_index - shift) % tensor_size, 0, keepdims=False
            )
            term = jnp.einsum("snc,cgf->sngf", piece, weight, preferred_element_type=jnp.float32)
            gate_up = term if gate_up is None else gate_up + term
        activated = (jax.nn.silu(gate_up[:, :, 0, :]) * gate_up[:, :, 1, :]).astype(
            jnp.bfloat16
        )
        partial_out = jnp.einsum(
            "snf,fuc->usnc", activated, split_w2, preferred_element_type=jnp.float32
        ).astype(jnp.bfloat16)
        expert_sum = ring_reduce_scatter_two_step(
            partial_out, "tensor", tensor_size, tensor_index
        )
        expert_sum = expert_sum.astype(jnp.bfloat16)
        returned_rows = dense_all_to_all(expert_sum, "dp")
        part_mix = jnp.dot(
            mixing[:, :, lo:hi].reshape(row_count, experts * slots),
            returned_rows.reshape(experts * slots, share_width).astype(jnp.float32),
            precision=lax.Precision.HIGHEST,
        )
        expert_mix = part_mix if expert_mix is None else expert_mix + part_mix
    return (state + expert_mix).astype(jnp.bfloat16)


def solution(mesh):
    return jax.shard_map(
        per_device,
        mesh=mesh,
        in_specs=(
            P("dp", "tensor"),
            P(None, "dp", "tensor"),
            P(None, "dp", None, "tensor"),
            P("dp", None),
            P("dp"),
            P("dp", None),
            P("tensor", None),
            P(),
            P("dp", None),
            P("dp", None),
            P("dp", None, None, "tensor"),
            P("dp", "tensor", None),
        ),
        out_specs=P("dp", "tensor"),
        check_vma=False,
    )
```

```python
import math

import jax
import jax.numpy as jnp
from jax import lax
from jax.experimental import pallas as pl
from jax.experimental.pallas import tpu as pltpu
from jax.sharding import PartitionSpec as P

HEAD_SIZE = 128
SHORT = 64


def attention_kernel(
    table_ref, len_ref, base_ref, q_ref, new_kv_ref, kv_hbm, o_ref,
    short_k, short_v, long_k, long_v, sem,
):
    rows = q_ref.shape[0]
    head_dim = new_kv_ref.shape[2]
    groups = q_ref.shape[1] // head_dim
    table_width = table_ref.shape[1]
    pool_pages = kv_hbm.shape[1]
    page_size = kv_hbm.shape[2]
    chunk = 16
    scale_of_score = 1.0 / math.sqrt(head_dim)
    base = base_ref[0]

    def local_page(r, j):
        return jnp.minimum(jnp.maximum(table_ref[r, j] - base, 0), pool_pages - 1)

    def longest(r, carry):
        best_row, best_len = carry
        length = len_ref[r]
        better = length > best_len
        return jnp.where(better, r, best_row), jnp.where(better, length, best_len)

    def short_copy(r, which, buf):
        return pltpu.make_async_copy(
            kv_hbm.at[which, local_page(r, 0), pl.ds(0, SHORT), :],
            buf.at[pl.ds(r * SHORT, SHORT), :],
            sem.at[which, r],
        )

    @pl.loop(0, rows)
    def _(r):
        short_copy(r, 0, short_k).start()
        short_copy(r, 1, short_v).start()

    long_row, long_len = lax.fori_loop(0, rows, longest, (jnp.int32(0), len_ref[0]))

    def long_copy(j, which, buf):
        return pltpu.make_async_copy(
            kv_hbm.at[which, local_page(long_row, j)],
            buf.at[pl.ds(j * page_size, page_size), :],
            sem.at[2 + which, j],
        )

    @pl.loop(0, table_width)
    def _(j):
        long_copy(j, 0, long_k).start()
        long_copy(j, 1, long_v).start()

    def attend(qh, keys, values, valid, new_k, new_v):
        scores = lax.dot_general(
            qh, keys, (((1,), (1,)), ((), ())), preferred_element_type=jnp.float32
        ) * scale_of_score
        fresh = jnp.sum(
            qh.astype(jnp.float32) * new_k.astype(jnp.float32), axis=1, keepdims=True
        ) * scale_of_score
        scores = jnp.where(valid, scores, -1e30)
        row_max = jnp.maximum(jnp.max(scores, axis=1, keepdims=True), fresh)
        weights = jnp.where(valid, jnp.exp(scores - row_max), 0.0)
        weight_new = jnp.exp(fresh - row_max)
        denominator = jnp.sum(weights, axis=1, keepdims=True) + weight_new
        numerator = jnp.dot(
            weights.astype(jnp.bfloat16), values, preferred_element_type=jnp.float32
        )
        numerator = numerator + (
            weight_new.astype(jnp.bfloat16).astype(jnp.float32) * new_v.astype(jnp.float32)
        )
        return (numerator / denominator).astype(o_ref.dtype)

    width = chunk * SHORT
    row = lax.broadcasted_iota(jnp.int32, (chunk, width), 0)
    col = lax.broadcasted_iota(jnp.int32, (chunk, width), 1)

    @pl.loop(0, rows // chunk)
    def _(c):
        r0 = pl.multiple_of(c * chunk, chunk)
        k0 = pl.multiple_of(c * width, width)

        @pl.loop(0, chunk)
        def _(i):
            short_copy(r0 + i, 0, short_k).wait()
            short_copy(r0 + i, 1, short_v).wait()

        keys = short_k[pl.ds(k0, width), :]
        values = short_v[pl.ds(k0, width), :]
        lengths = jnp.zeros((chunk, 1), jnp.int32)
        for i in range(chunk):
            lengths = jnp.where(row[:, :1] == i, jnp.minimum(len_ref[r0 + i], SHORT), lengths)
        valid = (col >= row * SHORT) & (col < row * SHORT + lengths)
        new_k = new_kv_ref[0, pl.ds(r0, chunk), :]
        new_v = new_kv_ref[1, pl.ds(r0, chunk), :]
        for h in range(groups):
            qh = q_ref[pl.ds(r0, chunk), h * head_dim:(h + 1) * head_dim]
            o_ref[pl.ds(r0, chunk), h * head_dim:(h + 1) * head_dim] = attend(
                qh, keys, values, valid, new_k, new_v
            )

    @pl.loop(0, table_width)
    def _(j):
        long_copy(j, 0, long_k).wait()
        long_copy(j, 1, long_v).wait()

    long_col = lax.broadcasted_iota(jnp.int32, (chunk, table_width * page_size), 1)
    long_valid = long_col < long_len
    own_row = lax.broadcasted_iota(jnp.int32, (chunk, 1), 0)

    @pl.when(long_len >= SHORT)
    def _():
        r0 = pl.multiple_of((long_row // chunk) * chunk, chunk)
        new_k = new_kv_ref[0, pl.ds(r0, chunk), :]
        new_v = new_kv_ref[1, pl.ds(r0, chunk), :]
        chosen = (own_row + r0) == long_row
        for h in range(groups):
            qh = q_ref[pl.ds(r0, chunk), h * head_dim:(h + 1) * head_dim]
            result = attend(qh, long_k[...], long_v[...], long_valid, new_k, new_v)
            current = o_ref[pl.ds(r0, chunk), h * head_dim:(h + 1) * head_dim]
            o_ref[pl.ds(r0, chunk), h * head_dim:(h + 1) * head_dim] = jnp.where(
                chosen, result, current
            )


def local_attention(query, new_kv, key_value_pages, page_table, cache_len):
    row_count = query.shape[0]
    pool_pages = key_value_pages.shape[1]
    page_size = key_value_pages.shape[2]
    head_dim = HEAD_SIZE
    table_width = page_table.shape[1]
    base = jnp.full((1,), lax.axis_index("dp") * pool_pages, jnp.int32)
    smem = pl.BlockSpec(memory_space=pltpu.SMEM)
    vmem = pl.BlockSpec(memory_space=pltpu.VMEM)
    rows = row_count * SHORT + table_width * page_size
    return pl.pallas_call(
        attention_kernel,
        out_shape=jax.ShapeDtypeStruct(query.shape, jnp.bfloat16),
        in_specs=[smem, smem, smem, vmem, vmem, pl.BlockSpec(memory_space=pl.ANY)],
        out_specs=vmem,
        scratch_shapes=[
            pltpu.VMEM((row_count * SHORT, head_dim), key_value_pages.dtype),
            pltpu.VMEM((row_count * SHORT, head_dim), key_value_pages.dtype),
            pltpu.VMEM((table_width * page_size, head_dim), key_value_pages.dtype),
            pltpu.VMEM((table_width * page_size, head_dim), key_value_pages.dtype),
            pltpu.SemaphoreType.DMA((4, row_count)),
        ],
        cost_estimate=pl.CostEstimate(
            flops=4 * 16 * query.shape[1] * rows,
            transcendentals=16 * query.shape[1] // head_dim * rows,
            bytes_accessed=2 * 2 * head_dim * rows,
        ),
    )(page_table, cache_len, base, query, new_kv, key_value_pages)


def ring_shift(x, shift, axis_name, size):
    return lax.ppermute(x, axis_name, [(i, (i + shift) % size) for i in range(size)])


def ring_reduce_scatter(blocks, axis_name, size, index):
    total = lax.dynamic_index_in_dim(blocks, index, 0, keepdims=False).astype(jnp.float32)
    for shift in range(1, size):
        outgoing = lax.dynamic_index_in_dim(blocks, (index + shift) % size, 0, keepdims=False)
        total = total + ring_shift(outgoing, shift, axis_name, size).astype(jnp.float32)
    return total


def ring_all_gather(x, axis_name, size):
    return [x] + [ring_shift(x, shift, axis_name, size) for shift in range(1, size)]


def dense_all_to_all(x, axis_name):
    lanes = 128
    flat = x.reshape(x.shape[0], x.shape[1] * x.shape[2] // lanes, lanes)
    moved = lax.all_to_all(flat, axis_name, split_axis=0, concat_axis=0, tiled=True)
    return moved.reshape(x.shape)


def ring_all_gather_two_step(x, axis_name, size, index):
    half = x.shape[0] // 2
    from_left = ring_shift(x, 1, axis_name, size)
    from_right = ring_shift(x, size - 1, axis_name, size)
    far = jnp.concatenate(
        [
            ring_shift(from_left[:half], 1, axis_name, size),
            ring_shift(from_right[half:], size - 1, axis_name, size),
        ],
        axis=0,
    )
    return [x, from_left, far, from_right]


def ring_reduce_scatter_two_step(blocks, axis_name, size, index):
    def block(shift):
        return lax.dynamic_index_in_dim(blocks, (index + shift) % size, 0, keepdims=False)

    far = block(2)
    half = far.shape[0] // 2
    to_left_far = ring_shift(far[:half], 1, axis_name, size)
    to_right_far = ring_shift(far[half:], size - 1, axis_name, size)
    from_left = ring_shift(block(1), 1, axis_name, size).astype(jnp.float32)
    from_right = ring_shift(block(size - 1), size - 1, axis_name, size).astype(jnp.float32)
    far_first = ring_shift(to_left_far, 1, axis_name, size).astype(jnp.float32)
    far_second = ring_shift(to_right_far, size - 1, axis_name, size).astype(jnp.float32)
    total = block(0).astype(jnp.float32) + from_left + from_right
    return total + jnp.concatenate([far_first, far_second], axis=0)


def per_device(
    query,
    new_kv,
    key_value_pages,
    page_table,
    cache_len,
    residual,
    out_weight,
    norm_gain,
    expert_ids,
    combine_weights,
    expert_w1,
    expert_w2,
):
    tensor_size = lax.axis_size("tensor")
    tensor_index = lax.axis_index("tensor")
    attn = local_attention(query, new_kv, key_value_pages, page_table, cache_len)
    row_count, model_width = residual.shape
    share_width = model_width // tensor_size
    share_start = tensor_index * share_width

    split_weight = out_weight.reshape(out_weight.shape[0], tensor_size, share_width)
    partial_proj = jnp.einsum(
        "rk,kuc->urc", attn, split_weight, preferred_element_type=jnp.float32
    )
    summed = ring_reduce_scatter(partial_proj, "tensor", tensor_size, tensor_index)
    residual_share = lax.dynamic_slice_in_dim(residual, share_start, share_width, 1)
    state = residual_share.astype(jnp.float32) + summed
    square_sum = sum(ring_all_gather(jnp.sum(state * state, axis=1, keepdims=True), "tensor", tensor_size))
    mean_square = square_sum / model_width
    gain_share = lax.dynamic_slice_in_dim(norm_gain, share_start, share_width, 0)
    normed = (state * lax.rsqrt(mean_square + 1e-05) * gain_share).astype(jnp.bfloat16)

    local_experts = expert_w1.shape[0]
    top_count = expert_ids.shape[1]
    experts = local_experts * lax.axis_size("dp")
    capacity = min(
        row_count, max(3, (3 * row_count * top_count + 2 * experts - 1) // (2 * experts))
    )
    flat_ids = expert_ids.reshape(-1)
    choice_rows = flat_ids.shape[0]
    row_iota = jnp.arange(choice_rows, dtype=jnp.int32)
    choice_hot = (flat_ids[:, None] == jnp.arange(experts, dtype=jnp.int32)[None, :]).astype(
        jnp.bfloat16
    )
    strictly_lower = (row_iota[:, None] > row_iota[None, :]).astype(jnp.bfloat16)
    earlier = jnp.dot(strictly_lower, choice_hot, preferred_element_type=jnp.float32)
    slot_rank = jnp.sum(earlier * choice_hot.astype(jnp.float32), axis=1).astype(jnp.int32)
    slot_index = (flat_ids * capacity + slot_rank).reshape(row_count, top_count)
    slot_ids = jnp.arange(experts * capacity, dtype=jnp.int32)
    hit = slot_index[:, :, None] == slot_ids[None, None, :]
    placing = jnp.any(hit, axis=1).astype(jnp.bfloat16)
    mixing = jnp.sum(jnp.where(hit, combine_weights[:, :, None], 0.0), axis=1)

    outgoing = jnp.dot(placing.T, normed, preferred_element_type=jnp.float32)
    outgoing = outgoing.astype(jnp.bfloat16).reshape(experts, capacity, share_width)
    mixing = mixing.reshape(row_count, experts, capacity)
    split_w1 = expert_w1.reshape(tensor_size, share_width, 2, expert_w1.shape[-1])
    split_w2 = expert_w2[0].reshape(expert_w2.shape[1], tensor_size, share_width)

    expert_mix = None
    streams = 1
    bounds = [capacity * i // streams for i in range(streams + 1)]
    for lo, hi in zip(bounds[:-1], bounds[1:]):
        slots = hi - lo
        arrived = dense_all_to_all(outgoing[:, lo:hi], "dp")
        pieces = ring_all_gather_two_step(arrived, "tensor", tensor_size, tensor_index)
        gate_up = None
        for shift, piece in enumerate(pieces):
            weight = lax.dynamic_index_in_dim(
                split_w1, (tensor_index - shift) % tensor_size, 0, keepdims=False
            )
            term = jnp.einsum("snc,cgf->sngf", piece, weight, preferred_element_type=jnp.float32)
            gate_up = term if gate_up is None else gate_up + term
        activated = (jax.nn.silu(gate_up[:, :, 0, :]) * gate_up[:, :, 1, :]).astype(
            jnp.bfloat16
        )
        partial_out = jnp.einsum(
            "snf,fuc->usnc", activated, split_w2, preferred_element_type=jnp.float32
        ).astype(jnp.bfloat16)
        expert_sum = ring_reduce_scatter_two_step(
            partial_out, "tensor", tensor_size, tensor_index
        )
        expert_sum = expert_sum.astype(jnp.bfloat16)
        returned_rows = dense_all_to_all(expert_sum, "dp")
        part_mix = jnp.dot(
            mixing[:, :, lo:hi].reshape(row_count, experts * slots),
            returned_rows.reshape(experts * slots, share_width).astype(jnp.float32),
            precision=lax.Precision.HIGHEST,
        )
        expert_mix = part_mix if expert_mix is None else expert_mix + part_mix
    return (state + expert_mix).astype(jnp.bfloat16)


def solution(mesh):
    return jax.shard_map(
        per_device,
        mesh=mesh,
        in_specs=(
            P("dp", "tensor"),
            P(None, "dp", "tensor"),
            P(None, "dp", None, "tensor"),
            P("dp", None),
            P("dp"),
            P("dp", None),
            P("tensor", None),
            P(),
            P("dp", None),
            P("dp", None),
            P("dp", None, None, "tensor"),
            P("dp", "tensor", None),
        ),
        out_specs=P("dp", "tensor"),
        check_vma=False,
    )
```
